32 devices in a mesh: gx: 8 (over y, x, core), gy: 4 (over z).
Axes of the slice: x: 2, y: 2, z: 4, core: 2. Of those that a mesh axis runs over, the one named last changes fastest.
Arguments:
- offsets: float32 [3, 16, 8, 4, 128], P(None, 'gx', 'gy'), may hold values from 0 to 1
- charges: float32 [16, 8, 4, 128], P('gx', 'gy'), may hold values from -0.12 to 0.12
- counts: int32 [16, 8, 4], P('gx', 'gy'), may hold values from 16 to 128, as said below
- c2e_leaf_up: float32 [256, 256], replicated, may hold values from -0.09375 to 0.09375
- c2e_leaf_down: float32 [256, 256], replicated, may hold values from -0.09375 to 0.09375
- c2e_top_up: float32 [256, 256], replicated, may hold values from -0.046875 to 0.046875
- c2e_top_down: float32 [256, 256], replicated, may hold values from -0.046875 to 0.046875
Outputs:
- potential: float32 [16, 8, 4, 128], P('gx', 'gy')
The draws below stay inside these ranges and needn't reach their ends.
Inputs may be any that keep to these rules, and one draw needn't show every extreme that they name: The first counts slots of a leaf box hold its particles, the rest are padding.
All inputs are finite; a program needn't handle non-finite values.
Results may differ from the reference program's by a relative error of at most 0.0003.
Values sent between devices are 32-bit elements; how exact they have to be, the bound alone decides.
No kernel may reach another device: no remote copies, remote signals or barrier semaphores. Data moves between devices by JAX's collectives and lax.ppermute only.
A program may use at most 64 MiB of HBM per device.

```python
import jax
import jax.numpy as jnp
from jax import lax

S = 128
NE = 256
BZ = 4
PZ = 2
NBX = 16
NBY = 8
N_GX = 8
N_GY = 4


def draw_counts(key, part):
    raw_counts = jax.random.randint(key, (NBX, NBY, BZ), S // 8, 2 * S)
    return jnp.minimum(raw_counts, S).astype(jnp.int32)


def level_of(key, dims, cuts, least, largest):
    level = 1.0
    for dim, blocks in cuts:
        heights = jax.random.uniform(jax.random.fold_in(jax.random.fold_in(key, 6), dim), (blocks,), jnp.float32, least / len(cuts), largest / len(cuts))
        level = level * jnp.repeat(jnp.exp(heights), dims[dim] // blocks).reshape((-1,) + (1,) * (len(dims) - 1 - dim))
    return level


def normal_values(key, extent, scale, reach, split=(), kind=jnp.bfloat16):
    factor_of = level_of(key, extent, split, -0.22, 0.18) if split else 1.0
    drawn = jax.random.normal(key, extent, jnp.float32) * scale * factor_of
    return jnp.minimum(jnp.maximum(drawn, -reach), reach).astype(kind)


def setup_inputs(seed: int = 0) -> dict:
    splits = jax.random.split(jax.random.key(seed), 8)
    return {
        "offsets": jnp.clip(1.0 * jax.random.uniform(splits[0], (3, NBX, NBY, BZ, S), jnp.float32) ** level_of(splits[0], (3, NBX, NBY, BZ, S), ((1, 8), (2, 4)), -0.2, 0.2), 0.0, 1.0),
        "charges": normal_values(splits[1], (NBX, NBY, BZ, S), 0.02, 0.12, ((0, 8), (1, 4)), jnp.float32),
        "counts": draw_counts(jax.random.fold_in(splits[7], 71), 0),
        "c2e_leaf_up": normal_values(splits[3], (NE, NE), (16 * NE) ** -0.5, 0.09375, (), jnp.float32),
        "c2e_leaf_down": normal_values(splits[4], (NE, NE), (16 * NE) ** -0.5, 0.09375, (), jnp.float32),
        "c2e_top_up": normal_values(splits[5], (NE, NE), (64 * NE) ** -0.5, 0.046875, (), jnp.float32),
        "c2e_top_down": normal_values(splits[6], (NE, NE), (64 * NE) ** -0.5, 0.046875, (), jnp.float32),
    }


softening_sq = 0.0004
golden_turn = 2.399963229728653
highest = lax.Precision.HIGHEST

def sphere(point_count):
    middle = jnp.arange(point_count).astype(jnp.float32) + 0.5
    height = 1.0 - 2.0 * middle / point_count
    radial = jnp.sqrt(jnp.maximum(1.0 - height * height, 0.0))
    angle_turn = middle * golden_turn
    return jnp.stack([radial * jnp.cos(angle_turn), radial * jnp.sin(angle_turn), height])

def point_sum(targets, sources, weights):
    delta_x = targets[0][..., :, None] - sources[0][..., None, :]
    delta_y = targets[1][..., :, None] - sources[1][..., None, :]
    delta_z = targets[2][..., :, None] - sources[2][..., None, :]
    kernel = lax.rsqrt(delta_x * delta_x + delta_y * delta_y + delta_z * delta_z + softening_sq)
    return lax.optimization_barrier(jnp.sum(kernel * weights[..., None, :], axis=-1))

def translation(unit_sphere, shift_x, shift_y, shift_z, radius):
    delta_x = radius * (unit_sphere[0][:, None] - unit_sphere[0][None, :]) - shift_x[..., None, None]
    delta_y = radius * (unit_sphere[1][:, None] - unit_sphere[1][None, :]) - shift_y[..., None, None]
    delta_z = radius * (unit_sphere[2][:, None] - unit_sphere[2][None, :]) - shift_z[..., None, None]
    return lax.rsqrt(delta_x * delta_x + delta_y * delta_y + delta_z * delta_z + softening_sq)

def child_points(unit_sphere):
    centre = jnp.arange(2).astype(jnp.float32) + 0.5
    point_count = unit_sphere.shape[1]
    box_shape = (2, 2, 2, point_count)
    along_x = jnp.broadcast_to(centre[:, None, None, None] + 0.9 * unit_sphere[0], box_shape)
    along_y = jnp.broadcast_to(centre[None, :, None, None] + 0.9 * unit_sphere[1], box_shape)
    along_z = jnp.broadcast_to(centre[None, None, :, None] + 0.9 * unit_sphere[2], box_shape)
    return jnp.stack([along_x, along_y, along_z]).reshape(3, 8 * point_count)

def reference(offsets, charges, counts, c2e_leaf_up, c2e_leaf_down, c2e_top_up, c2e_top_down):
    unit_sphere = sphere(NE)
    slot_index = jnp.arange(S)
    weights = jnp.where(slot_index < counts[..., None], charges, 0.0)
    packed = jnp.concatenate([offsets, weights[None]], axis=0)
    leaf_check_pts = 0.5 + 1.8 * unit_sphere

    def leaf_up_row(column):
        row_block = lax.dynamic_index_in_dim(packed, column, 1, keepdims=False)
        return point_sum(leaf_check_pts[:, None, None, :], row_block[:3], row_block[3])
    leaf_check = lax.map(leaf_up_row, jnp.arange(NBX))
    leaf_eq = jnp.einsum('ec,xyzc->xyze', c2e_leaf_up, leaf_check, precision=highest)
    children = child_points(unit_sphere)
    grouped = leaf_eq.reshape(N_GX, 2, N_GY, 2, PZ, 2, NE).transpose(0, 2, 4, 1, 3, 5, 6).reshape(N_GX, N_GY, PZ, 8 * NE)
    parent_check_pts = 1.0 + 3.6 * unit_sphere

    def parent_up_row(block_row):
        return point_sum(parent_check_pts[:, None, None, :], children[:, None, None, :], block_row)
    parent_check = lax.map(parent_up_row, grouped)
    parent_eq = jnp.einsum('ec,xymc->xyme', c2e_top_up, parent_check, precision=highest)
    layer_float = jnp.arange(PZ).astype(jnp.float32)
    depth_pairs = 2.0 * (layer_float[None, :] - layer_float[:, None])
    pair_ones = jnp.ones((PZ, PZ), jnp.float32)

    def far_step(running, combo):
        off_x = combo // N_GY - N_GX // 2
        off_y = combo % N_GY - N_GY // 2
        moved = jnp.roll(parent_eq, (-off_x, -off_y), axis=(0, 1))
        keep = ((jnp.abs(off_x) > 1) | (jnp.abs(off_y) > 1)).astype(jnp.float32)
        matrices = translation(unit_sphere, 2.0 * off_x.astype(jnp.float32) * pair_ones, 2.0 * off_y.astype(jnp.float32) * pair_ones, depth_pairs, 1.8)
        term = jnp.einsum('tsce,xyse->xytc', matrices, moved, precision=highest)
        return (running + keep * term, None)
    far_check, _ = lax.scan(far_step, jnp.zeros((N_GX, N_GY, PZ, NE), jnp.float32), jnp.arange(N_GX * N_GY))
    parent_local = jnp.einsum('ec,xymc->xyme', c2e_top_down, far_check, precision=highest)
    framed = jnp.pad(leaf_eq, ((0, 0), (0, 0), (3, 3), (0, 0)))
    parity_x = jnp.arange(NBX) % 2
    parity_y = jnp.arange(NBY) % 2
    layer_index = jnp.arange(BZ)
    depth_shift = jnp.arange(7) - 3
    seven_ones = jnp.ones((7,), jnp.float32)

    def list_step(running, combo):
        shift_x = combo // 7 - 3
        shift_y = combo % 7 - 3
        moved = jnp.roll(framed, (-shift_x, -shift_y), axis=(0, 1))
        stacked = jnp.stack([moved[:, :, depth:depth + BZ] for depth in range(7)])
        valid_x = (parity_x + shift_x >= -2) & (parity_x + shift_x <= 3)
        valid_y = (parity_y + shift_y >= -2) & (parity_y + shift_y <= 3)
        valid_z = (layer_index[None, :] + depth_shift[:, None] >= 0) & (layer_index[None, :] + depth_shift[:, None] <= BZ - 1)
        far_enough = (jnp.abs(shift_x) > 1) | (jnp.abs(shift_y) > 1) | (jnp.abs(depth_shift) > 1)
        keep = valid_x[None, :, None, None] & valid_y[None, None, :, None] & valid_z[:, None, None, :] & far_enough[:, None, None, None]
        matrices = translation(unit_sphere, shift_x.astype(jnp.float32) * seven_ones, shift_y.astype(jnp.float32) * seven_ones, depth_shift.astype(jnp.float32), 0.9)
        sources = jnp.where(keep[..., None], stacked, 0.0)
        return (running + jnp.einsum('zce,zxyke->xykc', matrices, sources, precision=highest), None)
    leaf_down_check, _ = lax.scan(list_step, jnp.zeros((NBX, NBY, BZ, NE), jnp.float32), jnp.arange(49))
    leaf_local = jnp.einsum('ec,xyzc->xyze', c2e_leaf_down, leaf_down_check, precision=highest)
    spread_local = jnp.repeat(jnp.repeat(jnp.repeat(parent_local, 2, axis=0), 2, axis=1), 2, axis=2)
    beside_all = jnp.pad(packed, ((0, 0), (1, 1), (1, 1), (0, 0), (0, 0)), mode='wrap')
    beside_all = jnp.pad(beside_all, ((0, 0), (0, 0), (0, 0), (1, 1), (0, 0)))
    diagonal = jnp.arange(S)[:, None] == jnp.arange(S)[None, :]
    leaf_down_pts = 0.5 + 1.8 * unit_sphere
    parent_down_pts = 1.0 + 3.6 * unit_sphere
    float_parity_y = (jnp.arange(NBY) % 2).astype(jnp.float32)
    float_parity_z = (jnp.arange(BZ) % 2).astype(jnp.float32)

    def finish_row(column):
        own_block = lax.dynamic_index_in_dim(packed, column, 1, keepdims=False)
        near = jnp.zeros((NBY, BZ, S), jnp.float32)
        for stencil in range(27):
            move_x = stencil // 9 - 1
            move_y = stencil // 3 % 3 - 1
            move_z = stencil % 3 - 1
            slab_row = lax.dynamic_index_in_dim(beside_all, column + 1 + move_x, 1, keepdims=False)
            source = slab_row[:, 1 + move_y:1 + move_y + NBY, 1 + move_z:1 + move_z + BZ]
            delta_x = own_block[0][..., :, None] - source[0][..., None, :] - float(move_x)
            delta_y = own_block[1][..., :, None] - source[1][..., None, :] - float(move_y)
            delta_z = own_block[2][..., :, None] - source[2][..., None, :] - float(move_z)
            kernel = lax.rsqrt(delta_x * delta_x + delta_y * delta_y + delta_z * delta_z + softening_sq)
            if stencil == 13:
                kernel = jnp.where(diagonal, 0.0, kernel)
            near = near + lax.optimization_barrier(jnp.sum(kernel * source[3][..., None, :], axis=-1))
        local_leaf = lax.dynamic_index_in_dim(leaf_local, column, 0, keepdims=False)
        local_parent = lax.dynamic_index_in_dim(spread_local, column, 0, keepdims=False)
        leaf_far = point_sum(own_block[:3], leaf_down_pts[:, None, None, :], local_leaf)
        column_parity = (column % 2).astype(jnp.float32)
        in_parent = jnp.stack([column_parity + own_block[0], float_parity_y[:, None, None] + own_block[1], float_parity_z[None, :, None] + own_block[2]])
        parent_far = point_sum(in_parent, parent_down_pts[:, None, None, :], local_parent)
        return near + leaf_far + parent_far
    total = lax.map(finish_row, jnp.arange(NBX))
    return jnp.where(slot_index < counts[..., None], total, 0.0)
```

```python
import jax
import jax.numpy as jnp
from jax import lax
from jax.sharding import PartitionSpec as P

softening_sq = 0.0004
golden_turn = 2.399963229728653
highest = lax.Precision.HIGHEST


def padded(cells, sides, width):
    for axis, dim in sides:
        count = lax.axis_size(axis)
        head = lax.slice_in_dim(cells, 0, width, axis=dim)
        tail = lax.slice_in_dim(cells, cells.shape[dim] - width, cells.shape[dim], axis=dim)
        cells = jnp.concatenate(
            [
                lax.ppermute(tail, axis, [(i, (i + 1) % count) for i in range(count)]),
                cells,
                lax.ppermute(head, axis, [((i + 1) % count, i) for i in range(count)]),
            ],
            axis=dim,
        )
    return cells


def sphere(point_count):
    middle = jnp.arange(point_count).astype(jnp.float32) + 0.5
    height = 1.0 - 2.0 * middle / point_count
    radial = jnp.sqrt(jnp.maximum(1.0 - height * height, 0.0))
    angle_turn = middle * golden_turn
    return jnp.stack([radial * jnp.cos(angle_turn), radial * jnp.sin(angle_turn), height])


def point_sum(targets, sources, weights):
    delta_x = targets[0][..., :, None] - sources[0][..., None, :]
    delta_y = targets[1][..., :, None] - sources[1][..., None, :]
    delta_z = targets[2][..., :, None] - sources[2][..., None, :]
    kernel = lax.rsqrt(delta_x * delta_x + delta_y * delta_y + delta_z * delta_z + softening_sq)
    return jnp.sum(kernel * weights[..., None, :], axis=-1)


def translation(unit_sphere, shift_x, shift_y, shift_z, radius):
    delta_x = (
        radius * (unit_sphere[0][:, None] - unit_sphere[0][None, :]) - shift_x[..., None, None]
    )
    delta_y = (
        radius * (unit_sphere[1][:, None] - unit_sphere[1][None, :]) - shift_y[..., None, None]
    )
    delta_z = (
        radius * (unit_sphere[2][:, None] - unit_sphere[2][None, :]) - shift_z[..., None, None]
    )
    return lax.rsqrt(delta_x * delta_x + delta_y * delta_y + delta_z * delta_z + softening_sq)


def child_points(unit_sphere):
    centre = jnp.arange(2).astype(jnp.float32) + 0.5
    point_count = unit_sphere.shape[1]
    box_shape = (2, 2, 2, point_count)
    along_x = jnp.broadcast_to(centre[:, None, None, None] + 0.9 * unit_sphere[0], box_shape)
    along_y = jnp.broadcast_to(centre[None, :, None, None] + 0.9 * unit_sphere[1], box_shape)
    along_z = jnp.broadcast_to(centre[None, None, :, None] + 0.9 * unit_sphere[2], box_shape)
    return jnp.stack([along_x, along_y, along_z]).reshape(3, 8 * point_count)


def rel_gather(buf, axis, dim):
    count = lax.axis_size(axis)
    have = 1
    while have < count:
        step = min(have, count - have)
        part = lax.slice_in_dim(buf, 0, step, axis=dim)
        got = lax.ppermute(part, axis, [(j, (j - have) % count) for j in range(count)])
        buf = jnp.concatenate([buf, got], axis=dim)
        have += step
    return buf


def far_shifts(span):
    shifts = []
    for dx in range(-span, span + 1):
        for dy in range(-span, span + 1):
            for dz in range(-span, span + 1):
                if max(abs(dx), abs(dy), abs(dz)) < 2:
                    continue
                if (dx, dy, dz) > (0, 0, 0):
                    shifts.append((dx, dy, dz))
    return shifts


def shards(offsets, charges, counts, c2e_leaf_up, c2e_leaf_down, c2e_top_up, c2e_top_down):
    slot_count = offsets.shape[-1]
    layers = offsets.shape[3]
    parent_layers = layers // 2
    points = c2e_leaf_up.shape[0]
    unit_sphere = sphere(points)
    slot_index = jnp.arange(slot_count)
    weights = jnp.where(slot_index < counts[..., None], charges, 0.0)
    packed = jnp.concatenate([offsets, weights[None]], axis=0)
    beside_all = padded(packed, (("gx", 1), ("gy", 2)), 1)
    leaf_check_pts = 0.5 + 1.8 * unit_sphere
    leaf_check = point_sum(leaf_check_pts[:, None, None, None, :], offsets, weights)
    leaf_eq = jnp.einsum("ec,xyzc->xyze", c2e_leaf_up, leaf_check, precision=highest)
    children = child_points(unit_sphere)
    parent_weights = (
        leaf_eq.reshape(2, 2, parent_layers, 2, points)
        .transpose(2, 0, 1, 3, 4)
        .reshape(parent_layers, 8 * points)
    )
    parent_check_pts = 1.0 + 3.6 * unit_sphere
    parent_check = point_sum(parent_check_pts[:, None, :], children[:, None, :], parent_weights)
    parent_eq = jnp.einsum("ec,mc->me", c2e_top_up, parent_check, precision=highest)
    count_x = lax.axis_size("gx")
    count_y = lax.axis_size("gy")

    gathered = rel_gather(rel_gather(parent_eq[None, None], "gy", 1), "gx", 0)
    layer_float = jnp.arange(parent_layers).astype(jnp.float32)
    depth_pairs = 2.0 * (layer_float[None, :] - layer_float[:, None])
    pair_ones = jnp.ones((parent_layers, parent_layers), jnp.float32)
    rel_y = jnp.arange(count_y)
    off_y = (rel_y + count_y // 2) % count_y - count_y // 2

    def far_column(rel_x, running):
        off_x = (rel_x + count_x // 2) % count_x - count_x // 2
        keep = ((jnp.abs(off_x) > 1) | (jnp.abs(off_y) > 1)).astype(jnp.float32)
        matrices = translation(
            unit_sphere,
            2.0 * off_x.astype(jnp.float32) * jnp.ones((count_y, parent_layers, parent_layers)),
            2.0 * off_y.astype(jnp.float32)[:, None, None] * pair_ones,
            jnp.broadcast_to(depth_pairs, (count_y, parent_layers, parent_layers)),
            1.8,
        )
        column = lax.dynamic_index_in_dim(gathered, rel_x, 0, keepdims=False)
        sources = column * keep[:, None, None]
        return running + jnp.einsum("ytsce,yse->tc", matrices, sources, precision=highest)

    far_check = lax.fori_loop(
        0, count_x, far_column, jnp.zeros((parent_layers, points), jnp.float32)
    )

    cycle = padded(leaf_eq, (("gx", 0), ("gy", 1)), 2)
    framed = jnp.pad(cycle, ((1, 1), (1, 1), (3, 3), (0, 0)))
    shifts = far_shifts(3)
    chunk = 16
    while len(shifts) % chunk:
        shifts.append((3, 3, 3))
    real = len(far_shifts(3))

    def window(dx, dy, dz):
        return framed[dx + 3 : dx + 5, dy + 3 : dy + 5, dz + 3 : dz + 3 + layers].reshape(
            4 * layers, points
        )

    plus = jnp.stack(
        [window(*d) if i < real else jnp.zeros((4 * layers, points)) for i, d in enumerate(shifts)]
    )
    minus = jnp.stack(
        [
            window(-d[0], -d[1], -d[2]) if i < real else jnp.zeros((4 * layers, points))
            for i, d in enumerate(shifts)
        ]
    )
    table = jnp.array(shifts, jnp.float32)
    groups = len(shifts) // chunk
    plus = plus.reshape(groups, chunk, 4 * layers, points)
    minus = minus.reshape(groups, chunk, 4 * layers, points)
    table = table.reshape(groups, chunk, 3)

    def list_chunk(running, parts):
        shift, fwd, back = parts
        matrices = translation(unit_sphere, shift[:, 0], shift[:, 1], shift[:, 2], 0.9)
        running = running + jnp.einsum("dce,dne->nc", matrices, fwd, precision=highest)
        running = running + jnp.einsum("dec,dne->nc", matrices, back, precision=highest)
        return running, None

    leaf_down_check, _ = lax.scan(
        list_chunk, jnp.zeros((4 * layers, points), jnp.float32), (table, plus, minus)
    )
    leaf_down_check = leaf_down_check.reshape(2, 2, layers, points)
    parent_local = jnp.einsum("ec,mc->me", c2e_top_down, far_check, precision=highest)
    leaf_local = jnp.einsum("ec,xyzc->xyze", c2e_leaf_down, leaf_down_check, precision=highest)

    padded_around = jnp.pad(beside_all, ((0, 0), (0, 0), (0, 0), (1, 1), (0, 0)))
    moves = [(mx, my, mz) for mx in (-1, 0, 1) for my in (-1, 0, 1) for mz in (-1, 0, 1)]
    source = jnp.stack(
        [
            padded_around[:, 1 + mx : 3 + mx, 1 + my : 3 + my, 1 + mz : 1 + mz + layers]
            for mx, my, mz in moves
        ],
        axis=1,
    )
    move = jnp.array(moves, jnp.float32)
    shape5 = (len(moves), 1, 1, 1, 1, 1)
    delta_x = packed[0][None, ..., :, None] - source[0][..., None, :] - move[:, 0].reshape(shape5)
    delta_y = packed[1][None, ..., :, None] - source[1][..., None, :] - move[:, 1].reshape(shape5)
    delta_z = packed[2][None, ..., :, None] - source[2][..., None, :] - move[:, 2].reshape(shape5)
    kernel = lax.rsqrt(delta_x * delta_x + delta_y * delta_y + delta_z * delta_z + softening_sq)
    diagonal = jnp.arange(slot_count)[:, None] == jnp.arange(slot_count)[None, :]
    centre = (jnp.arange(len(moves)) == 13).reshape(shape5)
    kernel = jnp.where(centre & diagonal, 0.0, kernel)
    near = jnp.sum(jnp.sum(kernel * source[3][..., None, :], axis=-1), axis=0)

    leaf_down_pts = 0.5 + 1.8 * unit_sphere
    leaf_far = point_sum(offsets, leaf_down_pts[:, None, None, None, :], leaf_local)
    parent_down_pts = 1.0 + 3.6 * unit_sphere
    local_float = jnp.arange(2).astype(jnp.float32)
    layer_parity = (jnp.arange(layers) % 2).astype(jnp.float32)
    in_parent = jnp.stack(
        [
            local_float[:, None, None, None] + offsets[0],
            local_float[None, :, None, None] + offsets[1],
            layer_parity[None, None, :, None] + offsets[2],
        ]
    )
    spread_local = jnp.repeat(parent_local, 2, axis=0)[None, None]
    parent_far = point_sum(in_parent, parent_down_pts[:, None, None, None, :], spread_local)
    total = near + leaf_far + parent_far
    return jnp.where(slot_index < counts[..., None], total, 0.0)


def solution(mesh):
    return jax.shard_map(
        shards,
        mesh=mesh,
        in_specs=(
            P(None, "gx", "gy", None, None),
            P("gx", "gy", None, None),
            P("gx", "gy", None),
            P(),
            P(),
            P(),
            P(),
        ),
        out_specs=P("gx", "gy", None, None),
        check_vma=False,
    )
```

```python
import jax
import numpy as np
import jax.numpy as jnp
from jax import lax
from jax.sharding import PartitionSpec as P

softening_sq = 0.0004
golden_turn = 2.399963229728653
highest = lax.Precision.HIGHEST


def padded(cells, sides, width):
    for axis, dim in sides:
        count = lax.axis_size(axis)
        head = lax.slice_in_dim(cells, 0, width, axis=dim)
        tail = lax.slice_in_dim(cells, cells.shape[dim] - width, cells.shape[dim], axis=dim)
        cells = jnp.concatenate(
            [
                lax.ppermute(tail, axis, [(i, (i + 1) % count) for i in range(count)]),
                cells,
                lax.ppermute(head, axis, [((i + 1) % count, i) for i in range(count)]),
            ],
            axis=dim,
        )
    return cells


def sphere(point_count):
    middle = jnp.arange(point_count).astype(jnp.float32) + 0.5
    height = 1.0 - 2.0 * middle / point_count
    radial = jnp.sqrt(jnp.maximum(1.0 - height * height, 0.0))
    angle_turn = middle * golden_turn
    return jnp.stack([radial * jnp.cos(angle_turn), radial * jnp.sin(angle_turn), height])


def point_sum(targets, sources, weights):
    delta_x = targets[0][..., :, None] - sources[0][..., None, :]
    delta_y = targets[1][..., :, None] - sources[1][..., None, :]
    delta_z = targets[2][..., :, None] - sources[2][..., None, :]
    kernel = lax.rsqrt(delta_x * delta_x + delta_y * delta_y + delta_z * delta_z + softening_sq)
    return jnp.sum(kernel * weights[..., None, :], axis=-1)


def translation(unit_sphere, shift_x, shift_y, shift_z, radius):
    delta_x = (
        radius * (unit_sphere[0][:, None] - unit_sphere[0][None, :]) - shift_x[..., None, None]
    )
    delta_y = (
        radius * (unit_sphere[1][:, None] - unit_sphere[1][None, :]) - shift_y[..., None, None]
    )
    delta_z = (
        radius * (unit_sphere[2][:, None] - unit_sphere[2][None, :]) - shift_z[..., None, None]
    )
    return lax.rsqrt(delta_x * delta_x + delta_y * delta_y + delta_z * delta_z + softening_sq)


def child_points(unit_sphere):
    centre = jnp.arange(2).astype(jnp.float32) + 0.5
    point_count = unit_sphere.shape[1]
    box_shape = (2, 2, 2, point_count)
    along_x = jnp.broadcast_to(centre[:, None, None, None] + 0.9 * unit_sphere[0], box_shape)
    along_y = jnp.broadcast_to(centre[None, :, None, None] + 0.9 * unit_sphere[1], box_shape)
    along_z = jnp.broadcast_to(centre[None, None, :, None] + 0.9 * unit_sphere[2], box_shape)
    return jnp.stack([along_x, along_y, along_z]).reshape(3, 8 * point_count)


def rel_gather(buf, axis, dim):
    count = lax.axis_size(axis)
    have = 1
    while have < count:
        step = min(have, count - have)
        part = lax.slice_in_dim(buf, 0, step, axis=dim)
        got = lax.ppermute(part, axis, [(j, (j - have) % count) for j in range(count)])
        buf = jnp.concatenate([buf, got], axis=dim)
        have += step
    return buf


def shards(offsets, charges, counts, c2e_leaf_up, c2e_leaf_down, c2e_top_up, c2e_top_down):
    slot_count = offsets.shape[-1]
    layers = offsets.shape[3]
    parent_layers = layers // 2
    points = c2e_leaf_up.shape[0]
    unit_sphere = sphere(points)
    slot_index = jnp.arange(slot_count)
    weights = jnp.where(slot_index < counts[..., None], charges, 0.0)
    packed = jnp.concatenate([offsets, weights[None]], axis=0)
    beside_all = padded(packed, (("gx", 1), ("gy", 2)), 1)
    leaf_check_pts = 0.5 + 1.8 * unit_sphere
    leaf_check = point_sum(leaf_check_pts[:, None, None, None, :], offsets, weights)
    leaf_eq = jnp.einsum("ec,xyzc->xyze", c2e_leaf_up, leaf_check, precision=highest)
    children = child_points(unit_sphere)
    parent_weights = (
        leaf_eq.reshape(2, 2, parent_layers, 2, points)
        .transpose(2, 0, 1, 3, 4)
        .reshape(parent_layers, 8 * points)
    )
    parent_check_pts = 1.0 + 3.6 * unit_sphere
    parent_check = point_sum(parent_check_pts[:, None, :], children[:, None, :], parent_weights)
    parent_eq = jnp.einsum("ec,mc->me", c2e_top_up, parent_check, precision=highest)
    count_x = lax.axis_size("gx")
    count_y = lax.axis_size("gy")

    gathered = rel_gather(rel_gather(parent_eq[None, None], "gy", 1), "gx", 0)
    kept = []
    for rel_x in range(count_x):
        for rel_y in range(count_y):
            off_x = (rel_x + count_x // 2) % count_x - count_x // 2
            off_y = (rel_y + count_y // 2) % count_y - count_y // 2
            if abs(off_x) > 1 or abs(off_y) > 1:
                kept.append((rel_x * count_y + rel_y, off_x, off_y))
    kept_index = np.array([k[0] for k in kept], np.int32)
    kept_x = np.array([2.0 * k[1] for k in kept], np.float32)
    kept_y = np.array([2.0 * k[2] for k in kept], np.float32)
    far_sources = jnp.take(gathered.reshape(count_x * count_y, parent_layers, points), kept_index, axis=0)
    layer_float = jnp.arange(parent_layers).astype(jnp.float32)
    depth_pairs = 2.0 * (layer_float[None, :] - layer_float[:, None])
    far_shape = (parent_layers, len(kept), parent_layers, points)
    source_pts = jnp.stack(
        [
            jnp.broadcast_to(kept_x[None, :, None, None] + 1.8 * unit_sphere[0], far_shape),
            jnp.broadcast_to(kept_y[None, :, None, None] + 1.8 * unit_sphere[1], far_shape),
            jnp.broadcast_to(depth_pairs[:, None, :, None] + 1.8 * unit_sphere[2], far_shape),
        ]
    ).reshape(3, parent_layers, -1)
    far_check = point_sum(
        jnp.broadcast_to(1.8 * unit_sphere[:, None, :], (3, parent_layers, points)),
        source_pts,
        far_sources.reshape(-1),
    )

    local_index = jnp.arange(2)
    layer_index = jnp.arange(layers)
    depth_shift = jnp.arange(7) - 3
    depth_float = depth_shift.astype(jnp.float32)
    seven_ones = jnp.ones((7,), jnp.float32)
    valid_z = (layer_index[None, :] + depth_shift[:, None] >= 0) & (
        layer_index[None, :] + depth_shift[:, None] <= layers - 1
    )
    cycle = padded(leaf_eq, (("gx", 0), ("gy", 1)), 2)
    framed = jnp.pad(cycle, ((1, 1), (1, 1), (3, 3), (0, 0)))

    def list_row(offset_x, running):
        shift_x = offset_x - 3
        valid_x = (local_index + shift_x >= -2) & (local_index + shift_x <= 3)
        for offset_y in range(7):
            shift_y = offset_y - 3
            valid_y = (local_index + shift_y >= -2) & (local_index + shift_y <= 3)
            block = lax.dynamic_slice(
                framed, (offset_x, offset_y, 0, 0), (2, 2, layers + 6, points)
            )
            stacked = jnp.stack([block[:, :, depth : depth + layers] for depth in range(7)])
            far_enough = (jnp.abs(shift_x) > 1) | (abs(shift_y) > 1) | (jnp.abs(depth_shift) > 1)
            keep = (
                valid_x[None, :, None, None]
                & valid_y[None, None, :, None]
                & valid_z[:, None, None, :]
                & far_enough[:, None, None, None]
            )
            matrices = translation(
                unit_sphere,
                shift_x.astype(jnp.float32) * seven_ones,
                float(shift_y) * seven_ones,
                depth_float,
                0.9,
            )
            sources = jnp.where(keep[..., None], stacked, 0.0)
            running = running + jnp.einsum("zce,zijke->ijkc", matrices, sources, precision=highest)
        return running

    leaf_down_check = lax.fori_loop(0, 7, list_row, jnp.zeros((2, 2, layers, points), jnp.float32))
    parent_local = jnp.einsum("ec,mc->me", c2e_top_down, far_check, precision=highest)
    leaf_local = jnp.einsum("ec,xyzc->xyze", c2e_leaf_down, leaf_down_check, precision=highest)

    padded_around = jnp.pad(beside_all, ((0, 0), (0, 0), (0, 0), (1, 1), (0, 0)))
    around_shape = padded_around.shape[1:4]
    moves = [(mx, my, mz) for mx in (-1, 0, 1) for my in (-1, 0, 1) for mz in (-1, 0, 1)]
    box_rows = np.array(
        [
            [
                np.ravel_multi_index((bx + 1 + mx, by + 1 + my, bz + 1 + mz), around_shape)
                for bx in range(2)
                for by in range(2)
                for bz in range(layers)
            ]
            for mx, my, mz in moves
        ],
        np.int32,
    )
    source = jnp.take(
        padded_around.reshape(4, -1, slot_count), box_rows, axis=1
    ).reshape(4, len(moves), 2, 2, layers, slot_count)
    move = jnp.array(moves, jnp.float32)
    shape6 = (len(moves), 1, 1, 1, 1, 1)
    delta_x = packed[0][None, ..., :, None] - source[0][..., None, :] - move[:, 0].reshape(shape6)
    delta_y = packed[1][None, ..., :, None] - source[1][..., None, :] - move[:, 1].reshape(shape6)
    delta_z = packed[2][None, ..., :, None] - source[2][..., None, :] - move[:, 2].reshape(shape6)
    kernel = lax.rsqrt(delta_x * delta_x + delta_y * delta_y + delta_z * delta_z + softening_sq)
    diagonal = jnp.arange(slot_count)[:, None] == jnp.arange(slot_count)[None, :]
    centre = (jnp.arange(len(moves)) == 13).reshape(shape6)
    kernel = jnp.where(centre & diagonal, 0.0, kernel)
    near = jnp.sum(jnp.sum(kernel * source[3][..., None, :], axis=-1), axis=0)

    leaf_down_pts = 0.5 + 1.8 * unit_sphere
    leaf_far = point_sum(offsets, leaf_down_pts[:, None, None, None, :], leaf_local)
    parent_down_pts = 1.0 + 3.6 * unit_sphere
    local_float = jnp.arange(2).astype(jnp.float32)
    layer_parity = (jnp.arange(layers) % 2).astype(jnp.float32)
    in_parent = jnp.stack(
        [
            local_float[:, None, None, None] + offsets[0],
            local_float[None, :, None, None] + offsets[1],
            layer_parity[None, None, :, None] + offsets[2],
        ]
    )
    spread_local = jnp.repeat(parent_local, 2, axis=0)[None, None]
    parent_far = point_sum(in_parent, parent_down_pts[:, None, None, None, :], spread_local)
    total = near + leaf_far + parent_far
    return jnp.where(slot_index < counts[..., None], total, 0.0)


def solution(mesh):
    return jax.shard_map(
        shards,
        mesh=mesh,
        in_specs=(
            P(None, "gx", "gy", None, None),
            P("gx", "gy", None, None),
            P("gx", "gy", None),
            P(),
            P(),
            P(),
            P(),
        ),
        out_specs=P("gx", "gy", None, None),
        check_vma=False,
    )
```

```python
import functools

import jax
import numpy as np
import jax.numpy as jnp
from jax import lax
from jax.experimental import pallas as pl
from jax.experimental.pallas import tpu as pltpu
from jax.sharding import PartitionSpec as P

softening_sq = 0.0004
golden_turn = 2.399963229728653
highest = lax.Precision.HIGHEST


def sphere(point_count):
    middle = jnp.arange(point_count).astype(jnp.float32) + 0.5
    height = 1.0 - 2.0 * middle / point_count
    radial = jnp.sqrt(jnp.maximum(1.0 - height * height, 0.0))
    angle_turn = middle * golden_turn
    return jnp.stack([radial * jnp.cos(angle_turn), radial * jnp.sin(angle_turn), height])


def point_sum(targets, sources, weights):
    delta_x = targets[0][..., :, None] - sources[0][..., None, :]
    delta_y = targets[1][..., :, None] - sources[1][..., None, :]
    delta_z = targets[2][..., :, None] - sources[2][..., None, :]
    kernel = lax.rsqrt(delta_x * delta_x + delta_y * delta_y + delta_z * delta_z + softening_sq)
    return jnp.sum(kernel * weights[..., None, :], axis=-1)


def translation(unit_sphere, shift_x, shift_y, shift_z, radius):
    delta_x = (
        radius * (unit_sphere[0][:, None] - unit_sphere[0][None, :]) - shift_x[..., None, None]
    )
    delta_y = (
        radius * (unit_sphere[1][:, None] - unit_sphere[1][None, :]) - shift_y[..., None, None]
    )
    delta_z = (
        radius * (unit_sphere[2][:, None] - unit_sphere[2][None, :]) - shift_z[..., None, None]
    )
    return lax.rsqrt(delta_x * delta_x + delta_y * delta_y + delta_z * delta_z + softening_sq)


def child_points(unit_sphere):
    centre = jnp.arange(2).astype(jnp.float32) + 0.5
    point_count = unit_sphere.shape[1]
    box_shape = (2, 2, 2, point_count)
    along_x = jnp.broadcast_to(centre[:, None, None, None] + 0.9 * unit_sphere[0], box_shape)
    along_y = jnp.broadcast_to(centre[None, :, None, None] + 0.9 * unit_sphere[1], box_shape)
    along_z = jnp.broadcast_to(centre[None, None, :, None] + 0.9 * unit_sphere[2], box_shape)
    return jnp.stack([along_x, along_y, along_z]).reshape(3, 8 * point_count)


def rel_gather(buf, axis, dim):
    count = lax.axis_size(axis)
    have = 1
    while have < count:
        step = min(have, count - have)
        part = lax.slice_in_dim(buf, 0, step, axis=dim)
        got = lax.ppermute(part, axis, [(j, (j - have) % count) for j in range(count)])
        buf = jnp.concatenate([buf, got], axis=dim)
        have += step
    return buf


def exchange(items, axis):
    count = lax.axis_size(axis)
    heads, tails = [], []
    for cells, dim, width in items:
        heads.append(lax.slice_in_dim(cells, 0, width, axis=dim))
        tails.append(lax.slice_in_dim(cells, cells.shape[dim] - width, cells.shape[dim], axis=dim))
    sent_tail = jnp.concatenate([t.reshape(-1) for t in tails])
    sent_head = jnp.concatenate([h.reshape(-1) for h in heads])
    from_left = lax.ppermute(sent_tail, axis, [(i, (i + 1) % count) for i in range(count)])
    from_right = lax.ppermute(sent_head, axis, [((i + 1) % count, i) for i in range(count)])
    out, start = [], 0
    for (cells, dim, width), head, tail in zip(items, heads, tails):
        size = head.size
        before = from_left[start : start + size].reshape(tail.shape)
        after = from_right[start : start + size].reshape(head.shape)
        out.append(jnp.concatenate([before, cells, after], axis=dim))
        start += size
    return out


def m2l_kernel(shift_count, rows, table_ref, base_ref, plus_ref, minus_ref, out_ref):
    out_ref[...] = jnp.zeros_like(out_ref)

    def body(index, carry):
        shift_x = table_ref[3 * index]
        shift_y = table_ref[3 * index + 1]
        shift_z = table_ref[3 * index + 2]
        fwd = plus_ref[index]
        back = minus_ref[index]
        for row in range(0, base_ref.shape[1], rows):
            delta_x = base_ref[0, row : row + rows, :] - shift_x
            delta_y = base_ref[1, row : row + rows, :] - shift_y
            delta_z = base_ref[2, row : row + rows, :] - shift_z
            matrix = lax.rsqrt(
                delta_x * delta_x + delta_y * delta_y + delta_z * delta_z + softening_sq
            )
            out_ref[:, row : row + rows] += lax.dot_general(
                fwd,
                matrix,
                (((1,), (1,)), ((), ())),
                precision=highest,
                preferred_element_type=jnp.float32,
            )
            out_ref[...] += lax.dot_general(
                back[:, row : row + rows],
                matrix,
                (((1,), (0,)), ((), ())),
                precision=highest,
                preferred_element_type=jnp.float32,
            )
        return carry

    lax.fori_loop(0, shift_count, body, 0)


def m2l(table, base, plus, minus):
    shift_count, vectors, points = plus.shape
    return pl.pallas_call(
        functools.partial(m2l_kernel, shift_count, 128),
        out_shape=jax.ShapeDtypeStruct((vectors, points), jnp.float32),
        in_specs=[
            pl.BlockSpec(memory_space=pltpu.SMEM),
            pl.BlockSpec(memory_space=pltpu.VMEM),
            pl.BlockSpec(memory_space=pltpu.VMEM),
            pl.BlockSpec(memory_space=pltpu.VMEM),
        ],
        out_specs=pl.BlockSpec(memory_space=pltpu.VMEM),
        compiler_params=pltpu.CompilerParams(vmem_limit_bytes=48 * 1024 * 1024),
        cost_estimate=pl.CostEstimate(
            flops=4 * shift_count * vectors * points * points + 10 * shift_count * points * points,
            transcendentals=shift_count * points * points,
            bytes_accessed=4 * (2 * plus.size + base.size + vectors * points),
        ),
    )(table, base, plus, minus)


def far_shifts(span):
    shifts = []
    for dx in range(-span, span + 1):
        for dy in range(-span, span + 1):
            for dz in range(-span, span + 1):
                if max(abs(dx), abs(dy), abs(dz)) >= 2 and (dx, dy, dz) > (0, 0, 0):
                    shifts.append((dx, dy, dz))
    return shifts


def shards(offsets, charges, counts, c2e_leaf_up, c2e_leaf_down, c2e_top_up, c2e_top_down):
    slot_count = offsets.shape[-1]
    layers = offsets.shape[3]
    parent_layers = layers // 2
    points = c2e_leaf_up.shape[0]
    unit_sphere = sphere(points)
    slot_index = jnp.arange(slot_count)
    weights = jnp.where(slot_index < counts[..., None], charges, 0.0)
    packed = jnp.concatenate([offsets, weights[None]], axis=0)
    leaf_check_pts = 0.5 + 1.8 * unit_sphere
    leaf_check = point_sum(leaf_check_pts[:, None, None, None, :], offsets, weights)
    leaf_eq = jnp.einsum("ec,xyzc->xyze", c2e_leaf_up, leaf_check, precision=highest)
    packed_x, eq_x = exchange([(packed, 1, 1), (leaf_eq, 0, 2)], "gx")
    beside_all, cycle = exchange([(packed_x, 2, 1), (eq_x, 1, 2)], "gy")
    children = child_points(unit_sphere)
    parent_weights = (
        leaf_eq.reshape(2, 2, parent_layers, 2, points)
        .transpose(2, 0, 1, 3, 4)
        .reshape(parent_layers, 8 * points)
    )
    parent_check_pts = 1.0 + 3.6 * unit_sphere
    parent_check = point_sum(parent_check_pts[:, None, :], children[:, None, :], parent_weights)
    parent_eq = jnp.einsum("ec,mc->me", c2e_top_up, parent_check, precision=highest)
    count_x = lax.axis_size("gx")
    count_y = lax.axis_size("gy")

    gathered = rel_gather(rel_gather(parent_eq[None, None], "gy", 1), "gx", 0)
    kept = []
    for rel_x in range(count_x):
        for rel_y in range(count_y):
            off_x = (rel_x + count_x // 2) % count_x - count_x // 2
            off_y = (rel_y + count_y // 2) % count_y - count_y // 2
            if abs(off_x) > 1 or abs(off_y) > 1:
                kept.append((rel_x * count_y + rel_y, off_x, off_y))
    kept_index = np.array([k[0] for k in kept], np.int32)
    kept_x = np.array([2.0 * k[1] for k in kept], np.float32)
    kept_y = np.array([2.0 * k[2] for k in kept], np.float32)
    far_sources = jnp.take(gathered.reshape(count_x * count_y, parent_layers, points), kept_index, axis=0)
    layer_float = jnp.arange(parent_layers).astype(jnp.float32)
    depth_pairs = 2.0 * (layer_float[None, :] - layer_float[:, None])
    far_shape = (parent_layers, len(kept), parent_layers, points)
    source_pts = jnp.stack(
        [
            jnp.broadcast_to(kept_x[None, :, None, None] + 1.8 * unit_sphere[0], far_shape),
            jnp.broadcast_to(kept_y[None, :, None, None] + 1.8 * unit_sphere[1], far_shape),
            jnp.broadcast_to(depth_pairs[:, None, :, None] + 1.8 * unit_sphere[2], far_shape),
        ]
    ).reshape(3, parent_layers, -1)
    far_check = point_sum(
        jnp.broadcast_to(1.8 * unit_sphere[:, None, :], (3, parent_layers, points)),
        source_pts,
        far_sources.reshape(-1),
    )

    framed = jnp.pad(cycle, ((1, 1), (1, 1), (3, 3), (0, 0)))
    shifts = far_shifts(3)
    targets = [(ix, iy, k) for ix in range(2) for iy in range(2) for k in range(layers)]

    def rows_for(sign):
        return np.array(
            [
                [
                    np.ravel_multi_index(
                        (ix + sign * dx + 3, iy + sign * dy + 3, k + sign * dz + 3), framed.shape[:3]
                    )
                    for ix, iy, k in targets
                ]
                for dx, dy, dz in shifts
            ],
            np.int32,
        )

    framed_rows = framed.reshape(-1, points)
    plus = jnp.take(framed_rows, rows_for(1), axis=0)
    minus = jnp.take(framed_rows, rows_for(-1), axis=0)
    base = jnp.stack(
        [0.9 * (unit_sphere[i][:, None] - unit_sphere[i][None, :]) for i in range(3)]
    )
    table = jnp.asarray(np.array(shifts, np.float32).reshape(-1))
    leaf_down_check = m2l(table, base, plus, minus).reshape(2, 2, layers, points)
    parent_local = jnp.einsum("ec,mc->me", c2e_top_down, far_check, precision=highest)
    leaf_local = jnp.einsum("ec,xyzc->xyze", c2e_leaf_down, leaf_down_check, precision=highest)

    padded_around = jnp.pad(beside_all, ((0, 0), (0, 0), (0, 0), (1, 1), (0, 0)))
    around_shape = padded_around.shape[1:4]
    moves = [(mx, my, mz) for mx in (-1, 0, 1) for my in (-1, 0, 1) for mz in (-1, 0, 1)]
    box_rows = np.array(
        [
            [
                np.ravel_multi_index((bx + 1 + mx, by + 1 + my, bz + 1 + mz), around_shape)
                for bx in range(2)
                for by in range(2)
                for bz in range(layers)
            ]
            for mx, my, mz in moves
        ],
        np.int32,
    )
    source = jnp.take(
        padded_around.reshape(4, -1, slot_count), box_rows, axis=1
    ).reshape(4, len(moves), 2, 2, layers, slot_count)
    move = jnp.array(moves, jnp.float32)
    shape6 = (len(moves), 1, 1, 1, 1, 1)
    delta_x = packed[0][None, ..., :, None] - source[0][..., None, :] - move[:, 0].reshape(shape6)
    delta_y = packed[1][None, ..., :, None] - source[1][..., None, :] - move[:, 1].reshape(shape6)
    delta_z = packed[2][None, ..., :, None] - source[2][..., None, :] - move[:, 2].reshape(shape6)
    kernel = lax.rsqrt(delta_x * delta_x + delta_y * delta_y + delta_z * delta_z + softening_sq)
    diagonal = jnp.arange(slot_count)[:, None] == jnp.arange(slot_count)[None, :]
    centre = (jnp.arange(len(moves)) == 13).reshape(shape6)
    kernel = jnp.where(centre & diagonal, 0.0, kernel)
    near = jnp.sum(jnp.sum(kernel * source[3][..., None, :], axis=-1), axis=0)

    leaf_down_pts = 0.5 + 1.8 * unit_sphere
    leaf_far = point_sum(offsets, leaf_down_pts[:, None, None, None, :], leaf_local)
    parent_down_pts = 1.0 + 3.6 * unit_sphere
    local_float = jnp.arange(2).astype(jnp.float32)
    layer_parity = (jnp.arange(layers) % 2).astype(jnp.float32)
    in_parent = jnp.stack(
        [
            local_float[:, None, None, None] + offsets[0],
            local_float[None, :, None, None] + offsets[1],
            layer_parity[None, None, :, None] + offsets[2],
        ]
    )
    spread_local = jnp.repeat(parent_local, 2, axis=0)[None, None]
    parent_far = point_sum(in_parent, parent_down_pts[:, None, None, None, :], spread_local)
    total = near + leaf_far + parent_far
    return jnp.where(slot_index < counts[..., None], total, 0.0)


def solution(mesh):
    return jax.shard_map(
        shards,
        mesh=mesh,
        in_specs=(
            P(None, "gx", "gy", None, None),
            P("gx", "gy", None, None),
            P("gx", "gy", None),
            P(),
            P(),
            P(),
            P(),
        ),
        out_specs=P("gx", "gy", None, None),
        check_vma=False,
    )
```

```python
import functools

import jax
import numpy as np
import jax.numpy as jnp
from jax import lax
from jax.experimental import pallas as pl
from jax.experimental.pallas import tpu as pltpu
from jax.sharding import PartitionSpec as P

softening_sq = 0.0004
golden_turn = 2.399963229728653
highest = lax.Precision.HIGHEST


def sphere(point_count):
    middle = jnp.arange(point_count).astype(jnp.float32) + 0.5
    height = 1.0 - 2.0 * middle / point_count
    radial = jnp.sqrt(jnp.maximum(1.0 - height * height, 0.0))
    angle_turn = middle * golden_turn
    return jnp.stack([radial * jnp.cos(angle_turn), radial * jnp.sin(angle_turn), height])


def point_sum(targets, sources, weights):
    delta_x = targets[0][..., :, None] - sources[0][..., None, :]
    delta_y = targets[1][..., :, None] - sources[1][..., None, :]
    delta_z = targets[2][..., :, None] - sources[2][..., None, :]
    kernel = lax.rsqrt(delta_x * delta_x + delta_y * delta_y + delta_z * delta_z + softening_sq)
    return jnp.sum(kernel * weights[..., None, :], axis=-1)


def translation(unit_sphere, shift_x, shift_y, shift_z, radius):
    delta_x = (
        radius * (unit_sphere[0][:, None] - unit_sphere[0][None, :]) - shift_x[..., None, None]
    )
    delta_y = (
        radius * (unit_sphere[1][:, None] - unit_sphere[1][None, :]) - shift_y[..., None, None]
    )
    delta_z = (
        radius * (unit_sphere[2][:, None] - unit_sphere[2][None, :]) - shift_z[..., None, None]
    )
    return lax.rsqrt(delta_x * delta_x + delta_y * delta_y + delta_z * delta_z + softening_sq)


def child_points(unit_sphere):
    centre = jnp.arange(2).astype(jnp.float32) + 0.5
    point_count = unit_sphere.shape[1]
    box_shape = (2, 2, 2, point_count)
    along_x = jnp.broadcast_to(centre[:, None, None, None] + 0.9 * unit_sphere[0], box_shape)
    along_y = jnp.broadcast_to(centre[None, :, None, None] + 0.9 * unit_sphere[1], box_shape)
    along_z = jnp.broadcast_to(centre[None, None, :, None] + 0.9 * unit_sphere[2], box_shape)
    return jnp.stack([along_x, along_y, along_z]).reshape(3, 8 * point_count)


def rel_gather(buf, axis, dim):
    count = lax.axis_size(axis)
    have = 1
    while have < count:
        step = min(have, count - have)
        part = lax.slice_in_dim(buf, 0, step, axis=dim)
        got = lax.ppermute(part, axis, [(j, (j - have) % count) for j in range(count)])
        buf = jnp.concatenate([buf, got], axis=dim)
        have += step
    return buf


def exchange(items, axis):
    count = lax.axis_size(axis)
    heads, tails = [], []
    for cells, dim, width in items:
        heads.append(lax.slice_in_dim(cells, 0, width, axis=dim))
        tails.append(lax.slice_in_dim(cells, cells.shape[dim] - width, cells.shape[dim], axis=dim))
    sent_tail = jnp.concatenate([t.reshape(-1) for t in tails])
    sent_head = jnp.concatenate([h.reshape(-1) for h in heads])
    from_left = lax.ppermute(sent_tail, axis, [(i, (i + 1) % count) for i in range(count)])
    from_right = lax.ppermute(sent_head, axis, [((i + 1) % count, i) for i in range(count)])
    out, start = [], 0
    for (cells, dim, width), head, tail in zip(items, heads, tails):
        size = head.size
        before = from_left[start : start + size].reshape(tail.shape)
        after = from_right[start : start + size].reshape(head.shape)
        out.append(jnp.concatenate([before, cells, after], axis=dim))
        start += size
    return out


def m2l_kernel(shift_count, rows, table_ref, base_ref, sources_ref, out_ref):
    out_ref[...] = jnp.zeros_like(out_ref)

    def body(index, carry):
        shift_x = table_ref[3 * index]
        shift_y = table_ref[3 * index + 1]
        shift_z = table_ref[3 * index + 2]
        fwd = sources_ref[0, index]
        back = sources_ref[1, index]
        for row in range(0, base_ref.shape[1], rows):
            delta_x = base_ref[0, row : row + rows, :] - shift_x
            delta_y = base_ref[1, row : row + rows, :] - shift_y
            delta_z = base_ref[2, row : row + rows, :] - shift_z
            matrix = lax.rsqrt(
                delta_x * delta_x + delta_y * delta_y + delta_z * delta_z + softening_sq
            )
            out_ref[:, row : row + rows] += lax.dot_general(
                fwd,
                matrix,
                (((1,), (1,)), ((), ())),
                precision=highest,
                preferred_element_type=jnp.float32,
            )
            out_ref[...] += lax.dot_general(
                back[:, row : row + rows],
                matrix,
                (((1,), (0,)), ((), ())),
                precision=highest,
                preferred_element_type=jnp.float32,
            )
        return carry

    lax.fori_loop(0, shift_count, body, 0)


def m2l(table, base, sources):
    shift_count, vectors, points = sources.shape[1:]
    return pl.pallas_call(
        functools.partial(m2l_kernel, shift_count, 128),
        out_shape=jax.ShapeDtypeStruct((vectors, points), jnp.float32),
        in_specs=[
            pl.BlockSpec(memory_space=pltpu.SMEM),
            pl.BlockSpec(memory_space=pltpu.VMEM),
            pl.BlockSpec(memory_space=pltpu.VMEM),
        ],
        out_specs=pl.BlockSpec(memory_space=pltpu.VMEM),
        compiler_params=pltpu.CompilerParams(vmem_limit_bytes=48 * 1024 * 1024),
        cost_estimate=pl.CostEstimate(
            flops=4 * shift_count * vectors * points * points + 10 * shift_count * points * points,
            transcendentals=shift_count * points * points,
            bytes_accessed=4 * (sources.size + base.size + vectors * points),
        ),
    )(table, base, sources)


def far_shifts(span):
    shifts = []
    for dx in range(-span, span + 1):
        for dy in range(-span, span + 1):
            for dz in range(-span, span + 1):
                if max(abs(dx), abs(dy), abs(dz)) >= 2 and (dx, dy, dz) > (0, 0, 0):
                    shifts.append((dx, dy, dz))
    return shifts


def shards(offsets, charges, counts, c2e_leaf_up, c2e_leaf_down, c2e_top_up, c2e_top_down):
    slot_count = offsets.shape[-1]
    layers = offsets.shape[3]
    parent_layers = layers // 2
    points = c2e_leaf_up.shape[0]
    unit_sphere = sphere(points)
    slot_index = jnp.arange(slot_count)
    weights = jnp.where(slot_index < counts[..., None], charges, 0.0)
    packed = jnp.concatenate([offsets, weights[None]], axis=0)
    leaf_check_pts = 0.5 + 1.8 * unit_sphere
    leaf_check = point_sum(leaf_check_pts[:, None, None, None, :], offsets, weights)
    leaf_eq = jnp.einsum("ec,xyzc->xyze", c2e_leaf_up, leaf_check, precision=highest)
    packed_x, eq_x = exchange([(packed, 1, 1), (leaf_eq, 0, 2)], "gx")
    beside_all, cycle = exchange([(packed_x, 2, 1), (eq_x, 1, 2)], "gy")
    children = child_points(unit_sphere)
    parent_weights = (
        leaf_eq.reshape(2, 2, parent_layers, 2, points)
        .transpose(2, 0, 1, 3, 4)
        .reshape(parent_layers, 8 * points)
    )
    parent_check_pts = 1.0 + 3.6 * unit_sphere
    parent_check = point_sum(parent_check_pts[:, None, :], children[:, None, :], parent_weights)
    parent_eq = jnp.einsum("ec,mc->me", c2e_top_up, parent_check, precision=highest)
    count_x = lax.axis_size("gx")
    count_y = lax.axis_size("gy")

    gathered = rel_gather(rel_gather(parent_eq[None, None], "gy", 1), "gx", 0)
    kept = []
    for rel_x in range(count_x):
        for rel_y in range(count_y):
            off_x = (rel_x + count_x // 2) % count_x - count_x // 2
            off_y = (rel_y + count_y // 2) % count_y - count_y // 2
            if abs(off_x) > 1 or abs(off_y) > 1:
                kept.append((rel_x * count_y + rel_y, off_x, off_y))
    kept_index = np.array([k[0] for k in kept], np.int32)
    kept_x = np.array([2.0 * k[1] for k in kept], np.float32)
    kept_y = np.array([2.0 * k[2] for k in kept], np.float32)
    far_sources = jnp.take(gathered.reshape(count_x * count_y, parent_layers, points), kept_index, axis=0)
    layer_float = jnp.arange(parent_layers).astype(jnp.float32)
    depth_pairs = 2.0 * (layer_float[None, :] - layer_float[:, None])
    far_shape = (parent_layers, len(kept), parent_layers, points)
    source_pts = jnp.stack(
        [
            jnp.broadcast_to(kept_x[None, :, None, None] + 1.8 * unit_sphere[0], far_shape),
            jnp.broadcast_to(kept_y[None, :, None, None] + 1.8 * unit_sphere[1], far_shape),
            jnp.broadcast_to(depth_pairs[:, None, :, None] + 1.8 * unit_sphere[2], far_shape),
        ]
    ).reshape(3, parent_layers, -1)
    far_check = point_sum(
        jnp.broadcast_to(1.8 * unit_sphere[:, None, :], (3, parent_layers, points)),
        source_pts,
        far_sources.reshape(-1),
    )

    framed = jnp.pad(cycle, ((1, 1), (1, 1), (3, 3), (0, 0)))
    shifts = far_shifts(3)
    depth_windows = jnp.stack(
        [framed[:, :, depth : depth + layers] for depth in range(7)], axis=2
    ).reshape(-1, layers * points)
    window_rows = np.array(
        [
            [
                [
                    np.ravel_multi_index(
                        (ix + sign * dx + 3, iy + sign * dy + 3, sign * dz + 3), framed.shape[:2] + (7,)
                    )
                    for ix in range(2)
                    for iy in range(2)
                ]
                for dx, dy, dz in shifts
            ]
            for sign in (1, -1)
        ],
        np.int32,
    )
    sources = jnp.take(depth_windows, window_rows, axis=0).reshape(2, len(shifts), 4 * layers, points)
    base = jnp.stack(
        [0.9 * (unit_sphere[i][:, None] - unit_sphere[i][None, :]) for i in range(3)]
    )
    table = jnp.asarray(np.array(shifts, np.float32).reshape(-1))
    leaf_down_check = m2l(table, base, sources).reshape(2, 2, layers, points)
    parent_local = jnp.einsum("ec,mc->me", c2e_top_down, far_check, precision=highest)
    leaf_local = jnp.einsum("ec,xyzc->xyze", c2e_leaf_down, leaf_down_check, precision=highest)

    padded_around = jnp.pad(beside_all, ((0, 0), (0, 0), (0, 0), (1, 1), (0, 0)))
    around_shape = padded_around.shape[1:4]
    moves = [(mx, my, mz) for mx in (-1, 0, 1) for my in (-1, 0, 1) for mz in (-1, 0, 1)]
    box_rows = np.array(
        [
            [
                np.ravel_multi_index((bx + 1 + mx, by + 1 + my, bz + 1 + mz), around_shape)
                for bx in range(2)
                for by in range(2)
                for bz in range(layers)
            ]
            for mx, my, mz in moves
        ],
        np.int32,
    )
    source = jnp.take(
        padded_around.reshape(4, -1, slot_count), box_rows, axis=1
    ).reshape(4, len(moves), 2, 2, layers, slot_count)
    move = jnp.array(moves, jnp.float32)
    shape6 = (len(moves), 1, 1, 1, 1, 1)
    delta_x = packed[0][None, ..., :, None] - source[0][..., None, :] - move[:, 0].reshape(shape6)
    delta_y = packed[1][None, ..., :, None] - source[1][..., None, :] - move[:, 1].reshape(shape6)
    delta_z = packed[2][None, ..., :, None] - source[2][..., None, :] - move[:, 2].reshape(shape6)
    kernel = lax.rsqrt(delta_x * delta_x + delta_y * delta_y + delta_z * delta_z + softening_sq)
    diagonal = jnp.arange(slot_count)[:, None] == jnp.arange(slot_count)[None, :]
    centre = (jnp.arange(len(moves)) == 13).reshape(shape6)
    kernel = jnp.where(centre & diagonal, 0.0, kernel)
    near = jnp.sum(jnp.sum(kernel * source[3][..., None, :], axis=-1), axis=0)

    leaf_down_pts = 0.5 + 1.8 * unit_sphere
    leaf_far = point_sum(offsets, leaf_down_pts[:, None, None, None, :], leaf_local)
    parent_down_pts = 1.0 + 3.6 * unit_sphere
    local_float = jnp.arange(2).astype(jnp.float32)
    layer_parity = (jnp.arange(layers) % 2).astype(jnp.float32)
    in_parent = jnp.stack(
        [
            local_float[:, None, None, None] + offsets[0],
            local_float[None, :, None, None] + offsets[1],
            layer_parity[None, None, :, None] + offsets[2],
        ]
    )
    spread_local = jnp.repeat(parent_local, 2, axis=0)[None, None]
    parent_far = point_sum(in_parent, parent_down_pts[:, None, None, None, :], spread_local)
    total = near + leaf_far + parent_far
    return jnp.where(slot_index < counts[..., None], total, 0.0)


def solution(mesh):
    return jax.shard_map(
        shards,
        mesh=mesh,
        in_specs=(
            P(None, "gx", "gy", None, None),
            P("gx", "gy", None, None),
            P("gx", "gy", None),
            P(),
            P(),
            P(),
            P(),
        ),
        out_specs=P("gx", "gy", None, None),
        check_vma=False,
    )
```

```python
import functools

import jax
import numpy as np
import jax.numpy as jnp
from jax import lax
from jax.experimental import pallas as pl
from jax.experimental.pallas import tpu as pltpu
from jax.sharding import PartitionSpec as P

softening_sq = 0.0004
golden_turn = 2.399963229728653
highest = lax.Precision.HIGHEST


def sphere(point_count):
    middle = jnp.arange(point_count).astype(jnp.float32) + 0.5
    height = 1.0 - 2.0 * middle / point_count
    radial = jnp.sqrt(jnp.maximum(1.0 - height * height, 0.0))
    angle_turn = middle * golden_turn
    return jnp.stack([radial * jnp.cos(angle_turn), radial * jnp.sin(angle_turn), height])


def point_sum(targets, sources, weights):
    delta_x = targets[0][..., :, None] - sources[0][..., None, :]
    delta_y = targets[1][..., :, None] - sources[1][..., None, :]
    delta_z = targets[2][..., :, None] - sources[2][..., None, :]
    kernel = lax.rsqrt(delta_x * delta_x + delta_y * delta_y + delta_z * delta_z + softening_sq)
    return jnp.sum(kernel * weights[..., None, :], axis=-1)


def translation(unit_sphere, shift_x, shift_y, shift_z, radius):
    delta_x = (
        radius * (unit_sphere[0][:, None] - unit_sphere[0][None, :]) - shift_x[..., None, None]
    )
    delta_y = (
        radius * (unit_sphere[1][:, None] - unit_sphere[1][None, :]) - shift_y[..., None, None]
    )
    delta_z = (
        radius * (unit_sphere[2][:, None] - unit_sphere[2][None, :]) - shift_z[..., None, None]
    )
    return lax.rsqrt(delta_x * delta_x + delta_y * delta_y + delta_z * delta_z + softening_sq)


def child_points(unit_sphere):
    centre = jnp.arange(2).astype(jnp.float32) + 0.5
    point_count = unit_sphere.shape[1]
    box_shape = (2, 2, 2, point_count)
    along_x = jnp.broadcast_to(centre[:, None, None, None] + 0.9 * unit_sphere[0], box_shape)
    along_y = jnp.broadcast_to(centre[None, :, None, None] + 0.9 * unit_sphere[1], box_shape)
    along_z = jnp.broadcast_to(centre[None, None, :, None] + 0.9 * unit_sphere[2], box_shape)
    return jnp.stack([along_x, along_y, along_z]).reshape(3, 8 * point_count)


def rel_gather(buf, axis, dim):
    count = lax.axis_size(axis)
    have = 1
    while have < count:
        step = min(have, count - have)
        part = lax.slice_in_dim(buf, 0, step, axis=dim)
        got = lax.ppermute(part, axis, [(j, (j - have) % count) for j in range(count)])
        buf = jnp.concatenate([buf, got], axis=dim)
        have += step
    return buf


def exchange(items, axis):
    count = lax.axis_size(axis)
    heads, tails = [], []
    for cells, dim, width in items:
        heads.append(lax.slice_in_dim(cells, 0, width, axis=dim))
        tails.append(lax.slice_in_dim(cells, cells.shape[dim] - width, cells.shape[dim], axis=dim))
    sent_tail = jnp.concatenate([t.reshape(-1) for t in tails])
    sent_head = jnp.concatenate([h.reshape(-1) for h in heads])
    from_left = lax.ppermute(sent_tail, axis, [(i, (i + 1) % count) for i in range(count)])
    from_right = lax.ppermute(sent_head, axis, [((i + 1) % count, i) for i in range(count)])
    out, start = [], 0
    for (cells, dim, width), head, tail in zip(items, heads, tails):
        size = head.size
        before = from_left[start : start + size].reshape(tail.shape)
        after = from_right[start : start + size].reshape(head.shape)
        out.append(jnp.concatenate([before, cells, after], axis=dim))
        start += size
    return out


def split_top(values):
    scaled = values * 65537.0
    return scaled - (scaled - values)


def m2l_kernel(shift_count, rows, table_ref, base_ref, sources_ref, out_ref):
    out_ref[...] = jnp.zeros_like(out_ref)
    vectors = out_ref.shape[0]

    def split_dot(left, matrix_high, matrix_low, dims):
        both = lax.dot_general(left, matrix_high, dims, preferred_element_type=jnp.float32)
        cross = lax.dot_general(
            left[:vectors], matrix_low, dims, preferred_element_type=jnp.float32
        )
        return both[:vectors] + both[vectors:] + cross

    def body(index, carry):
        shift_x = table_ref[3 * index]
        shift_y = table_ref[3 * index + 1]
        shift_z = table_ref[3 * index + 2]
        fwd = sources_ref[0, index]
        back = sources_ref[1, index]
        for row in range(0, base_ref.shape[1], rows):
            delta_x = base_ref[0, row : row + rows, :] - shift_x
            delta_y = base_ref[1, row : row + rows, :] - shift_y
            delta_z = base_ref[2, row : row + rows, :] - shift_z
            matrix = lax.rsqrt(
                delta_x * delta_x + delta_y * delta_y + delta_z * delta_z + softening_sq
            )
            matrix_top = split_top(matrix)
            matrix_high = matrix_top.astype(jnp.bfloat16)
            matrix_low = (matrix - matrix_top).astype(jnp.bfloat16)
            out_ref[:, row : row + rows] += split_dot(
                fwd, matrix_high, matrix_low, (((1,), (1,)), ((), ()))
            )
            out_ref[...] += split_dot(
                back[:, row : row + rows], matrix_high, matrix_low, (((1,), (0,)), ((), ()))
            )
        return carry

    lax.fori_loop(0, shift_count, body, 0)


def m2l(table, base, sources):
    top = split_top(sources)
    split = jnp.concatenate([top, sources - top], axis=2).astype(jnp.bfloat16)
    shift_count, vectors, points = sources.shape[1:]
    return pl.pallas_call(
        functools.partial(m2l_kernel, shift_count, 128),
        out_shape=jax.ShapeDtypeStruct((vectors, points), jnp.float32),
        in_specs=[
            pl.BlockSpec(memory_space=pltpu.SMEM),
            pl.BlockSpec(memory_space=pltpu.VMEM),
            pl.BlockSpec(memory_space=pltpu.VMEM),
        ],
        out_specs=pl.BlockSpec(memory_space=pltpu.VMEM),
        compiler_params=pltpu.CompilerParams(vmem_limit_bytes=48 * 1024 * 1024),
        cost_estimate=pl.CostEstimate(
            flops=12 * shift_count * vectors * points * points + 14 * shift_count * points * points,
            transcendentals=shift_count * points * points,
            bytes_accessed=4 * (sources.size + base.size + vectors * points),
        ),
    )(table, base, split)


def far_shifts(span):
    shifts = []
    for dx in range(-span, span + 1):
        for dy in range(-span, span + 1):
            for dz in range(-span, span + 1):
                if max(abs(dx), abs(dy), abs(dz)) >= 2 and (dx, dy, dz) > (0, 0, 0):
                    shifts.append((dx, dy, dz))
    return shifts


def shards(offsets, charges, counts, c2e_leaf_up, c2e_leaf_down, c2e_top_up, c2e_top_down):
    slot_count = offsets.shape[-1]
    layers = offsets.shape[3]
    parent_layers = layers // 2
    points = c2e_leaf_up.shape[0]
    unit_sphere = sphere(points)
    slot_index = jnp.arange(slot_count)
    weights = jnp.where(slot_index < counts[..., None], charges, 0.0)
    packed = jnp.concatenate([offsets, weights[None]], axis=0)
    leaf_check_pts = 0.5 + 1.8 * unit_sphere
    leaf_check = point_sum(leaf_check_pts[:, None, None, None, :], offsets, weights)
    leaf_eq = jnp.einsum("ec,xyzc->xyze", c2e_leaf_up, leaf_check, precision=highest)
    packed_x, eq_x = exchange([(packed, 1, 1), (leaf_eq, 0, 2)], "gx")
    beside_all, cycle = exchange([(packed_x, 2, 1), (eq_x, 1, 2)], "gy")
    children = child_points(unit_sphere)
    parent_weights = (
        leaf_eq.reshape(2, 2, parent_layers, 2, points)
        .transpose(2, 0, 1, 3, 4)
        .reshape(parent_layers, 8 * points)
    )
    parent_check_pts = 1.0 + 3.6 * unit_sphere
    parent_check = point_sum(parent_check_pts[:, None, :], children[:, None, :], parent_weights)
    parent_eq = jnp.einsum("ec,mc->me", c2e_top_up, parent_check, precision=highest)
    count_x = lax.axis_size("gx")
    count_y = lax.axis_size("gy")

    gathered = rel_gather(rel_gather(parent_eq[None, None], "gy", 1), "gx", 0)
    kept = []
    for rel_x in range(count_x):
        for rel_y in range(count_y):
            off_x = (rel_x + count_x // 2) % count_x - count_x // 2
            off_y = (rel_y + count_y // 2) % count_y - count_y // 2
            if abs(off_x) > 1 or abs(off_y) > 1:
                kept.append((rel_x * count_y + rel_y, off_x, off_y))
    kept_index = np.array([k[0] for k in kept], np.int32)
    kept_x = np.array([2.0 * k[1] for k in kept], np.float32)
    kept_y = np.array([2.0 * k[2] for k in kept], np.float32)
    far_sources = jnp.take(gathered.reshape(count_x * count_y, parent_layers, points), kept_index, axis=0)
    layer_float = jnp.arange(parent_layers).astype(jnp.float32)
    depth_pairs = 2.0 * (layer_float[None, :] - layer_float[:, None])
    far_shape = (parent_layers, len(kept), parent_layers, points)
    source_pts = jnp.stack(
        [
            jnp.broadcast_to(kept_x[None, :, None, None] + 1.8 * unit_sphere[0], far_shape),
            jnp.broadcast_to(kept_y[None, :, None, None] + 1.8 * unit_sphere[1], far_shape),
            jnp.broadcast_to(depth_pairs[:, None, :, None] + 1.8 * unit_sphere[2], far_shape),
        ]
    ).reshape(3, parent_layers, -1)
    far_check = point_sum(
        jnp.broadcast_to(1.8 * unit_sphere[:, None, :], (3, parent_layers, points)),
        source_pts,
        far_sources.reshape(-1),
    )

    framed = jnp.pad(cycle, ((1, 1), (1, 1), (3, 3), (0, 0)))
    shifts = far_shifts(3)
    depth_windows = jnp.stack(
        [framed[:, :, depth : depth + layers] for depth in range(7)], axis=2
    ).reshape(-1, layers * points)
    window_rows = np.array(
        [
            [
                [
                    np.ravel_multi_index(
                        (ix + sign * dx + 3, iy + sign * dy + 3, sign * dz + 3), framed.shape[:2] + (7,)
                    )
                    for ix in range(2)
                    for iy in range(2)
                ]
                for dx, dy, dz in shifts
            ]
            for sign in (1, -1)
        ],
        np.int32,
    )
    sources = jnp.take(depth_windows, window_rows, axis=0).reshape(2, len(shifts), 4 * layers, points)
    base = jnp.stack(
        [0.9 * (unit_sphere[i][:, None] - unit_sphere[i][None, :]) for i in range(3)]
    )
    table = jnp.asarray(np.array(shifts, np.float32).reshape(-1))
    leaf_down_check = m2l(table, base, sources).reshape(2, 2, layers, points)
    parent_local = jnp.einsum("ec,mc->me", c2e_top_down, far_check, precision=highest)
    leaf_local = jnp.einsum("ec,xyzc->xyze", c2e_leaf_down, leaf_down_check, precision=highest)

    padded_around = jnp.pad(beside_all, ((0, 0), (0, 0), (0, 0), (1, 1), (0, 0)))
    around_shape = padded_around.shape[1:4]
    moves = [(mx, my, mz) for mx in (-1, 0, 1) for my in (-1, 0, 1) for mz in (-1, 0, 1)]
    box_rows = np.array(
        [
            [
                np.ravel_multi_index((bx + 1 + mx, by + 1 + my, bz + 1 + mz), around_shape)
                for bx in range(2)
                for by in range(2)
                for bz in range(layers)
            ]
            for mx, my, mz in moves
        ],
        np.int32,
    )
    source = jnp.take(
        padded_around.reshape(4, -1, slot_count), box_rows, axis=1
    ).reshape(4, len(moves), 2, 2, layers, slot_count)
    move = jnp.array(moves, jnp.float32)
    shape6 = (len(moves), 1, 1, 1, 1, 1)
    delta_x = packed[0][None, ..., :, None] - source[0][..., None, :] - move[:, 0].reshape(shape6)
    delta_y = packed[1][None, ..., :, None] - source[1][..., None, :] - move[:, 1].reshape(shape6)
    delta_z = packed[2][None, ..., :, None] - source[2][..., None, :] - move[:, 2].reshape(shape6)
    kernel = lax.rsqrt(delta_x * delta_x + delta_y * delta_y + delta_z * delta_z + softening_sq)
    diagonal = jnp.arange(slot_count)[:, None] == jnp.arange(slot_count)[None, :]
    centre = (jnp.arange(len(moves)) == 13).reshape(shape6)
    kernel = jnp.where(centre & diagonal, 0.0, kernel)
    near = jnp.sum(jnp.sum(kernel * source[3][..., None, :], axis=-1), axis=0)

    leaf_down_pts = 0.5 + 1.8 * unit_sphere
    leaf_far = point_sum(offsets, leaf_down_pts[:, None, None, None, :], leaf_local)
    parent_down_pts = 1.0 + 3.6 * unit_sphere
    local_float = jnp.arange(2).astype(jnp.float32)
    layer_parity = (jnp.arange(layers) % 2).astype(jnp.float32)
    in_parent = jnp.stack(
        [
            local_float[:, None, None, None] + offsets[0],
            local_float[None, :, None, None] + offsets[1],
            layer_parity[None, None, :, None] + offsets[2],
        ]
    )
    spread_local = jnp.repeat(parent_local, 2, axis=0)[None, None]
    parent_far = point_sum(in_parent, parent_down_pts[:, None, None, None, :], spread_local)
    total = near + leaf_far + parent_far
    return jnp.where(slot_index < counts[..., None], total, 0.0)


def solution(mesh):
    return jax.shard_map(
        shards,
        mesh=mesh,
        in_specs=(
            P(None, "gx", "gy", None, None),
            P("gx", "gy", None, None),
            P("gx", "gy", None),
            P(),
            P(),
            P(),
            P(),
        ),
        out_specs=P("gx", "gy", None, None),
        check_vma=False,
    )
```

```python
import functools

import jax
import numpy as np
import jax.numpy as jnp
from jax import lax
from jax.experimental import pallas as pl
from jax.experimental.pallas import tpu as pltpu
from jax.sharding import PartitionSpec as P

softening_sq = 0.0004
golden_turn = 2.399963229728653
highest = lax.Precision.HIGHEST


def sphere(point_count):
    middle = jnp.arange(point_count).astype(jnp.float32) + 0.5
    height = 1.0 - 2.0 * middle / point_count
    radial = jnp.sqrt(jnp.maximum(1.0 - height * height, 0.0))
    angle_turn = middle * golden_turn
    return jnp.stack([radial * jnp.cos(angle_turn), radial * jnp.sin(angle_turn), height])


def point_sum(targets, sources, weights):
    delta_x = targets[0][..., :, None] - sources[0][..., None, :]
    delta_y = targets[1][..., :, None] - sources[1][..., None, :]
    delta_z = targets[2][..., :, None] - sources[2][..., None, :]
    kernel = lax.rsqrt(delta_x * delta_x + delta_y * delta_y + delta_z * delta_z + softening_sq)
    return jnp.sum(kernel * weights[..., None, :], axis=-1)


def translation(unit_sphere, shift_x, shift_y, shift_z, radius):
    delta_x = (
        radius * (unit_sphere[0][:, None] - unit_sphere[0][None, :]) - shift_x[..., None, None]
    )
    delta_y = (
        radius * (unit_sphere[1][:, None] - unit_sphere[1][None, :]) - shift_y[..., None, None]
    )
    delta_z = (
        radius * (unit_sphere[2][:, None] - unit_sphere[2][None, :]) - shift_z[..., None, None]
    )
    return lax.rsqrt(delta_x * delta_x + delta_y * delta_y + delta_z * delta_z + softening_sq)


def child_points(unit_sphere):
    centre = jnp.arange(2).astype(jnp.float32) + 0.5
    point_count = unit_sphere.shape[1]
    box_shape = (2, 2, 2, point_count)
    along_x = jnp.broadcast_to(centre[:, None, None, None] + 0.9 * unit_sphere[0], box_shape)
    along_y = jnp.broadcast_to(centre[None, :, None, None] + 0.9 * unit_sphere[1], box_shape)
    along_z = jnp.broadcast_to(centre[None, None, :, None] + 0.9 * unit_sphere[2], box_shape)
    return jnp.stack([along_x, along_y, along_z]).reshape(3, 8 * point_count)


def rel_gather(buf, axis, dim):
    count = lax.axis_size(axis)
    have = 1
    while have < count:
        step = min(have, count - have)
        part = lax.slice_in_dim(buf, 0, step, axis=dim)
        got = lax.ppermute(part, axis, [(j, (j - have) % count) for j in range(count)])
        buf = jnp.concatenate([buf, got], axis=dim)
        have += step
    return buf


def exchange(items, axis):
    count = lax.axis_size(axis)
    heads, tails = [], []
    for cells, dim, width in items:
        heads.append(lax.slice_in_dim(cells, 0, width, axis=dim))
        tails.append(lax.slice_in_dim(cells, cells.shape[dim] - width, cells.shape[dim], axis=dim))
    sent_tail = jnp.concatenate([t.reshape(-1) for t in tails])
    sent_head = jnp.concatenate([h.reshape(-1) for h in heads])
    from_left = lax.ppermute(sent_tail, axis, [(i, (i + 1) % count) for i in range(count)])
    from_right = lax.ppermute(sent_head, axis, [((i + 1) % count, i) for i in range(count)])
    out, start = [], 0
    for (cells, dim, width), head, tail in zip(items, heads, tails):
        size = head.size
        before = from_left[start : start + size].reshape(tail.shape)
        after = from_right[start : start + size].reshape(head.shape)
        out.append(jnp.concatenate([before, cells, after], axis=dim))
        start += size
    return out


def split_top(values):
    scaled = values * 65537.0
    return scaled - (scaled - values)


def m2l_kernel(shift_count, rows, table_ref, index_ref, base_ref, windows_ref, out_ref):
    out_ref[...] = jnp.zeros_like(out_ref)
    vectors = out_ref.shape[0]
    pieces = index_ref.shape[0] // (2 * shift_count)

    def split_dot(left, matrix_high, matrix_low, dims):
        both = lax.dot_general(left, matrix_high, dims, preferred_element_type=jnp.float32)
        cross = lax.dot_general(
            left[:vectors], matrix_low, dims, preferred_element_type=jnp.float32
        )
        return both[:vectors] + both[vectors:] + cross

    def gathered(sign, index):
        first = (sign * shift_count + index) * pieces
        block = jnp.concatenate(
            [windows_ref[index_ref[first + piece]] for piece in range(pieces)], axis=0
        )
        top = split_top(block)
        return jnp.concatenate([top, block - top], axis=0).astype(jnp.bfloat16)

    def body(index, carry):
        shift_x = table_ref[3 * index]
        shift_y = table_ref[3 * index + 1]
        shift_z = table_ref[3 * index + 2]
        fwd = gathered(0, index)
        back = gathered(1, index)
        for row in range(0, base_ref.shape[1], rows):
            delta_x = base_ref[0, row : row + rows, :] - shift_x
            delta_y = base_ref[1, row : row + rows, :] - shift_y
            delta_z = base_ref[2, row : row + rows, :] - shift_z
            matrix = lax.rsqrt(
                delta_x * delta_x + delta_y * delta_y + delta_z * delta_z + softening_sq
            )
            matrix_top = split_top(matrix)
            matrix_high = matrix_top.astype(jnp.bfloat16)
            matrix_low = (matrix - matrix_top).astype(jnp.bfloat16)
            out_ref[:, row : row + rows] += split_dot(
                fwd, matrix_high, matrix_low, (((1,), (1,)), ((), ()))
            )
            out_ref[...] += split_dot(
                back[:, row : row + rows], matrix_high, matrix_low, (((1,), (0,)), ((), ()))
            )
        return carry

    lax.fori_loop(0, shift_count, body, 0)


def m2l(table, window_index, base, windows, vectors):
    shift_count = table.shape[0] // 3
    points = windows.shape[-1]
    return pl.pallas_call(
        functools.partial(m2l_kernel, shift_count, 128),
        out_shape=jax.ShapeDtypeStruct((vectors, points), jnp.float32),
        in_specs=[
            pl.BlockSpec(memory_space=pltpu.SMEM),
            pl.BlockSpec(memory_space=pltpu.SMEM),
            pl.BlockSpec(memory_space=pltpu.VMEM),
            pl.BlockSpec(memory_space=pltpu.VMEM),
        ],
        out_specs=pl.BlockSpec(memory_space=pltpu.VMEM),
        compiler_params=pltpu.CompilerParams(vmem_limit_bytes=48 * 1024 * 1024),
        cost_estimate=pl.CostEstimate(
            flops=12 * shift_count * vectors * points * points + 14 * shift_count * points * points,
            transcendentals=shift_count * points * points,
            bytes_accessed=4 * (windows.size + base.size + vectors * points),
        ),
    )(table, window_index, base, windows)


def far_shifts(span):
    shifts = []
    for dx in range(-span, span + 1):
        for dy in range(-span, span + 1):
            for dz in range(-span, span + 1):
                if max(abs(dx), abs(dy), abs(dz)) >= 2 and (dx, dy, dz) > (0, 0, 0):
                    shifts.append((dx, dy, dz))
    return shifts


def shards(offsets, charges, counts, c2e_leaf_up, c2e_leaf_down, c2e_top_up, c2e_top_down):
    slot_count = offsets.shape[-1]
    layers = offsets.shape[3]
    parent_layers = layers // 2
    points = c2e_leaf_up.shape[0]
    unit_sphere = sphere(points)
    slot_index = jnp.arange(slot_count)
    weights = jnp.where(slot_index < counts[..., None], charges, 0.0)
    packed = jnp.concatenate([offsets, weights[None]], axis=0)
    leaf_check_pts = 0.5 + 1.8 * unit_sphere
    leaf_check = point_sum(leaf_check_pts[:, None, None, None, :], offsets, weights)
    leaf_eq = jnp.einsum("ec,xyzc->xyze", c2e_leaf_up, leaf_check, precision=highest)
    packed_x, eq_x = exchange([(packed, 1, 1), (leaf_eq, 0, 2)], "gx")
    beside_all, cycle = exchange([(packed_x, 2, 1), (eq_x, 1, 2)], "gy")
    children = child_points(unit_sphere)
    parent_weights = (
        leaf_eq.reshape(2, 2, parent_layers, 2, points)
        .transpose(2, 0, 1, 3, 4)
        .reshape(parent_layers, 8 * points)
    )
    parent_check_pts = 1.0 + 3.6 * unit_sphere
    parent_check = point_sum(parent_check_pts[:, None, :], children[:, None, :], parent_weights)
    parent_eq = jnp.einsum("ec,mc->me", c2e_top_up, parent_check, precision=highest)
    count_x = lax.axis_size("gx")
    count_y = lax.axis_size("gy")

    gathered = rel_gather(rel_gather(parent_eq[None, None], "gy", 1), "gx", 0)
    kept = []
    for rel_x in range(count_x):
        for rel_y in range(count_y):
            off_x = (rel_x + count_x // 2) % count_x - count_x // 2
            off_y = (rel_y + count_y // 2) % count_y - count_y // 2
            if abs(off_x) > 1 or abs(off_y) > 1:
                kept.append((rel_x * count_y + rel_y, off_x, off_y))
    kept_index = np.array([k[0] for k in kept], np.int32)
    kept_x = np.array([2.0 * k[1] for k in kept], np.float32)
    kept_y = np.array([2.0 * k[2] for k in kept], np.float32)
    far_sources = jnp.take(gathered.reshape(count_x * count_y, parent_layers, points), kept_index, axis=0)
    layer_float = jnp.arange(parent_layers).astype(jnp.float32)
    depth_pairs = 2.0 * (layer_float[None, :] - layer_float[:, None])
    far_shape = (parent_layers, len(kept), parent_layers, points)
    source_pts = jnp.stack(
        [
            jnp.broadcast_to(kept_x[None, :, None, None] + 1.8 * unit_sphere[0], far_shape),
            jnp.broadcast_to(kept_y[None, :, None, None] + 1.8 * unit_sphere[1], far_shape),
            jnp.broadcast_to(depth_pairs[:, None, :, None] + 1.8 * unit_sphere[2], far_shape),
        ]
    ).reshape(3, parent_layers, -1)
    far_check = point_sum(
        jnp.broadcast_to(1.8 * unit_sphere[:, None, :], (3, parent_layers, points)),
        source_pts,
        far_sources.reshape(-1),
    )

    framed = jnp.pad(cycle, ((1, 1), (1, 1), (3, 3), (0, 0)))
    shifts = far_shifts(3)
    depth_windows = jnp.stack(
        [framed[:, :, depth : depth + layers] for depth in range(7)], axis=2
    ).reshape(-1, layers, points)
    window_index = np.array(
        [
            np.ravel_multi_index(
                (ix + sign * dx + 3, iy + sign * dy + 3, sign * dz + 3), framed.shape[:2] + (7,)
            )
            for sign in (1, -1)
            for dx, dy, dz in shifts
            for ix in range(2)
            for iy in range(2)
        ],
        np.int32,
    )
    base = jnp.stack(
        [0.9 * (unit_sphere[i][:, None] - unit_sphere[i][None, :]) for i in range(3)]
    )
    table = jnp.asarray(np.array(shifts, np.float32).reshape(-1))
    leaf_down_check = m2l(table, jnp.asarray(window_index), base, depth_windows, 4 * layers).reshape(
        2, 2, layers, points
    )
    parent_local = jnp.einsum("ec,mc->me", c2e_top_down, far_check, precision=highest)
    leaf_local = jnp.einsum("ec,xyzc->xyze", c2e_leaf_down, leaf_down_check, precision=highest)

    padded_around = jnp.pad(beside_all, ((0, 0), (0, 0), (0, 0), (1, 1), (0, 0)))
    around_shape = padded_around.shape[1:4]
    moves = [(mx, my, mz) for mx in (-1, 0, 1) for my in (-1, 0, 1) for mz in (-1, 0, 1)]
    box_rows = np.array(
        [
            [
                np.ravel_multi_index((bx + 1 + mx, by + 1 + my, bz + 1 + mz), around_shape)
                for bx in range(2)
                for by in range(2)
                for bz in range(layers)
            ]
            for mx, my, mz in moves
        ],
        np.int32,
    )
    source = jnp.take(
        padded_around.reshape(4, -1, slot_count), box_rows, axis=1
    ).reshape(4, len(moves), 2, 2, layers, slot_count)
    move = jnp.array(moves, jnp.float32)
    shape6 = (len(moves), 1, 1, 1, 1, 1)
    delta_x = packed[0][None, ..., :, None] - source[0][..., None, :] - move[:, 0].reshape(shape6)
    delta_y = packed[1][None, ..., :, None] - source[1][..., None, :] - move[:, 1].reshape(shape6)
    delta_z = packed[2][None, ..., :, None] - source[2][..., None, :] - move[:, 2].reshape(shape6)
    kernel = lax.rsqrt(delta_x * delta_x + delta_y * delta_y + delta_z * delta_z + softening_sq)
    diagonal = jnp.arange(slot_count)[:, None] == jnp.arange(slot_count)[None, :]
    centre = (jnp.arange(len(moves)) == 13).reshape(shape6)
    kernel = jnp.where(centre & diagonal, 0.0, kernel)
    near = jnp.sum(jnp.sum(kernel * source[3][..., None, :], axis=-1), axis=0)

    leaf_down_pts = 0.5 + 1.8 * unit_sphere
    leaf_far = point_sum(offsets, leaf_down_pts[:, None, None, None, :], leaf_local)
    parent_down_pts = 1.0 + 3.6 * unit_sphere
    local_float = jnp.arange(2).astype(jnp.float32)
    layer_parity = (jnp.arange(layers) % 2).astype(jnp.float32)
    in_parent = jnp.stack(
        [
            local_float[:, None, None, None] + offsets[0],
            local_float[None, :, None, None] + offsets[1],
            layer_parity[None, None, :, None] + offsets[2],
        ]
    )
    spread_local = jnp.repeat(parent_local, 2, axis=0)[None, None]
    parent_far = point_sum(in_parent, parent_down_pts[:, None, None, None, :], spread_local)
    total = near + leaf_far + parent_far
    return jnp.where(slot_index < counts[..., None], total, 0.0)


def solution(mesh):
    return jax.shard_map(
        shards,
        mesh=mesh,
        in_specs=(
            P(None, "gx", "gy", None, None),
            P("gx", "gy", None, None),
            P("gx", "gy", None),
            P(),
            P(),
            P(),
            P(),
        ),
        out_specs=P("gx", "gy", None, None),
        check_vma=False,
    )
```

```python
import functools

import jax
import numpy as np
import jax.numpy as jnp
from jax import lax
from jax.experimental import pallas as pl
from jax.experimental.pallas import tpu as pltpu
from jax.sharding import PartitionSpec as P

softening_sq = 0.0004
golden_turn = 2.399963229728653
highest = lax.Precision.HIGHEST


def sphere(point_count):
    middle = jnp.arange(point_count).astype(jnp.float32) + 0.5
    height = 1.0 - 2.0 * middle / point_count
    radial = jnp.sqrt(jnp.maximum(1.0 - height * height, 0.0))
    angle_turn = middle * golden_turn
    return jnp.stack([radial * jnp.cos(angle_turn), radial * jnp.sin(angle_turn), height])


def point_sum(targets, sources, weights):
    delta_x = targets[0][..., :, None] - sources[0][..., None, :]
    delta_y = targets[1][..., :, None] - sources[1][..., None, :]
    delta_z = targets[2][..., :, None] - sources[2][..., None, :]
    kernel = lax.rsqrt(delta_x * delta_x + delta_y * delta_y + delta_z * delta_z + softening_sq)
    return jnp.sum(kernel * weights[..., None, :], axis=-1)


def translation(unit_sphere, shift_x, shift_y, shift_z, radius):
    delta_x = (
        radius * (unit_sphere[0][:, None] - unit_sphere[0][None, :]) - shift_x[..., None, None]
    )
    delta_y = (
        radius * (unit_sphere[1][:, None] - unit_sphere[1][None, :]) - shift_y[..., None, None]
    )
    delta_z = (
        radius * (unit_sphere[2][:, None] - unit_sphere[2][None, :]) - shift_z[..., None, None]
    )
    return lax.rsqrt(delta_x * delta_x + delta_y * delta_y + delta_z * delta_z + softening_sq)


def child_points(unit_sphere):
    centre = jnp.arange(2).astype(jnp.float32) + 0.5
    point_count = unit_sphere.shape[1]
    box_shape = (2, 2, 2, point_count)
    along_x = jnp.broadcast_to(centre[:, None, None, None] + 0.9 * unit_sphere[0], box_shape)
    along_y = jnp.broadcast_to(centre[None, :, None, None] + 0.9 * unit_sphere[1], box_shape)
    along_z = jnp.broadcast_to(centre[None, None, :, None] + 0.9 * unit_sphere[2], box_shape)
    return jnp.stack([along_x, along_y, along_z]).reshape(3, 8 * point_count)


def rel_gather(buf, axis, dim):
    count = lax.axis_size(axis)
    have = 1
    while have < count:
        step = min(have, count - have)
        part = lax.slice_in_dim(buf, 0, step, axis=dim)
        got = lax.ppermute(part, axis, [(j, (j - have) % count) for j in range(count)])
        buf = jnp.concatenate([buf, got], axis=dim)
        have += step
    return buf


def exchange(items, axis):
    count = lax.axis_size(axis)
    heads, tails = [], []
    for cells, dim, width in items:
        heads.append(lax.slice_in_dim(cells, 0, width, axis=dim))
        tails.append(lax.slice_in_dim(cells, cells.shape[dim] - width, cells.shape[dim], axis=dim))
    sent_tail = jnp.concatenate([t.reshape(-1) for t in tails])
    sent_head = jnp.concatenate([h.reshape(-1) for h in heads])
    from_left = lax.ppermute(sent_tail, axis, [(i, (i + 1) % count) for i in range(count)])
    from_right = lax.ppermute(sent_head, axis, [((i + 1) % count, i) for i in range(count)])
    out, start = [], 0
    for (cells, dim, width), head, tail in zip(items, heads, tails):
        size = head.size
        before = from_left[start : start + size].reshape(tail.shape)
        after = from_right[start : start + size].reshape(head.shape)
        out.append(jnp.concatenate([before, cells, after], axis=dim))
        start += size
    return out


def split_top(values):
    scaled = values * 65537.0
    return scaled - (scaled - values)


def m2l_kernel(shift_count, rows, table_ref, index_ref, base_ref, windows_ref, out_ref):
    out_ref[...] = jnp.zeros_like(out_ref)
    vectors = out_ref.shape[0]
    pieces = index_ref.shape[0] // (2 * shift_count)

    def split_dot(left, matrix_high, matrix_low, dims):
        both = lax.dot_general(left, matrix_high, dims, preferred_element_type=jnp.float32)
        cross = lax.dot_general(
            left[:vectors], matrix_low, dims, preferred_element_type=jnp.float32
        )
        return both[:vectors] + both[vectors:] + cross

    def gathered(sign, index):
        first = (sign * shift_count + index) * pieces
        block = jnp.concatenate(
            [windows_ref[index_ref[first + piece]] for piece in range(pieces)], axis=0
        )
        top = split_top(block)
        return jnp.concatenate([top, block - top], axis=0).astype(jnp.bfloat16)

    def body(index, carry):
        shift_x = table_ref[3 * index]
        shift_y = table_ref[3 * index + 1]
        shift_z = table_ref[3 * index + 2]
        fwd = gathered(0, index)
        back = gathered(1, index)
        for row in range(0, base_ref.shape[1], rows):
            delta_x = base_ref[0, row : row + rows, :] - shift_x
            delta_y = base_ref[1, row : row + rows, :] - shift_y
            delta_z = base_ref[2, row : row + rows, :] - shift_z
            matrix = lax.rsqrt(
                delta_x * delta_x + delta_y * delta_y + delta_z * delta_z + softening_sq
            )
            matrix_top = split_top(matrix)
            matrix_high = matrix_top.astype(jnp.bfloat16)
            matrix_low = (matrix - matrix_top).astype(jnp.bfloat16)
            out_ref[:, row : row + rows] += split_dot(
                fwd, matrix_high, matrix_low, (((1,), (1,)), ((), ()))
            )
            out_ref[...] += split_dot(
                back[:, row : row + rows], matrix_high, matrix_low, (((1,), (0,)), ((), ()))
            )
        return carry

    lax.fori_loop(0, shift_count, body, 0)


def m2l(table, window_index, base, windows, vectors):
    shift_count = table.shape[0] // 3
    points = windows.shape[-1]
    return pl.pallas_call(
        functools.partial(m2l_kernel, shift_count, 128),
        out_shape=jax.ShapeDtypeStruct((vectors, points), jnp.float32),
        in_specs=[
            pl.BlockSpec(memory_space=pltpu.SMEM),
            pl.BlockSpec(memory_space=pltpu.SMEM),
            pl.BlockSpec(memory_space=pltpu.VMEM),
            pl.BlockSpec(memory_space=pltpu.VMEM),
        ],
        out_specs=pl.BlockSpec(memory_space=pltpu.VMEM),
        compiler_params=pltpu.CompilerParams(vmem_limit_bytes=48 * 1024 * 1024),
        cost_estimate=pl.CostEstimate(
            flops=12 * shift_count * vectors * points * points + 14 * shift_count * points * points,
            transcendentals=shift_count * points * points,
            bytes_accessed=4 * (windows.size + base.size + vectors * points),
        ),
    )(table, window_index, base, windows)


def far_shifts(span):
    shifts = []
    for dx in range(-span, span + 1):
        for dy in range(-span, span + 1):
            for dz in range(-span, span + 1):
                if max(abs(dx), abs(dy), abs(dz)) >= 2 and (dx, dy, dz) > (0, 0, 0):
                    shifts.append((dx, dy, dz))
    return shifts


def shards(offsets, charges, counts, c2e_leaf_up, c2e_leaf_down, c2e_top_up, c2e_top_down):
    slot_count = offsets.shape[-1]
    layers = offsets.shape[3]
    parent_layers = layers // 2
    points = c2e_leaf_up.shape[0]
    unit_sphere = sphere(points)
    slot_index = jnp.arange(slot_count)
    weights = jnp.where(slot_index < counts[..., None], charges, 0.0)
    packed = jnp.concatenate([offsets, weights[None]], axis=0)
    leaf_check_pts = 0.5 + 1.8 * unit_sphere
    leaf_check = point_sum(leaf_check_pts[:, None, None, None, :], offsets, weights)
    leaf_eq = jnp.einsum("ec,xyzc->xyze", c2e_leaf_up, leaf_check, precision=highest)
    packed_x, eq_x = exchange([(packed, 1, 1), (leaf_eq, 0, 2)], "gx")
    beside_all, cycle = exchange([(packed_x, 2, 1), (eq_x, 1, 2)], "gy")
    children = child_points(unit_sphere)
    parent_weights = (
        leaf_eq.reshape(2, 2, parent_layers, 2, points)
        .transpose(2, 0, 1, 3, 4)
        .reshape(parent_layers, 8 * points)
    )
    parent_check_pts = 1.0 + 3.6 * unit_sphere
    parent_check = point_sum(parent_check_pts[:, None, :], children[:, None, :], parent_weights)
    parent_eq = jnp.einsum("ec,mc->me", c2e_top_up, parent_check, precision=highest)
    count_x = lax.axis_size("gx")
    count_y = lax.axis_size("gy")

    gathered = rel_gather(rel_gather(parent_eq[None, None], "gy", 1), "gx", 0)
    kept = []
    for rel_x in range(count_x):
        for rel_y in range(count_y):
            off_x = (rel_x + count_x // 2) % count_x - count_x // 2
            off_y = (rel_y + count_y // 2) % count_y - count_y // 2
            if abs(off_x) > 1 or abs(off_y) > 1:
                kept.append((rel_x * count_y + rel_y, off_x, off_y))
    kept_index = np.array([k[0] for k in kept], np.int32)
    kept_x = np.array([2.0 * k[1] for k in kept], np.float32)
    kept_y = np.array([2.0 * k[2] for k in kept], np.float32)
    far_sources = jnp.take(gathered.reshape(count_x * count_y, parent_layers, points), kept_index, axis=0)
    layer_float = jnp.arange(parent_layers).astype(jnp.float32)
    depth_pairs = 2.0 * (layer_float[None, :] - layer_float[:, None])
    far_shape = (parent_layers, len(kept), parent_layers, points)
    source_pts = jnp.stack(
        [
            jnp.broadcast_to(kept_x[None, :, None, None] + 1.8 * unit_sphere[0], far_shape),
            jnp.broadcast_to(kept_y[None, :, None, None] + 1.8 * unit_sphere[1], far_shape),
            jnp.broadcast_to(depth_pairs[:, None, :, None] + 1.8 * unit_sphere[2], far_shape),
        ]
    ).reshape(3, parent_layers, -1)
    far_check = point_sum(
        jnp.broadcast_to(1.8 * unit_sphere[:, None, :], (3, parent_layers, points)),
        source_pts,
        far_sources.reshape(-1),
    )

    framed = jnp.pad(cycle, ((1, 1), (1, 1), (3, 3), (0, 0)))
    shifts = far_shifts(3)
    depth_windows = jnp.stack(
        [framed[:, :, depth : depth + layers] for depth in range(7)], axis=2
    ).reshape(-1, layers, points)
    window_index = np.array(
        [
            np.ravel_multi_index(
                (ix + sign * dx + 3, iy + sign * dy + 3, sign * dz + 3), framed.shape[:2] + (7,)
            )
            for sign in (1, -1)
            for dx, dy, dz in shifts
            for ix in range(2)
            for iy in range(2)
        ],
        np.int32,
    )
    base = jnp.stack(
        [0.9 * (unit_sphere[i][:, None] - unit_sphere[i][None, :]) for i in range(3)]
    )
    table = jnp.asarray(np.array(shifts, np.float32).reshape(-1))
    leaf_down_check = m2l(table, jnp.asarray(window_index), base, depth_windows, 4 * layers).reshape(
        2, 2, layers, points
    )
    parent_local = jnp.einsum("ec,mc->me", c2e_top_down, far_check, precision=highest)
    leaf_local = jnp.einsum("ec,xyzc->xyze", c2e_leaf_down, leaf_down_check, precision=highest)

    padded_around = jnp.pad(beside_all, ((0, 0), (0, 0), (0, 0), (1, 1), (0, 0)))
    around_shape = padded_around.shape[1:4]
    moves = [(mx, my, mz) for mx in (-1, 0, 1) for my in (-1, 0, 1) for mz in (-1, 0, 1)]
    box_rows = np.array(
        [
            [
                np.ravel_multi_index((bx + 1 + mx, by + 1 + my, bz + 1 + mz), around_shape)
                for bx in range(2)
                for by in range(2)
                for bz in range(layers)
            ]
            for mx, my, mz in moves
        ],
        np.int32,
    )
    source = jnp.take(
        padded_around.reshape(4, -1, slot_count), box_rows, axis=1
    ).reshape(4, len(moves), 2, 2, layers, slot_count)
    source = source.reshape(4, len(moves), 4 * layers, slot_count).transpose(0, 2, 1, 3)
    source = source.reshape(4, 4 * layers, len(moves) * slot_count)
    move = np.repeat(np.array(moves, np.float32), slot_count, axis=0)
    own = packed.reshape(4, 4 * layers, slot_count)
    delta_x = own[0][..., :, None] - source[0][..., None, :] - move[:, 0]
    delta_y = own[1][..., :, None] - source[1][..., None, :] - move[:, 1]
    delta_z = own[2][..., :, None] - source[2][..., None, :] - move[:, 2]
    kernel = lax.rsqrt(delta_x * delta_x + delta_y * delta_y + delta_z * delta_z + softening_sq)
    centre = moves.index((0, 0, 0))
    column = jnp.arange(len(moves) * slot_count)[None, :]
    itself = column == jnp.arange(slot_count)[:, None] + centre * slot_count
    kernel = jnp.where(itself, 0.0, kernel)
    near = jnp.sum(kernel * source[3][..., None, :], axis=-1).reshape(2, 2, layers, slot_count)

    leaf_down_pts = 0.5 + 1.8 * unit_sphere
    leaf_far = point_sum(offsets, leaf_down_pts[:, None, None, None, :], leaf_local)
    parent_down_pts = 1.0 + 3.6 * unit_sphere
    local_float = jnp.arange(2).astype(jnp.float32)
    layer_parity = (jnp.arange(layers) % 2).astype(jnp.float32)
    in_parent = jnp.stack(
        [
            local_float[:, None, None, None] + offsets[0],
            local_float[None, :, None, None] + offsets[1],
            layer_parity[None, None, :, None] + offsets[2],
        ]
    )
    spread_local = jnp.repeat(parent_local, 2, axis=0)[None, None]
    parent_far = point_sum(in_parent, parent_down_pts[:, None, None, None, :], spread_local)
    total = near + leaf_far + parent_far
    return jnp.where(slot_index < counts[..., None], total, 0.0)


def solution(mesh):
    return jax.shard_map(
        shards,
        mesh=mesh,
        in_specs=(
            P(None, "gx", "gy", None, None),
            P("gx", "gy", None, None),
            P("gx", "gy", None),
            P(),
            P(),
            P(),
            P(),
        ),
        out_specs=P("gx", "gy", None, None),
        check_vma=False,
    )
```

```python
import functools

import jax
import numpy as np
import jax.numpy as jnp
from jax import lax
from jax.experimental import pallas as pl
from jax.experimental.pallas import tpu as pltpu
from jax.sharding import PartitionSpec as P

softening_sq = 0.0004
golden_turn = 2.399963229728653
highest = lax.Precision.HIGHEST


def sphere(point_count):
    middle = jnp.arange(point_count).astype(jnp.float32) + 0.5
    height = 1.0 - 2.0 * middle / point_count
    radial = jnp.sqrt(jnp.maximum(1.0 - height * height, 0.0))
    angle_turn = middle * golden_turn
    return jnp.stack([radial * jnp.cos(angle_turn), radial * jnp.sin(angle_turn), height])


def point_sum(targets, sources, weights):
    delta_x = targets[0][..., :, None] - sources[0][..., None, :]
    delta_y = targets[1][..., :, None] - sources[1][..., None, :]
    delta_z = targets[2][..., :, None] - sources[2][..., None, :]
    kernel = lax.rsqrt(delta_x * delta_x + delta_y * delta_y + delta_z * delta_z + softening_sq)
    return jnp.sum(kernel * weights[..., None, :], axis=-1)


def translation(unit_sphere, shift_x, shift_y, shift_z, radius):
    delta_x = (
        radius * (unit_sphere[0][:, None] - unit_sphere[0][None, :]) - shift_x[..., None, None]
    )
    delta_y = (
        radius * (unit_sphere[1][:, None] - unit_sphere[1][None, :]) - shift_y[..., None, None]
    )
    delta_z = (
        radius * (unit_sphere[2][:, None] - unit_sphere[2][None, :]) - shift_z[..., None, None]
    )
    return lax.rsqrt(delta_x * delta_x + delta_y * delta_y + delta_z * delta_z + softening_sq)


def child_points(unit_sphere):
    centre = jnp.arange(2).astype(jnp.float32) + 0.5
    point_count = unit_sphere.shape[1]
    box_shape = (2, 2, 2, point_count)
    along_x = jnp.broadcast_to(centre[:, None, None, None] + 0.9 * unit_sphere[0], box_shape)
    along_y = jnp.broadcast_to(centre[None, :, None, None] + 0.9 * unit_sphere[1], box_shape)
    along_z = jnp.broadcast_to(centre[None, None, :, None] + 0.9 * unit_sphere[2], box_shape)
    return jnp.stack([along_x, along_y, along_z]).reshape(3, 8 * point_count)


def rel_gather(buf, axis, dim):
    count = lax.axis_size(axis)
    have = 1
    while have < count:
        step = min(have, count - have)
        part = lax.slice_in_dim(buf, 0, step, axis=dim)
        got = lax.ppermute(part, axis, [(j, (j - have) % count) for j in range(count)])
        buf = jnp.concatenate([buf, got], axis=dim)
        have += step
    return buf


def exchange(items, axis):
    count = lax.axis_size(axis)
    heads, tails = [], []
    for cells, dim, width in items:
        heads.append(lax.slice_in_dim(cells, 0, width, axis=dim))
        tails.append(lax.slice_in_dim(cells, cells.shape[dim] - width, cells.shape[dim], axis=dim))
    sent_tail = jnp.concatenate([t.reshape(-1) for t in tails])
    sent_head = jnp.concatenate([h.reshape(-1) for h in heads])
    from_left = lax.ppermute(sent_tail, axis, [(i, (i + 1) % count) for i in range(count)])
    from_right = lax.ppermute(sent_head, axis, [((i + 1) % count, i) for i in range(count)])
    out, start = [], 0
    for (cells, dim, width), head, tail in zip(items, heads, tails):
        size = head.size
        before = from_left[start : start + size].reshape(tail.shape)
        after = from_right[start : start + size].reshape(head.shape)
        out.append(jnp.concatenate([before, cells, after], axis=dim))
        start += size
    return out


def split_top(values):
    scaled = values * 65537.0
    return scaled - (scaled - values)


def m2l_kernel(shift_count, rows, table_ref, index_ref, base_ref, windows_ref, out_ref):
    out_ref[...] = jnp.zeros_like(out_ref)
    vectors = out_ref.shape[0]
    pieces = index_ref.shape[0] // (2 * shift_count)

    def split_dot(left, matrix_high, matrix_low, dims):
        both = lax.dot_general(left, matrix_high, dims, preferred_element_type=jnp.float32)
        cross = lax.dot_general(
            left[:vectors], matrix_low, dims, preferred_element_type=jnp.float32
        )
        return both[:vectors] + both[vectors:] + cross

    def gathered(sign, index):
        first = (sign * shift_count + index) * pieces
        block = jnp.concatenate(
            [windows_ref[index_ref[first + piece]] for piece in range(pieces)], axis=0
        )
        top = split_top(block)
        return jnp.concatenate([top, block - top], axis=0).astype(jnp.bfloat16)

    def body(index, carry):
        shift_x = table_ref[3 * index]
        shift_y = table_ref[3 * index + 1]
        shift_z = table_ref[3 * index + 2]
        fwd = gathered(0, index)
        back = gathered(1, index)
        for row in range(0, base_ref.shape[1], rows):
            delta_x = base_ref[0, row : row + rows, :] - shift_x
            delta_y = base_ref[1, row : row + rows, :] - shift_y
            delta_z = base_ref[2, row : row + rows, :] - shift_z
            matrix = lax.rsqrt(
                delta_x * delta_x + delta_y * delta_y + delta_z * delta_z + softening_sq
            )
            matrix_top = split_top(matrix)
            matrix_high = matrix_top.astype(jnp.bfloat16)
            matrix_low = (matrix - matrix_top).astype(jnp.bfloat16)
            out_ref[:, row : row + rows] += split_dot(
                fwd, matrix_high, matrix_low, (((1,), (1,)), ((), ()))
            )
            out_ref[...] += split_dot(
                back[:, row : row + rows], matrix_high, matrix_low, (((1,), (0,)), ((), ()))
            )
        return carry

    lax.fori_loop(0, shift_count, body, 0)


def m2l(table, window_index, base, windows, vectors):
    shift_count = table.shape[0] // 3
    points = windows.shape[-1]
    return pl.pallas_call(
        functools.partial(m2l_kernel, shift_count, 128),
        out_shape=jax.ShapeDtypeStruct((vectors, points), jnp.float32),
        in_specs=[
            pl.BlockSpec(memory_space=pltpu.SMEM),
            pl.BlockSpec(memory_space=pltpu.SMEM),
            pl.BlockSpec(memory_space=pltpu.VMEM),
            pl.BlockSpec(memory_space=pltpu.VMEM),
        ],
        out_specs=pl.BlockSpec(memory_space=pltpu.VMEM),
        compiler_params=pltpu.CompilerParams(vmem_limit_bytes=48 * 1024 * 1024),
        cost_estimate=pl.CostEstimate(
            flops=12 * shift_count * vectors * points * points + 14 * shift_count * points * points,
            transcendentals=shift_count * points * points,
            bytes_accessed=4 * (windows.size + base.size + vectors * points),
        ),
    )(table, window_index, base, windows)


def far_shifts(span):
    shifts = []
    for dx in range(-span, span + 1):
        for dy in range(-span, span + 1):
            for dz in range(-span, span + 1):
                if max(abs(dx), abs(dy), abs(dz)) >= 2 and (dx, dy, dz) > (0, 0, 0):
                    shifts.append((dx, dy, dz))
    return shifts


def shards(offsets, charges, counts, c2e_leaf_up, c2e_leaf_down, c2e_top_up, c2e_top_down):
    slot_count = offsets.shape[-1]
    layers = offsets.shape[3]
    parent_layers = layers // 2
    points = c2e_leaf_up.shape[0]
    unit_sphere = sphere(points)
    slot_index = jnp.arange(slot_count)
    weights = jnp.where(slot_index < counts[..., None], charges, 0.0)
    packed = jnp.concatenate([offsets, weights[None]], axis=0)
    leaf_check_pts = 0.5 + 1.8 * unit_sphere
    leaf_check = point_sum(leaf_check_pts[:, None, None, None, :], offsets, weights)
    leaf_eq = jnp.einsum("ec,xyzc->xyze", c2e_leaf_up, leaf_check, precision=highest)
    packed_x, eq_x = exchange([(packed, 1, 1), (leaf_eq, 0, 2)], "gx")
    beside_all, cycle = exchange([(packed_x, 2, 1), (eq_x, 1, 2)], "gy")
    children = child_points(unit_sphere)
    parent_weights = (
        leaf_eq.reshape(2, 2, parent_layers, 2, points)
        .transpose(2, 0, 1, 3, 4)
        .reshape(parent_layers, 8 * points)
    )
    parent_check_pts = 1.0 + 3.6 * unit_sphere
    parent_check = point_sum(parent_check_pts[:, None, :], children[:, None, :], parent_weights)
    parent_eq = jnp.einsum("ec,mc->me", c2e_top_up, parent_check, precision=highest)
    count_x = lax.axis_size("gx")
    count_y = lax.axis_size("gy")

    own_x = lax.axis_index("gx")
    own_y = lax.axis_index("gy")
    every = lax.all_gather(parent_eq, ("gx", "gy"), axis=0, tiled=False).reshape(
        count_x, count_y, parent_layers, points
    )
    twice = jnp.concatenate([every, every], axis=0)
    twice = jnp.concatenate([twice, twice], axis=1)
    gathered = lax.dynamic_slice(
        twice, (own_x, own_y, 0, 0), (count_x, count_y, parent_layers, points)
    )
    kept = []
    for rel_x in range(count_x):
        for rel_y in range(count_y):
            off_x = (rel_x + count_x // 2) % count_x - count_x // 2
            off_y = (rel_y + count_y // 2) % count_y - count_y // 2
            if abs(off_x) > 1 or abs(off_y) > 1:
                kept.append((rel_x * count_y + rel_y, off_x, off_y))
    kept_index = np.array([k[0] for k in kept], np.int32)
    kept_x = np.array([2.0 * k[1] for k in kept], np.float32)
    kept_y = np.array([2.0 * k[2] for k in kept], np.float32)
    far_sources = jnp.take(gathered.reshape(count_x * count_y, parent_layers, points), kept_index, axis=0)
    layer_float = jnp.arange(parent_layers).astype(jnp.float32)
    depth_pairs = 2.0 * (layer_float[None, :] - layer_float[:, None])
    far_shape = (parent_layers, len(kept), parent_layers, points)
    source_pts = jnp.stack(
        [
            jnp.broadcast_to(kept_x[None, :, None, None] + 1.8 * unit_sphere[0], far_shape),
            jnp.broadcast_to(kept_y[None, :, None, None] + 1.8 * unit_sphere[1], far_shape),
            jnp.broadcast_to(depth_pairs[:, None, :, None] + 1.8 * unit_sphere[2], far_shape),
        ]
    ).reshape(3, parent_layers, -1)
    far_check = point_sum(
        jnp.broadcast_to(1.8 * unit_sphere[:, None, :], (3, parent_layers, points)),
        source_pts,
        far_sources.reshape(-1),
    )

    framed = jnp.pad(cycle, ((1, 1), (1, 1), (3, 3), (0, 0)))
    shifts = far_shifts(3)
    depth_windows = jnp.stack(
        [framed[:, :, depth : depth + layers] for depth in range(7)], axis=2
    ).reshape(-1, layers, points)
    window_index = np.array(
        [
            np.ravel_multi_index(
                (ix + sign * dx + 3, iy + sign * dy + 3, sign * dz + 3), framed.shape[:2] + (7,)
            )
            for sign in (1, -1)
            for dx, dy, dz in shifts
            for ix in range(2)
            for iy in range(2)
        ],
        np.int32,
    )
    base = jnp.stack(
        [0.9 * (unit_sphere[i][:, None] - unit_sphere[i][None, :]) for i in range(3)]
    )
    table = jnp.asarray(np.array(shifts, np.float32).reshape(-1))
    leaf_down_check = m2l(table, jnp.asarray(window_index), base, depth_windows, 4 * layers).reshape(
        2, 2, layers, points
    )
    parent_local = jnp.einsum("ec,mc->me", c2e_top_down, far_check, precision=highest)
    leaf_local = jnp.einsum("ec,xyzc->xyze", c2e_leaf_down, leaf_down_check, precision=highest)

    padded_around = jnp.pad(beside_all, ((0, 0), (0, 0), (0, 0), (1, 1), (0, 0)))
    around_shape = padded_around.shape[1:4]
    moves = [(mx, my, mz) for mx in (-1, 0, 1) for my in (-1, 0, 1) for mz in (-1, 0, 1)]
    box_rows = np.array(
        [
            [
                np.ravel_multi_index((bx + 1 + mx, by + 1 + my, bz + 1 + mz), around_shape)
                for bx in range(2)
                for by in range(2)
                for bz in range(layers)
            ]
            for mx, my, mz in moves
        ],
        np.int32,
    )
    source = jnp.take(
        padded_around.reshape(4, -1, slot_count), box_rows, axis=1
    ).reshape(4, len(moves), 2, 2, layers, slot_count)
    source = source.reshape(4, len(moves), 4 * layers, slot_count).transpose(0, 2, 1, 3)
    source = source.reshape(4, 4 * layers, len(moves) * slot_count)
    move = np.repeat(np.array(moves, np.float32), slot_count, axis=0)
    own = packed.reshape(4, 4 * layers, slot_count)
    delta_x = own[0][..., :, None] - source[0][..., None, :] - move[:, 0]
    delta_y = own[1][..., :, None] - source[1][..., None, :] - move[:, 1]
    delta_z = own[2][..., :, None] - source[2][..., None, :] - move[:, 2]
    kernel = lax.rsqrt(delta_x * delta_x + delta_y * delta_y + delta_z * delta_z + softening_sq)
    centre = moves.index((0, 0, 0))
    column = jnp.arange(len(moves) * slot_count)[None, :]
    itself = column == jnp.arange(slot_count)[:, None] + centre * slot_count
    kernel = jnp.where(itself, 0.0, kernel)
    near = jnp.sum(kernel * source[3][..., None, :], axis=-1).reshape(2, 2, layers, slot_count)

    leaf_down_pts = 0.5 + 1.8 * unit_sphere
    leaf_far = point_sum(offsets, leaf_down_pts[:, None, None, None, :], leaf_local)
    parent_down_pts = 1.0 + 3.6 * unit_sphere
    local_float = jnp.arange(2).astype(jnp.float32)
    layer_parity = (jnp.arange(layers) % 2).astype(jnp.float32)
    in_parent = jnp.stack(
        [
            local_float[:, None, None, None] + offsets[0],
            local_float[None, :, None, None] + offsets[1],
            layer_parity[None, None, :, None] + offsets[2],
        ]
    )
    spread_local = jnp.repeat(parent_local, 2, axis=0)[None, None]
    parent_far = point_sum(in_parent, parent_down_pts[:, None, None, None, :], spread_local)
    total = near + leaf_far + parent_far
    return jnp.where(slot_index < counts[..., None], total, 0.0)


def solution(mesh):
    return jax.shard_map(
        shards,
        mesh=mesh,
        in_specs=(
            P(None, "gx", "gy", None, None),
            P("gx", "gy", None, None),
            P("gx", "gy", None),
            P(),
            P(),
            P(),
            P(),
        ),
        out_specs=P("gx", "gy", None, None),
        check_vma=False,
    )
```

```python
import functools

import jax
import numpy as np
import jax.numpy as jnp
from jax import lax
from jax.experimental import pallas as pl
from jax.experimental.pallas import tpu as pltpu
from jax.sharding import PartitionSpec as P

softening_sq = 0.0004
golden_turn = 2.399963229728653
highest = lax.Precision.HIGHEST


def sphere(point_count):
    middle = jnp.arange(point_count).astype(jnp.float32) + 0.5
    height = 1.0 - 2.0 * middle / point_count
    radial = jnp.sqrt(jnp.maximum(1.0 - height * height, 0.0))
    angle_turn = middle * golden_turn
    return jnp.stack([radial * jnp.cos(angle_turn), radial * jnp.sin(angle_turn), height])


def point_sum(targets, sources, weights):
    delta_x = targets[0][..., :, None] - sources[0][..., None, :]
    delta_y = targets[1][..., :, None] - sources[1][..., None, :]
    delta_z = targets[2][..., :, None] - sources[2][..., None, :]
    kernel = lax.rsqrt(delta_x * delta_x + delta_y * delta_y + delta_z * delta_z + softening_sq)
    return jnp.sum(kernel * weights[..., None, :], axis=-1)


def translation(unit_sphere, shift_x, shift_y, shift_z, radius):
    delta_x = (
        radius * (unit_sphere[0][:, None] - unit_sphere[0][None, :]) - shift_x[..., None, None]
    )
    delta_y = (
        radius * (unit_sphere[1][:, None] - unit_sphere[1][None, :]) - shift_y[..., None, None]
    )
    delta_z = (
        radius * (unit_sphere[2][:, None] - unit_sphere[2][None, :]) - shift_z[..., None, None]
    )
    return lax.rsqrt(delta_x * delta_x + delta_y * delta_y + delta_z * delta_z + softening_sq)


def child_points(unit_sphere):
    centre = jnp.arange(2).astype(jnp.float32) + 0.5
    point_count = unit_sphere.shape[1]
    box_shape = (2, 2, 2, point_count)
    along_x = jnp.broadcast_to(centre[:, None, None, None] + 0.9 * unit_sphere[0], box_shape)
    along_y = jnp.broadcast_to(centre[None, :, None, None] + 0.9 * unit_sphere[1], box_shape)
    along_z = jnp.broadcast_to(centre[None, None, :, None] + 0.9 * unit_sphere[2], box_shape)
    return jnp.stack([along_x, along_y, along_z]).reshape(3, 8 * point_count)


def rel_gather(buf, axis, dim):
    count = lax.axis_size(axis)
    have = 1
    while have < count:
        step = min(have, count - have)
        part = lax.slice_in_dim(buf, 0, step, axis=dim)
        got = lax.ppermute(part, axis, [(j, (j - have) % count) for j in range(count)])
        buf = jnp.concatenate([buf, got], axis=dim)
        have += step
    return buf


def exchange(items, axis):
    count = lax.axis_size(axis)
    heads, tails = [], []
    for cells, dim, width in items:
        heads.append(lax.slice_in_dim(cells, 0, width, axis=dim))
        tails.append(lax.slice_in_dim(cells, cells.shape[dim] - width, cells.shape[dim], axis=dim))
    sent_tail = jnp.concatenate([t.reshape(-1) for t in tails])
    sent_head = jnp.concatenate([h.reshape(-1) for h in heads])
    from_left = lax.ppermute(sent_tail, axis, [(i, (i + 1) % count) for i in range(count)])
    from_right = lax.ppermute(sent_head, axis, [((i + 1) % count, i) for i in range(count)])
    out, start = [], 0
    for (cells, dim, width), head, tail in zip(items, heads, tails):
        size = head.size
        before = from_left[start : start + size].reshape(tail.shape)
        after = from_right[start : start + size].reshape(head.shape)
        out.append(jnp.concatenate([before, cells, after], axis=dim))
        start += size
    return out


def split_top(values):
    scaled = values * 65537.0
    return scaled - (scaled - values)


def m2l_kernel(shift_count, rows, table_ref, index_ref, base_ref, windows_ref, out_ref):
    out_ref[...] = jnp.zeros_like(out_ref)
    vectors = out_ref.shape[0]
    pieces = index_ref.shape[0] // (2 * shift_count)

    def split_dot(left, matrix_high, matrix_low, dims):
        both = lax.dot_general(left, matrix_high, dims, preferred_element_type=jnp.float32)
        cross = lax.dot_general(
            left[:vectors], matrix_low, dims, preferred_element_type=jnp.float32
        )
        return both[:vectors] + both[vectors:] + cross

    def gathered(sign, index):
        first = (sign * shift_count + index) * pieces
        block = jnp.concatenate(
            [windows_ref[index_ref[first + piece]] for piece in range(pieces)], axis=0
        )
        top = split_top(block)
        return jnp.concatenate([top, block - top], axis=0).astype(jnp.bfloat16)

    def body(index, carry):
        shift_x = table_ref[3 * index]
        shift_y = table_ref[3 * index + 1]
        shift_z = table_ref[3 * index + 2]
        fwd = gathered(0, index)
        back = gathered(1, index)
        for row in range(0, base_ref.shape[1], rows):
            delta_x = base_ref[0, row : row + rows, :] - shift_x
            delta_y = base_ref[1, row : row + rows, :] - shift_y
            delta_z = base_ref[2, row : row + rows, :] - shift_z
            matrix = lax.rsqrt(
                delta_x * delta_x + delta_y * delta_y + delta_z * delta_z + softening_sq
            )
            matrix_top = split_top(matrix)
            matrix_high = matrix_top.astype(jnp.bfloat16)
            matrix_low = (matrix - matrix_top).astype(jnp.bfloat16)
            out_ref[:, row : row + rows] += split_dot(
                fwd, matrix_high, matrix_low, (((1,), (1,)), ((), ()))
            )
            out_ref[...] += split_dot(
                back[:, row : row + rows], matrix_high, matrix_low, (((1,), (0,)), ((), ()))
            )
        return carry

    lax.fori_loop(0, shift_count, body, 0)


def m2l(table, window_index, base, windows, vectors):
    shift_count = table.shape[0] // 3
    points = windows.shape[-1]
    return pl.pallas_call(
        functools.partial(m2l_kernel, shift_count, 128),
        out_shape=jax.ShapeDtypeStruct((vectors, points), jnp.float32),
        in_specs=[
            pl.BlockSpec(memory_space=pltpu.SMEM),
            pl.BlockSpec(memory_space=pltpu.SMEM),
            pl.BlockSpec(memory_space=pltpu.VMEM),
            pl.BlockSpec(memory_space=pltpu.VMEM),
        ],
        out_specs=pl.BlockSpec(memory_space=pltpu.VMEM),
        compiler_params=pltpu.CompilerParams(vmem_limit_bytes=48 * 1024 * 1024),
        cost_estimate=pl.CostEstimate(
            flops=12 * shift_count * vectors * points * points + 14 * shift_count * points * points,
            transcendentals=shift_count * points * points,
            bytes_accessed=4 * (windows.size + base.size + vectors * points),
        ),
    )(table, window_index, base, windows)


def far_shifts(span):
    shifts = []
    for dx in range(-span, span + 1):
        for dy in range(-span, span + 1):
            for dz in range(-span, span + 1):
                if max(abs(dx), abs(dy), abs(dz)) >= 2 and (dx, dy, dz) > (0, 0, 0):
                    shifts.append((dx, dy, dz))
    return shifts


def shards(offsets, charges, counts, c2e_leaf_up, c2e_leaf_down, c2e_top_up, c2e_top_down):
    slot_count = offsets.shape[-1]
    layers = offsets.shape[3]
    parent_layers = layers // 2
    points = c2e_leaf_up.shape[0]
    unit_sphere = sphere(points)
    slot_index = jnp.arange(slot_count)
    weights = jnp.where(slot_index < counts[..., None], charges, 0.0)
    packed = jnp.concatenate([offsets, weights[None]], axis=0)
    leaf_check_pts = 0.5 + 1.8 * unit_sphere
    leaf_check = point_sum(leaf_check_pts[:, None, None, None, :], offsets, weights)
    leaf_eq = jnp.einsum("ec,xyzc->xyze", c2e_leaf_up, leaf_check, precision=highest)
    packed_x, eq_x = exchange([(packed, 1, 1), (leaf_eq, 0, 2)], "gx")
    beside_all, cycle = exchange([(packed_x, 2, 1), (eq_x, 1, 2)], "gy")
    leaf_eq, beside_all, cycle = lax.optimization_barrier((leaf_eq, beside_all, cycle))
    children = child_points(unit_sphere)
    parent_weights = (
        leaf_eq.reshape(2, 2, parent_layers, 2, points)
        .transpose(2, 0, 1, 3, 4)
        .reshape(parent_layers, 8 * points)
    )
    parent_check_pts = 1.0 + 3.6 * unit_sphere
    parent_check = point_sum(parent_check_pts[:, None, :], children[:, None, :], parent_weights)
    parent_eq = jnp.einsum("ec,mc->me", c2e_top_up, parent_check, precision=highest)
    count_x = lax.axis_size("gx")
    count_y = lax.axis_size("gy")

    gathered = rel_gather(rel_gather(parent_eq[None, None], "gy", 1), "gx", 0)
    kept = []
    for rel_x in range(count_x):
        for rel_y in range(count_y):
            off_x = (rel_x + count_x // 2) % count_x - count_x // 2
            off_y = (rel_y + count_y // 2) % count_y - count_y // 2
            if abs(off_x) > 1 or abs(off_y) > 1:
                kept.append((rel_x * count_y + rel_y, off_x, off_y))
    kept_index = np.array([k[0] for k in kept], np.int32)
    kept_x = np.array([2.0 * k[1] for k in kept], np.float32)
    kept_y = np.array([2.0 * k[2] for k in kept], np.float32)
    far_sources = jnp.take(gathered.reshape(count_x * count_y, parent_layers, points), kept_index, axis=0)
    layer_float = jnp.arange(parent_layers).astype(jnp.float32)
    depth_pairs = 2.0 * (layer_float[None, :] - layer_float[:, None])
    far_shape = (parent_layers, len(kept), parent_layers, points)
    source_pts = jnp.stack(
        [
            jnp.broadcast_to(kept_x[None, :, None, None] + 1.8 * unit_sphere[0], far_shape),
            jnp.broadcast_to(kept_y[None, :, None, None] + 1.8 * unit_sphere[1], far_shape),
            jnp.broadcast_to(depth_pairs[:, None, :, None] + 1.8 * unit_sphere[2], far_shape),
        ]
    ).reshape(3, parent_layers, -1)
    far_check = point_sum(
        jnp.broadcast_to(1.8 * unit_sphere[:, None, :], (3, parent_layers, points)),
        source_pts,
        far_sources.reshape(-1),
    )

    framed = jnp.pad(cycle, ((1, 1), (1, 1), (3, 3), (0, 0)))
    shifts = far_shifts(3)
    depth_windows = jnp.stack(
        [framed[:, :, depth : depth + layers] for depth in range(7)], axis=2
    ).reshape(-1, layers, points)
    window_index = np.array(
        [
            np.ravel_multi_index(
                (ix + sign * dx + 3, iy + sign * dy + 3, sign * dz + 3), framed.shape[:2] + (7,)
            )
            for sign in (1, -1)
            for dx, dy, dz in shifts
            for ix in range(2)
            for iy in range(2)
        ],
        np.int32,
    )
    base = jnp.stack(
        [0.9 * (unit_sphere[i][:, None] - unit_sphere[i][None, :]) for i in range(3)]
    )
    table = jnp.asarray(np.array(shifts, np.float32).reshape(-1))
    leaf_down_check = m2l(table, jnp.asarray(window_index), base, depth_windows, 4 * layers).reshape(
        2, 2, layers, points
    )
    parent_local = jnp.einsum("ec,mc->me", c2e_top_down, far_check, precision=highest)
    leaf_local = jnp.einsum("ec,xyzc->xyze", c2e_leaf_down, leaf_down_check, precision=highest)

    padded_around = jnp.pad(beside_all, ((0, 0), (0, 0), (0, 0), (1, 1), (0, 0)))
    around_shape = padded_around.shape[1:4]
    moves = [(mx, my, mz) for mx in (-1, 0, 1) for my in (-1, 0, 1) for mz in (-1, 0, 1)]
    box_rows = np.array(
        [
            [
                np.ravel_multi_index((bx + 1 + mx, by + 1 + my, bz + 1 + mz), around_shape)
                for bx in range(2)
                for by in range(2)
                for bz in range(layers)
            ]
            for mx, my, mz in moves
        ],
        np.int32,
    )
    source = jnp.take(
        padded_around.reshape(4, -1, slot_count), box_rows, axis=1
    ).reshape(4, len(moves), 2, 2, layers, slot_count)
    source = source.reshape(4, len(moves), 4 * layers, slot_count).transpose(0, 2, 1, 3)
    source = source.reshape(4, 4 * layers, len(moves) * slot_count)
    move = np.repeat(np.array(moves, np.float32), slot_count, axis=0)
    own = packed.reshape(4, 4 * layers, slot_count)
    delta_x = own[0][..., :, None] - source[0][..., None, :] - move[:, 0]
    delta_y = own[1][..., :, None] - source[1][..., None, :] - move[:, 1]
    delta_z = own[2][..., :, None] - source[2][..., None, :] - move[:, 2]
    kernel = lax.rsqrt(delta_x * delta_x + delta_y * delta_y + delta_z * delta_z + softening_sq)
    centre = moves.index((0, 0, 0))
    column = jnp.arange(len(moves) * slot_count)[None, :]
    itself = column == jnp.arange(slot_count)[:, None] + centre * slot_count
    kernel = jnp.where(itself, 0.0, kernel)
    near = jnp.sum(kernel * source[3][..., None, :], axis=-1).reshape(2, 2, layers, slot_count)

    leaf_down_pts = 0.5 + 1.8 * unit_sphere
    leaf_far = point_sum(offsets, leaf_down_pts[:, None, None, None, :], leaf_local)
    parent_down_pts = 1.0 + 3.6 * unit_sphere
    local_float = jnp.arange(2).astype(jnp.float32)
    layer_parity = (jnp.arange(layers) % 2).astype(jnp.float32)
    in_parent = jnp.stack(
        [
            local_float[:, None, None, None] + offsets[0],
            local_float[None, :, None, None] + offsets[1],
            layer_parity[None, None, :, None] + offsets[2],
        ]
    )
    spread_local = jnp.repeat(parent_local, 2, axis=0)[None, None]
    parent_far = point_sum(in_parent, parent_down_pts[:, None, None, None, :], spread_local)
    total = near + leaf_far + parent_far
    return jnp.where(slot_index < counts[..., None], total, 0.0)


def solution(mesh):
    return jax.shard_map(
        shards,
        mesh=mesh,
        in_specs=(
            P(None, "gx", "gy", None, None),
            P("gx", "gy", None, None),
            P("gx", "gy", None),
            P(),
            P(),
            P(),
            P(),
        ),
        out_specs=P("gx", "gy", None, None),
        check_vma=False,
    )
```

```python
import functools

import jax
import numpy as np
import jax.numpy as jnp
from jax import lax
from jax.experimental import pallas as pl
from jax.experimental.pallas import tpu as pltpu
from jax.sharding import PartitionSpec as P

softening_sq = 0.0004
golden_turn = 2.399963229728653
highest = lax.Precision.HIGHEST


def sphere(point_count):
    middle = jnp.arange(point_count).astype(jnp.float32) + 0.5
    height = 1.0 - 2.0 * middle / point_count
    radial = jnp.sqrt(jnp.maximum(1.0 - height * height, 0.0))
    angle_turn = middle * golden_turn
    return jnp.stack([radial * jnp.cos(angle_turn), radial * jnp.sin(angle_turn), height])


def point_sum(targets, sources, weights):
    delta_x = targets[0][..., :, None] - sources[0][..., None, :]
    delta_y = targets[1][..., :, None] - sources[1][..., None, :]
    delta_z = targets[2][..., :, None] - sources[2][..., None, :]
    kernel = lax.rsqrt(delta_x * delta_x + delta_y * delta_y + delta_z * delta_z + softening_sq)
    return jnp.sum(kernel * weights[..., None, :], axis=-1)


def translation(unit_sphere, shift_x, shift_y, shift_z, radius):
    delta_x = (
        radius * (unit_sphere[0][:, None] - unit_sphere[0][None, :]) - shift_x[..., None, None]
    )
    delta_y = (
        radius * (unit_sphere[1][:, None] - unit_sphere[1][None, :]) - shift_y[..., None, None]
    )
    delta_z = (
        radius * (unit_sphere[2][:, None] - unit_sphere[2][None, :]) - shift_z[..., None, None]
    )
    return lax.rsqrt(delta_x * delta_x + delta_y * delta_y + delta_z * delta_z + softening_sq)


def child_points(unit_sphere):
    centre = jnp.arange(2).astype(jnp.float32) + 0.5
    point_count = unit_sphere.shape[1]
    box_shape = (2, 2, 2, point_count)
    along_x = jnp.broadcast_to(centre[:, None, None, None] + 0.9 * unit_sphere[0], box_shape)
    along_y = jnp.broadcast_to(centre[None, :, None, None] + 0.9 * unit_sphere[1], box_shape)
    along_z = jnp.broadcast_to(centre[None, None, :, None] + 0.9 * unit_sphere[2], box_shape)
    return jnp.stack([along_x, along_y, along_z]).reshape(3, 8 * point_count)


def exchange(items, axis):
    count = lax.axis_size(axis)
    heads, tails = [], []
    for cells, dim, width in items:
        heads.append(lax.slice_in_dim(cells, 0, width, axis=dim))
        tails.append(lax.slice_in_dim(cells, cells.shape[dim] - width, cells.shape[dim], axis=dim))
    sent_tail = jnp.concatenate([t.reshape(-1) for t in tails])
    sent_head = jnp.concatenate([h.reshape(-1) for h in heads])
    from_left = lax.ppermute(sent_tail, axis, [(i, (i + 1) % count) for i in range(count)])
    from_right = lax.ppermute(sent_head, axis, [((i + 1) % count, i) for i in range(count)])
    out, start = [], 0
    for (cells, dim, width), head, tail in zip(items, heads, tails):
        size = head.size
        before = from_left[start : start + size].reshape(tail.shape)
        after = from_right[start : start + size].reshape(head.shape)
        out.append(jnp.concatenate([before, cells, after], axis=dim))
        start += size
    return out


def split_top(values):
    scaled = values * 65537.0
    return scaled - (scaled - values)


def m2l_kernel(shift_count, rows, table_ref, index_ref, base_ref, windows_ref, out_ref):
    out_ref[...] = jnp.zeros_like(out_ref)
    vectors = out_ref.shape[0]
    pieces = index_ref.shape[0] // (2 * shift_count)

    def split_dot(left, matrix_high, matrix_low, dims):
        both = lax.dot_general(left, matrix_high, dims, preferred_element_type=jnp.float32)
        cross = lax.dot_general(
            left[:vectors], matrix_low, dims, preferred_element_type=jnp.float32
        )
        return both[:vectors] + both[vectors:] + cross

    def gathered(sign, index):
        first = (sign * shift_count + index) * pieces
        block = jnp.concatenate(
            [windows_ref[index_ref[first + piece]] for piece in range(pieces)], axis=0
        )
        top = split_top(block)
        return jnp.concatenate([top, block - top], axis=0).astype(jnp.bfloat16)

    def body(index, carry):
        shift_x = table_ref[3 * index]
        shift_y = table_ref[3 * index + 1]
        shift_z = table_ref[3 * index + 2]
        fwd = gathered(0, index)
        back = gathered(1, index)
        for row in range(0, base_ref.shape[1], rows):
            delta_x = base_ref[0, row : row + rows, :] - shift_x
            delta_y = base_ref[1, row : row + rows, :] - shift_y
            delta_z = base_ref[2, row : row + rows, :] - shift_z
            matrix = lax.rsqrt(
                delta_x * delta_x + delta_y * delta_y + delta_z * delta_z + softening_sq
            )
            matrix_top = split_top(matrix)
            matrix_high = matrix_top.astype(jnp.bfloat16)
            matrix_low = (matrix - matrix_top).astype(jnp.bfloat16)
            out_ref[:, row : row + rows] += split_dot(
                fwd, matrix_high, matrix_low, (((1,), (1,)), ((), ()))
            )
            out_ref[...] += split_dot(
                back[:, row : row + rows], matrix_high, matrix_low, (((1,), (0,)), ((), ()))
            )
        return carry

    lax.fori_loop(0, shift_count, body, 0)


def m2l(table, window_index, base, windows, vectors):
    shift_count = table.shape[0] // 3
    points = windows.shape[-1]
    return pl.pallas_call(
        functools.partial(m2l_kernel, shift_count, 128),
        out_shape=jax.ShapeDtypeStruct((vectors, points), jnp.float32),
        in_specs=[
            pl.BlockSpec(memory_space=pltpu.SMEM),
            pl.BlockSpec(memory_space=pltpu.SMEM),
            pl.BlockSpec(memory_space=pltpu.VMEM),
            pl.BlockSpec(memory_space=pltpu.VMEM),
        ],
        out_specs=pl.BlockSpec(memory_space=pltpu.VMEM),
        compiler_params=pltpu.CompilerParams(vmem_limit_bytes=48 * 1024 * 1024),
        cost_estimate=pl.CostEstimate(
            flops=12 * shift_count * vectors * points * points + 14 * shift_count * points * points,
            transcendentals=shift_count * points * points,
            bytes_accessed=4 * (windows.size + base.size + vectors * points),
        ),
    )(table, window_index, base, windows)


def far_shifts(span):
    shifts = []
    for dx in range(-span, span + 1):
        for dy in range(-span, span + 1):
            for dz in range(-span, span + 1):
                if max(abs(dx), abs(dy), abs(dz)) >= 2 and (dx, dy, dz) > (0, 0, 0):
                    shifts.append((dx, dy, dz))
    return shifts


def shards(offsets, charges, counts, c2e_leaf_up, c2e_leaf_down, c2e_top_up, c2e_top_down):
    slot_count = offsets.shape[-1]
    layers = offsets.shape[3]
    parent_layers = layers // 2
    points = c2e_leaf_up.shape[0]
    unit_sphere = sphere(points)
    slot_index = jnp.arange(slot_count)
    weights = jnp.where(slot_index < counts[..., None], charges, 0.0)
    packed = jnp.concatenate([offsets, weights[None]], axis=0)
    leaf_check_pts = 0.5 + 1.8 * unit_sphere
    leaf_check = point_sum(leaf_check_pts[:, None, None, None, :], offsets, weights)
    leaf_eq = jnp.einsum("ec,xyzc->xyze", c2e_leaf_up, leaf_check, precision=highest)
    packed_x, eq_x = exchange([(packed, 1, 1), (leaf_eq, 0, 2)], "gx")
    beside_all, cycle = exchange([(packed_x, 2, 1), (eq_x, 1, 2)], "gy")
    children = child_points(unit_sphere)
    parent_weights = (
        leaf_eq.reshape(2, 2, parent_layers, 2, points)
        .transpose(2, 0, 1, 3, 4)
        .reshape(parent_layers, 8 * points)
    )
    parent_check_pts = 1.0 + 3.6 * unit_sphere
    parent_check = point_sum(parent_check_pts[:, None, :], children[:, None, :], parent_weights)
    parent_eq = jnp.einsum("ec,mc->me", c2e_top_up, parent_check, precision=highest)
    count_x = lax.axis_size("gx")
    count_y = lax.axis_size("gy")

    kept = []
    for rel_x in range(count_x):
        for rel_y in range(count_y):
            off_x = (count_x // 2 - rel_x) % count_x - count_x // 2
            off_y = (count_y // 2 - rel_y) % count_y - count_y // 2
            if abs(off_x) > 1 or abs(off_y) > 1:
                kept.append((rel_x * count_y + rel_y, off_x, off_y))
    kept_index = np.array([k[0] for k in kept], np.int32)
    kept_x = np.array([2.0 * k[1] for k in kept], np.float32)
    kept_y = np.array([2.0 * k[2] for k in kept], np.float32)
    layer_float = jnp.arange(parent_layers).astype(jnp.float32)
    far_shape = (len(kept), parent_layers, points)
    check_pts = jnp.stack(
        [
            jnp.broadcast_to(1.8 * unit_sphere[0] - kept_x[:, None, None], far_shape),
            jnp.broadcast_to(1.8 * unit_sphere[1] - kept_y[:, None, None], far_shape),
            jnp.broadcast_to(1.8 * unit_sphere[2] + 2.0 * layer_float[:, None], far_shape),
        ]
    ).reshape(3, -1)
    equivalent_pts = jnp.stack(
        [
            jnp.broadcast_to(1.8 * unit_sphere[0], (parent_layers, points)),
            jnp.broadcast_to(1.8 * unit_sphere[1], (parent_layers, points)),
            2.0 * layer_float[:, None] + 1.8 * unit_sphere[2],
        ]
    ).reshape(3, -1)
    outgoing = point_sum(check_pts, equivalent_pts, parent_eq.reshape(-1))
    partial = (
        jnp.zeros((count_x * count_y, parent_layers * points), jnp.float32)
        .at[kept_index]
        .set(outgoing.reshape(len(kept), -1))
        .reshape(count_x, count_y, parent_layers, points)
    )
    for axis, dim, count in (("gy", 1, count_y), ("gx", 0, count_x)):
        half = count // 2
        while half >= 1:
            keep_part = lax.slice_in_dim(partial, 0, half, axis=dim)
            send_part = lax.slice_in_dim(partial, half, 2 * half, axis=dim)
            got = lax.ppermute(send_part, axis, [(j, (j + half) % count) for j in range(count)])
            partial = keep_part + got
            half //= 2
    far_check = partial[0, 0]

    framed = jnp.pad(cycle, ((1, 1), (1, 1), (3, 3), (0, 0)))
    shifts = far_shifts(3)
    depth_windows = jnp.stack(
        [framed[:, :, depth : depth + layers] for depth in range(7)], axis=2
    ).reshape(-1, layers, points)
    window_index = np.array(
        [
            np.ravel_multi_index(
                (ix + sign * dx + 3, iy + sign * dy + 3, sign * dz + 3), framed.shape[:2] + (7,)
            )
            for sign in (1, -1)
            for dx, dy, dz in shifts
            for ix in range(2)
            for iy in range(2)
        ],
        np.int32,
    )
    base = jnp.stack(
        [0.9 * (unit_sphere[i][:, None] - unit_sphere[i][None, :]) for i in range(3)]
    )
    table = jnp.asarray(np.array(shifts, np.float32).reshape(-1))
    leaf_down_check = m2l(table, jnp.asarray(window_index), base, depth_windows, 4 * layers).reshape(
        2, 2, layers, points
    )
    parent_local = jnp.einsum("ec,mc->me", c2e_top_down, far_check, precision=highest)
    leaf_local = jnp.einsum("ec,xyzc->xyze", c2e_leaf_down, leaf_down_check, precision=highest)

    padded_around = jnp.pad(beside_all, ((0, 0), (0, 0), (0, 0), (1, 1), (0, 0)))
    around_shape = padded_around.shape[1:4]
    moves = [(mx, my, mz) for mx in (-1, 0, 1) for my in (-1, 0, 1) for mz in (-1, 0, 1)]
    box_rows = np.array(
        [
            [
                np.ravel_multi_index((bx + 1 + mx, by + 1 + my, bz + 1 + mz), around_shape)
                for bx in range(2)
                for by in range(2)
                for bz in range(layers)
            ]
            for mx, my, mz in moves
        ],
        np.int32,
    )
    source = jnp.take(
        padded_around.reshape(4, -1, slot_count), box_rows, axis=1
    ).reshape(4, len(moves), 2, 2, layers, slot_count)
    source = source.reshape(4, len(moves), 4 * layers, slot_count).transpose(0, 2, 1, 3)
    source = source.reshape(4, 4 * layers, len(moves) * slot_count)
    move = np.repeat(np.array(moves, np.float32), slot_count, axis=0)
    own = packed.reshape(4, 4 * layers, slot_count)
    delta_x = own[0][..., :, None] - source[0][..., None, :] - move[:, 0]
    delta_y = own[1][..., :, None] - source[1][..., None, :] - move[:, 1]
    delta_z = own[2][..., :, None] - source[2][..., None, :] - move[:, 2]
    kernel = lax.rsqrt(delta_x * delta_x + delta_y * delta_y + delta_z * delta_z + softening_sq)
    centre = moves.index((0, 0, 0))
    column = jnp.arange(len(moves) * slot_count)[None, :]
    itself = column == jnp.arange(slot_count)[:, None] + centre * slot_count
    kernel = jnp.where(itself, 0.0, kernel)
    near = jnp.sum(kernel * source[3][..., None, :], axis=-1).reshape(2, 2, layers, slot_count)

    leaf_down_pts = 0.5 + 1.8 * unit_sphere
    leaf_far = point_sum(offsets, leaf_down_pts[:, None, None, None, :], leaf_local)
    parent_down_pts = 1.0 + 3.6 * unit_sphere
    local_float = jnp.arange(2).astype(jnp.float32)
    layer_parity = (jnp.arange(layers) % 2).astype(jnp.float32)
    in_parent = jnp.stack(
        [
            local_float[:, None, None, None] + offsets[0],
            local_float[None, :, None, None] + offsets[1],
            layer_parity[None, None, :, None] + offsets[2],
        ]
    )
    spread_local = jnp.repeat(parent_local, 2, axis=0)[None, None]
    parent_far = point_sum(in_parent, parent_down_pts[:, None, None, None, :], spread_local)
    total = near + leaf_far + parent_far
    return jnp.where(slot_index < counts[..., None], total, 0.0)


def solution(mesh):
    return jax.shard_map(
        shards,
        mesh=mesh,
        in_specs=(
            P(None, "gx", "gy", None, None),
            P("gx", "gy", None, None),
            P("gx", "gy", None),
            P(),
            P(),
            P(),
            P(),
        ),
        out_specs=P("gx", "gy", None, None),
        check_vma=False,
    )
```

```python
import functools

import jax
import numpy as np
import jax.numpy as jnp
from jax import lax
from jax.experimental import pallas as pl
from jax.experimental.pallas import tpu as pltpu
from jax.sharding import PartitionSpec as P

softening_sq = 0.0004
golden_turn = 2.399963229728653
highest = lax.Precision.HIGHEST


def sphere(point_count):
    middle = jnp.arange(point_count).astype(jnp.float32) + 0.5
    height = 1.0 - 2.0 * middle / point_count
    radial = jnp.sqrt(jnp.maximum(1.0 - height * height, 0.0))
    angle_turn = middle * golden_turn
    return jnp.stack([radial * jnp.cos(angle_turn), radial * jnp.sin(angle_turn), height])


def point_sum(targets, sources, weights):
    delta_x = targets[0][..., :, None] - sources[0][..., None, :]
    delta_y = targets[1][..., :, None] - sources[1][..., None, :]
    delta_z = targets[2][..., :, None] - sources[2][..., None, :]
    kernel = lax.rsqrt(delta_x * delta_x + delta_y * delta_y + delta_z * delta_z + softening_sq)
    return jnp.sum(kernel * weights[..., None, :], axis=-1)


def translation(unit_sphere, shift_x, shift_y, shift_z, radius):
    delta_x = (
        radius * (unit_sphere[0][:, None] - unit_sphere[0][None, :]) - shift_x[..., None, None]
    )
    delta_y = (
        radius * (unit_sphere[1][:, None] - unit_sphere[1][None, :]) - shift_y[..., None, None]
    )
    delta_z = (
        radius * (unit_sphere[2][:, None] - unit_sphere[2][None, :]) - shift_z[..., None, None]
    )
    return lax.rsqrt(delta_x * delta_x + delta_y * delta_y + delta_z * delta_z + softening_sq)


def child_points(unit_sphere):
    centre = jnp.arange(2).astype(jnp.float32) + 0.5
    point_count = unit_sphere.shape[1]
    box_shape = (2, 2, 2, point_count)
    along_x = jnp.broadcast_to(centre[:, None, None, None] + 0.9 * unit_sphere[0], box_shape)
    along_y = jnp.broadcast_to(centre[None, :, None, None] + 0.9 * unit_sphere[1], box_shape)
    along_z = jnp.broadcast_to(centre[None, None, :, None] + 0.9 * unit_sphere[2], box_shape)
    return jnp.stack([along_x, along_y, along_z]).reshape(3, 8 * point_count)


def rel_gather(buf, axis, dim):
    count = lax.axis_size(axis)
    have = 1
    while have < count:
        step = min(have, count - have)
        part = lax.slice_in_dim(buf, 0, step, axis=dim)
        got = lax.ppermute(part, axis, [(j, (j - have) % count) for j in range(count)])
        buf = jnp.concatenate([buf, got], axis=dim)
        have += step
    return buf


def exchange(items, axis):
    count = lax.axis_size(axis)
    heads, tails = [], []
    for cells, dim, width in items:
        heads.append(lax.slice_in_dim(cells, 0, width, axis=dim))
        tails.append(lax.slice_in_dim(cells, cells.shape[dim] - width, cells.shape[dim], axis=dim))
    sent_tail = jnp.concatenate([t.reshape(-1) for t in tails])
    sent_head = jnp.concatenate([h.reshape(-1) for h in heads])
    from_left = lax.ppermute(sent_tail, axis, [(i, (i + 1) % count) for i in range(count)])
    from_right = lax.ppermute(sent_head, axis, [((i + 1) % count, i) for i in range(count)])
    out, start = [], 0
    for (cells, dim, width), head, tail in zip(items, heads, tails):
        size = head.size
        before = from_left[start : start + size].reshape(tail.shape)
        after = from_right[start : start + size].reshape(head.shape)
        out.append(jnp.concatenate([before, cells, after], axis=dim))
        start += size
    return out


def split_top(values):
    scaled = values * 65537.0
    return scaled - (scaled - values)


def m2l_kernel(shift_count, rows, table_ref, index_ref, base_ref, windows_ref, out_ref):
    out_ref[...] = jnp.zeros_like(out_ref)
    vectors = out_ref.shape[0]
    pieces = index_ref.shape[0] // (2 * shift_count)

    def split_dot(left, matrix_high, matrix_low, dims):
        both = lax.dot_general(left, matrix_high, dims, preferred_element_type=jnp.float32)
        cross = lax.dot_general(
            left[:vectors], matrix_low, dims, preferred_element_type=jnp.float32
        )
        return both[:vectors] + both[vectors:] + cross

    def gathered(sign, index):
        first = (sign * shift_count + index) * pieces
        block = jnp.concatenate(
            [windows_ref[index_ref[first + piece]] for piece in range(pieces)], axis=0
        )
        top = split_top(block)
        return jnp.concatenate([top, block - top], axis=0).astype(jnp.bfloat16)

    def body(index, carry):
        shift_x = table_ref[3 * index]
        shift_y = table_ref[3 * index + 1]
        shift_z = table_ref[3 * index + 2]
        fwd = gathered(0, index)
        back = gathered(1, index)
        for row in range(0, base_ref.shape[1], rows):
            delta_x = base_ref[0, row : row + rows, :] - shift_x
            delta_y = base_ref[1, row : row + rows, :] - shift_y
            delta_z = base_ref[2, row : row + rows, :] - shift_z
            matrix = lax.rsqrt(
                delta_x * delta_x + delta_y * delta_y + delta_z * delta_z + softening_sq
            )
            matrix_top = split_top(matrix)
            matrix_high = matrix_top.astype(jnp.bfloat16)
            matrix_low = (matrix - matrix_top).astype(jnp.bfloat16)
            out_ref[:, row : row + rows] += split_dot(
                fwd, matrix_high, matrix_low, (((1,), (1,)), ((), ()))
            )
            out_ref[...] += split_dot(
                back[:, row : row + rows], matrix_high, matrix_low, (((1,), (0,)), ((), ()))
            )
        return carry

    lax.fori_loop(0, shift_count, body, 0)


def m2l(table, window_index, base, windows, vectors):
    shift_count = table.shape[0] // 3
    points = windows.shape[-1]
    return pl.pallas_call(
        functools.partial(m2l_kernel, shift_count, 256),
        out_shape=jax.ShapeDtypeStruct((vectors, points), jnp.float32),
        in_specs=[
            pl.BlockSpec(memory_space=pltpu.SMEM),
            pl.BlockSpec(memory_space=pltpu.SMEM),
            pl.BlockSpec(memory_space=pltpu.VMEM),
            pl.BlockSpec(memory_space=pltpu.VMEM),
        ],
        out_specs=pl.BlockSpec(memory_space=pltpu.VMEM),
        compiler_params=pltpu.CompilerParams(vmem_limit_bytes=48 * 1024 * 1024),
        cost_estimate=pl.CostEstimate(
            flops=12 * shift_count * vectors * points * points + 14 * shift_count * points * points,
            transcendentals=shift_count * points * points,
            bytes_accessed=4 * (windows.size + base.size + vectors * points),
        ),
    )(table, window_index, base, windows)


def far_shifts(span):
    shifts = []
    for dx in range(-span, span + 1):
        for dy in range(-span, span + 1):
            for dz in range(-span, span + 1):
                if max(abs(dx), abs(dy), abs(dz)) >= 2 and (dx, dy, dz) > (0, 0, 0):
                    shifts.append((dx, dy, dz))
    return shifts


def shards(offsets, charges, counts, c2e_leaf_up, c2e_leaf_down, c2e_top_up, c2e_top_down):
    slot_count = offsets.shape[-1]
    layers = offsets.shape[3]
    parent_layers = layers // 2
    points = c2e_leaf_up.shape[0]
    unit_sphere = sphere(points)
    slot_index = jnp.arange(slot_count)
    weights = jnp.where(slot_index < counts[..., None], charges, 0.0)
    packed = jnp.concatenate([offsets, weights[None]], axis=0)
    leaf_check_pts = 0.5 + 1.8 * unit_sphere
    leaf_check = point_sum(leaf_check_pts[:, None, None, None, :], offsets, weights)
    leaf_eq = jnp.einsum("ec,xyzc->xyze", c2e_leaf_up, leaf_check, precision=highest)
    packed_x, eq_x = exchange([(packed, 1, 1), (leaf_eq, 0, 2)], "gx")
    beside_all, cycle = exchange([(packed_x, 2, 1), (eq_x, 1, 2)], "gy")
    children = child_points(unit_sphere)
    parent_weights = (
        leaf_eq.reshape(2, 2, parent_layers, 2, points)
        .transpose(2, 0, 1, 3, 4)
        .reshape(parent_layers, 8 * points)
    )
    parent_check_pts = 1.0 + 3.6 * unit_sphere
    parent_check = point_sum(parent_check_pts[:, None, :], children[:, None, :], parent_weights)
    parent_eq = jnp.einsum("ec,mc->me", c2e_top_up, parent_check, precision=highest)
    count_x = lax.axis_size("gx")
    count_y = lax.axis_size("gy")

    gathered = rel_gather(rel_gather(parent_eq[None, None], "gy", 1), "gx", 0)
    kept = []
    for rel_x in range(count_x):
        for rel_y in range(count_y):
            off_x = (rel_x + count_x // 2) % count_x - count_x // 2
            off_y = (rel_y + count_y // 2) % count_y - count_y // 2
            if abs(off_x) > 1 or abs(off_y) > 1:
                kept.append((rel_x * count_y + rel_y, off_x, off_y))
    kept_index = np.array([k[0] for k in kept], np.int32)
    kept_x = np.array([2.0 * k[1] for k in kept], np.float32)
    kept_y = np.array([2.0 * k[2] for k in kept], np.float32)
    far_sources = jnp.take(gathered.reshape(count_x * count_y, parent_layers, points), kept_index, axis=0)
    layer_float = jnp.arange(parent_layers).astype(jnp.float32)
    depth_pairs = 2.0 * (layer_float[None, :] - layer_float[:, None])
    far_shape = (parent_layers, len(kept), parent_layers, points)
    source_pts = jnp.stack(
        [
            jnp.broadcast_to(kept_x[None, :, None, None] + 1.8 * unit_sphere[0], far_shape),
            jnp.broadcast_to(kept_y[None, :, None, None] + 1.8 * unit_sphere[1], far_shape),
            jnp.broadcast_to(depth_pairs[:, None, :, None] + 1.8 * unit_sphere[2], far_shape),
        ]
    ).reshape(3, parent_layers, -1)
    far_check = point_sum(
        jnp.broadcast_to(1.8 * unit_sphere[:, None, :], (3, parent_layers, points)),
        source_pts,
        far_sources.reshape(-1),
    )

    framed = jnp.pad(cycle, ((1, 1), (1, 1), (3, 3), (0, 0)))
    shifts = far_shifts(3)
    depth_windows = jnp.stack(
        [framed[:, :, depth : depth + layers] for depth in range(7)], axis=2
    ).reshape(-1, layers, points)
    window_index = np.array(
        [
            np.ravel_multi_index(
                (ix + sign * dx + 3, iy + sign * dy + 3, sign * dz + 3), framed.shape[:2] + (7,)
            )
            for sign in (1, -1)
            for dx, dy, dz in shifts
            for ix in range(2)
            for iy in range(2)
        ],
        np.int32,
    )
    base = jnp.stack(
        [0.9 * (unit_sphere[i][:, None] - unit_sphere[i][None, :]) for i in range(3)]
    )
    table = jnp.asarray(np.array(shifts, np.float32).reshape(-1))
    leaf_down_check = m2l(table, jnp.asarray(window_index), base, depth_windows, 4 * layers).reshape(
        2, 2, layers, points
    )
    parent_local = jnp.einsum("ec,mc->me", c2e_top_down, far_check, precision=highest)
    leaf_local = jnp.einsum("ec,xyzc->xyze", c2e_leaf_down, leaf_down_check, precision=highest)

    padded_around = jnp.pad(beside_all, ((0, 0), (0, 0), (0, 0), (1, 1), (0, 0)))
    around_shape = padded_around.shape[1:4]
    moves = [(mx, my, mz) for mx in (-1, 0, 1) for my in (-1, 0, 1) for mz in (-1, 0, 1)]
    box_rows = np.array(
        [
            [
                np.ravel_multi_index((bx + 1 + mx, by + 1 + my, bz + 1 + mz), around_shape)
                for bx in range(2)
                for by in range(2)
                for bz in range(layers)
            ]
            for mx, my, mz in moves
        ],
        np.int32,
    )
    source = jnp.take(
        padded_around.reshape(4, -1, slot_count), box_rows, axis=1
    ).reshape(4, len(moves), 2, 2, layers, slot_count)
    source = source.reshape(4, len(moves), 4 * layers, slot_count).transpose(0, 2, 1, 3)
    source = source.reshape(4, 4 * layers, len(moves) * slot_count)
    move = np.repeat(np.array(moves, np.float32), slot_count, axis=0)
    own = packed.reshape(4, 4 * layers, slot_count)
    delta_x = own[0][..., :, None] - source[0][..., None, :] - move[:, 0]
    delta_y = own[1][..., :, None] - source[1][..., None, :] - move[:, 1]
    delta_z = own[2][..., :, None] - source[2][..., None, :] - move[:, 2]
    kernel = lax.rsqrt(delta_x * delta_x + delta_y * delta_y + delta_z * delta_z + softening_sq)
    centre = moves.index((0, 0, 0))
    column = jnp.arange(len(moves) * slot_count)[None, :]
    itself = column == jnp.arange(slot_count)[:, None] + centre * slot_count
    kernel = jnp.where(itself, 0.0, kernel)
    near = jnp.sum(kernel * source[3][..., None, :], axis=-1).reshape(2, 2, layers, slot_count)

    leaf_down_pts = 0.5 + 1.8 * unit_sphere
    leaf_far = point_sum(offsets, leaf_down_pts[:, None, None, None, :], leaf_local)
    parent_down_pts = 1.0 + 3.6 * unit_sphere
    local_float = jnp.arange(2).astype(jnp.float32)
    layer_parity = (jnp.arange(layers) % 2).astype(jnp.float32)
    in_parent = jnp.stack(
        [
            local_float[:, None, None, None] + offsets[0],
            local_float[None, :, None, None] + offsets[1],
            layer_parity[None, None, :, None] + offsets[2],
        ]
    )
    spread_local = jnp.repeat(parent_local, 2, axis=0)[None, None]
    parent_far = point_sum(in_parent, parent_down_pts[:, None, None, None, :], spread_local)
    total = near + leaf_far + parent_far
    return jnp.where(slot_index < counts[..., None], total, 0.0)


def solution(mesh):
    return jax.shard_map(
        shards,
        mesh=mesh,
        in_specs=(
            P(None, "gx", "gy", None, None),
            P("gx", "gy", None, None),
            P("gx", "gy", None),
            P(),
            P(),
            P(),
            P(),
        ),
        out_specs=P("gx", "gy", None, None),
        check_vma=False,
    )
```

```python
import functools

import jax
import numpy as np
import jax.numpy as jnp
from jax import lax
from jax.experimental import pallas as pl
from jax.experimental.pallas import tpu as pltpu
from jax.sharding import PartitionSpec as P

softening_sq = 0.0004
golden_turn = 2.399963229728653
highest = lax.Precision.HIGHEST


def sphere(point_count):
    middle = jnp.arange(point_count).astype(jnp.float32) + 0.5
    height = 1.0 - 2.0 * middle / point_count
    radial = jnp.sqrt(jnp.maximum(1.0 - height * height, 0.0))
    angle_turn = middle * golden_turn
    return jnp.stack([radial * jnp.cos(angle_turn), radial * jnp.sin(angle_turn), height])


def point_sum(targets, sources, weights):
    delta_x = targets[0][..., :, None] - sources[0][..., None, :]
    delta_y = targets[1][..., :, None] - sources[1][..., None, :]
    delta_z = targets[2][..., :, None] - sources[2][..., None, :]
    kernel = lax.rsqrt(delta_x * delta_x + delta_y * delta_y + delta_z * delta_z + softening_sq)
    return jnp.sum(kernel * weights[..., None, :], axis=-1)


def translation(unit_sphere, shift_x, shift_y, shift_z, radius):
    delta_x = (
        radius * (unit_sphere[0][:, None] - unit_sphere[0][None, :]) - shift_x[..., None, None]
    )
    delta_y = (
        radius * (unit_sphere[1][:, None] - unit_sphere[1][None, :]) - shift_y[..., None, None]
    )
    delta_z = (
        radius * (unit_sphere[2][:, None] - unit_sphere[2][None, :]) - shift_z[..., None, None]
    )
    return lax.rsqrt(delta_x * delta_x + delta_y * delta_y + delta_z * delta_z + softening_sq)


def child_points(unit_sphere):
    centre = jnp.arange(2).astype(jnp.float32) + 0.5
    point_count = unit_sphere.shape[1]
    box_shape = (2, 2, 2, point_count)
    along_x = jnp.broadcast_to(centre[:, None, None, None] + 0.9 * unit_sphere[0], box_shape)
    along_y = jnp.broadcast_to(centre[None, :, None, None] + 0.9 * unit_sphere[1], box_shape)
    along_z = jnp.broadcast_to(centre[None, None, :, None] + 0.9 * unit_sphere[2], box_shape)
    return jnp.stack([along_x, along_y, along_z]).reshape(3, 8 * point_count)


def rel_gather(buf, axis, dim, have=1):
    count = lax.axis_size(axis)
    while have < count:
        step = min(have, count - have)
        part = lax.slice_in_dim(buf, 0, step, axis=dim)
        got = lax.ppermute(part, axis, [(j, (j - have) % count) for j in range(count)])
        buf = jnp.concatenate([buf, got], axis=dim)
        have += step
    return buf


def exchange(items, axis, rider=None):
    count = lax.axis_size(axis)
    heads, tails = [], []
    for cells, dim, width in items:
        heads.append(lax.slice_in_dim(cells, 0, width, axis=dim))
        tails.append(lax.slice_in_dim(cells, cells.shape[dim] - width, cells.shape[dim], axis=dim))
    sent_tail = jnp.concatenate([t.reshape(-1) for t in tails])
    sent_head = jnp.concatenate(
        [h.reshape(-1) for h in heads] + ([] if rider is None else [rider.reshape(-1)])
    )
    from_left = lax.ppermute(sent_tail, axis, [(i, (i + 1) % count) for i in range(count)])
    from_right = lax.ppermute(sent_head, axis, [((i + 1) % count, i) for i in range(count)])
    out, start = [], 0
    for (cells, dim, width), head, tail in zip(items, heads, tails):
        size = head.size
        before = from_left[start : start + size].reshape(tail.shape)
        after = from_right[start : start + size].reshape(head.shape)
        out.append(jnp.concatenate([before, cells, after], axis=dim))
        start += size
    if rider is not None:
        out.append(from_right[start:].reshape(rider.shape))
    return out


def split_top(values):
    scaled = values * 65537.0
    return scaled - (scaled - values)


def m2l_kernel(shift_count, rows, table_ref, index_ref, base_ref, windows_ref, out_ref):
    out_ref[...] = jnp.zeros_like(out_ref)
    vectors = out_ref.shape[0]
    pieces = index_ref.shape[0] // (2 * shift_count)

    def split_dot(left, matrix_high, matrix_low, dims):
        both = lax.dot_general(left, matrix_high, dims, preferred_element_type=jnp.float32)
        cross = lax.dot_general(
            left[:vectors], matrix_low, dims, preferred_element_type=jnp.float32
        )
        return both[:vectors] + both[vectors:] + cross

    def gathered(sign, index):
        first = (sign * shift_count + index) * pieces
        block = jnp.concatenate(
            [windows_ref[index_ref[first + piece]] for piece in range(pieces)], axis=0
        )
        top = split_top(block)
        return jnp.concatenate([top, block - top], axis=0).astype(jnp.bfloat16)

    def body(index, carry):
        shift_x = table_ref[3 * index]
        shift_y = table_ref[3 * index + 1]
        shift_z = table_ref[3 * index + 2]
        fwd = gathered(0, index)
        back = gathered(1, index)
        for row in range(0, base_ref.shape[1], rows):
            delta_x = base_ref[0, row : row + rows, :] - shift_x
            delta_y = base_ref[1, row : row + rows, :] - shift_y
            delta_z = base_ref[2, row : row + rows, :] - shift_z
            matrix = lax.rsqrt(
                delta_x * delta_x + delta_y * delta_y + delta_z * delta_z + softening_sq
            )
            matrix_top = split_top(matrix)
            matrix_high = matrix_top.astype(jnp.bfloat16)
            matrix_low = (matrix - matrix_top).astype(jnp.bfloat16)
            out_ref[:, row : row + rows] += split_dot(
                fwd, matrix_high, matrix_low, (((1,), (1,)), ((), ()))
            )
            out_ref[...] += split_dot(
                back[:, row : row + rows], matrix_high, matrix_low, (((1,), (0,)), ((), ()))
            )
        return carry

    lax.fori_loop(0, shift_count, body, 0)


def m2l(table, window_index, base, windows, vectors):
    shift_count = table.shape[0] // 3
    points = windows.shape[-1]
    return pl.pallas_call(
        functools.partial(m2l_kernel, shift_count, 128),
        out_shape=jax.ShapeDtypeStruct((vectors, points), jnp.float32),
        in_specs=[
            pl.BlockSpec(memory_space=pltpu.SMEM),
            pl.BlockSpec(memory_space=pltpu.SMEM),
            pl.BlockSpec(memory_space=pltpu.VMEM),
            pl.BlockSpec(memory_space=pltpu.VMEM),
        ],
        out_specs=pl.BlockSpec(memory_space=pltpu.VMEM),
        compiler_params=pltpu.CompilerParams(vmem_limit_bytes=48 * 1024 * 1024),
        cost_estimate=pl.CostEstimate(
            flops=12 * shift_count * vectors * points * points + 14 * shift_count * points * points,
            transcendentals=shift_count * points * points,
            bytes_accessed=4 * (windows.size + base.size + vectors * points),
        ),
    )(table, window_index, base, windows)


def far_shifts(span):
    shifts = []
    for dx in range(-span, span + 1):
        for dy in range(-span, span + 1):
            for dz in range(-span, span + 1):
                if max(abs(dx), abs(dy), abs(dz)) >= 2 and (dx, dy, dz) > (0, 0, 0):
                    shifts.append((dx, dy, dz))
    return shifts


def shards(offsets, charges, counts, c2e_leaf_up, c2e_leaf_down, c2e_top_up, c2e_top_down):
    slot_count = offsets.shape[-1]
    layers = offsets.shape[3]
    parent_layers = layers // 2
    points = c2e_leaf_up.shape[0]
    unit_sphere = sphere(points)
    slot_index = jnp.arange(slot_count)
    weights = jnp.where(slot_index < counts[..., None], charges, 0.0)
    packed = jnp.concatenate([offsets, weights[None]], axis=0)
    leaf_check_pts = 0.5 + 1.8 * unit_sphere
    leaf_check = point_sum(leaf_check_pts[:, None, None, None, :], offsets, weights)
    leaf_eq = jnp.einsum("ec,xyzc->xyze", c2e_leaf_up, leaf_check, precision=highest)
    children = child_points(unit_sphere)
    parent_weights = (
        leaf_eq.reshape(2, 2, parent_layers, 2, points)
        .transpose(2, 0, 1, 3, 4)
        .reshape(parent_layers, 8 * points)
    )
    parent_check_pts = 1.0 + 3.6 * unit_sphere
    parent_check = point_sum(parent_check_pts[:, None, :], children[:, None, :], parent_weights)
    parent_eq = jnp.einsum("ec,mc->me", c2e_top_up, parent_check, precision=highest)
    count_x = lax.axis_size("gx")
    count_y = lax.axis_size("gy")

    packed_x, eq_x, right_eq = exchange(
        [(packed, 1, 1), (leaf_eq, 0, 2)], "gx", rider=parent_eq
    )
    beside_all, cycle = exchange([(packed_x, 2, 1), (eq_x, 1, 2)], "gy")
    pair = jnp.stack([parent_eq, right_eq])[:, None]
    if count_x == 1:
        pair = parent_eq[None, None]
    gathered = rel_gather(rel_gather(pair, "gx", 0, min(2, count_x)), "gy", 1)
    kept = []
    for rel_x in range(count_x):
        for rel_y in range(count_y):
            off_x = (rel_x + count_x // 2) % count_x - count_x // 2
            off_y = (rel_y + count_y // 2) % count_y - count_y // 2
            if abs(off_x) > 1 or abs(off_y) > 1:
                kept.append((rel_x * count_y + rel_y, off_x, off_y))
    kept_index = np.array([k[0] for k in kept], np.int32)
    kept_x = np.array([2.0 * k[1] for k in kept], np.float32)
    kept_y = np.array([2.0 * k[2] for k in kept], np.float32)
    far_sources = jnp.take(gathered.reshape(count_x * count_y, parent_layers, points), kept_index, axis=0)
    layer_float = jnp.arange(parent_layers).astype(jnp.float32)
    depth_pairs = 2.0 * (layer_float[None, :] - layer_float[:, None])
    far_shape = (parent_layers, len(kept), parent_layers, points)
    source_pts = jnp.stack(
        [
            jnp.broadcast_to(kept_x[None, :, None, None] + 1.8 * unit_sphere[0], far_shape),
            jnp.broadcast_to(kept_y[None, :, None, None] + 1.8 * unit_sphere[1], far_shape),
            jnp.broadcast_to(depth_pairs[:, None, :, None] + 1.8 * unit_sphere[2], far_shape),
        ]
    ).reshape(3, parent_layers, -1)
    far_check = point_sum(
        jnp.broadcast_to(1.8 * unit_sphere[:, None, :], (3, parent_layers, points)),
        source_pts,
        far_sources.reshape(-1),
    )

    framed = jnp.pad(cycle, ((1, 1), (1, 1), (3, 3), (0, 0)))
    shifts = far_shifts(3)
    depth_windows = jnp.stack(
        [framed[:, :, depth : depth + layers] for depth in range(7)], axis=2
    ).reshape(-1, layers, points)
    window_index = np.array(
        [
            np.ravel_multi_index(
                (ix + sign * dx + 3, iy + sign * dy + 3, sign * dz + 3), framed.shape[:2] + (7,)
            )
            for sign in (1, -1)
            for dx, dy, dz in shifts
            for ix in range(2)
            for iy in range(2)
        ],
        np.int32,
    )
    base = jnp.stack(
        [0.9 * (unit_sphere[i][:, None] - unit_sphere[i][None, :]) for i in range(3)]
    )
    table = jnp.asarray(np.array(shifts, np.float32).reshape(-1))
    leaf_down_check = m2l(table, jnp.asarray(window_index), base, depth_windows, 4 * layers).reshape(
        2, 2, layers, points
    )
    parent_local = jnp.einsum("ec,mc->me", c2e_top_down, far_check, precision=highest)
    leaf_local = jnp.einsum("ec,xyzc->xyze", c2e_leaf_down, leaf_down_check, precision=highest)

    padded_around = jnp.pad(beside_all, ((0, 0), (0, 0), (0, 0), (1, 1), (0, 0)))
    around_shape = padded_around.shape[1:4]
    moves = [(mx, my, mz) for mx in (-1, 0, 1) for my in (-1, 0, 1) for mz in (-1, 0, 1)]
    box_rows = np.array(
        [
            [
                np.ravel_multi_index((bx + 1 + mx, by + 1 + my, bz + 1 + mz), around_shape)
                for bx in range(2)
                for by in range(2)
                for bz in range(layers)
            ]
            for mx, my, mz in moves
        ],
        np.int32,
    )
    source = jnp.take(
        padded_around.reshape(4, -1, slot_count), box_rows, axis=1
    ).reshape(4, len(moves), 2, 2, layers, slot_count)
    source = source.reshape(4, len(moves), 4 * layers, slot_count).transpose(0, 2, 1, 3)
    source = source.reshape(4, 4 * layers, len(moves) * slot_count)
    move = np.repeat(np.array(moves, np.float32), slot_count, axis=0)
    own = packed.reshape(4, 4 * layers, slot_count)
    delta_x = own[0][..., :, None] - source[0][..., None, :] - move[:, 0]
    delta_y = own[1][..., :, None] - source[1][..., None, :] - move[:, 1]
    delta_z = own[2][..., :, None] - source[2][..., None, :] - move[:, 2]
    kernel = lax.rsqrt(delta_x * delta_x + delta_y * delta_y + delta_z * delta_z + softening_sq)
    centre = moves.index((0, 0, 0))
    column = jnp.arange(len(moves) * slot_count)[None, :]
    itself = column == jnp.arange(slot_count)[:, None] + centre * slot_count
    kernel = jnp.where(itself, 0.0, kernel)
    near = jnp.sum(kernel * source[3][..., None, :], axis=-1).reshape(2, 2, layers, slot_count)

    leaf_down_pts = 0.5 + 1.8 * unit_sphere
    leaf_far = point_sum(offsets, leaf_down_pts[:, None, None, None, :], leaf_local)
    parent_down_pts = 1.0 + 3.6 * unit_sphere
    local_float = jnp.arange(2).astype(jnp.float32)
    layer_parity = (jnp.arange(layers) % 2).astype(jnp.float32)
    in_parent = jnp.stack(
        [
            local_float[:, None, None, None] + offsets[0],
            local_float[None, :, None, None] + offsets[1],
            layer_parity[None, None, :, None] + offsets[2],
        ]
    )
    spread_local = jnp.repeat(parent_local, 2, axis=0)[None, None]
    parent_far = point_sum(in_parent, parent_down_pts[:, None, None, None, :], spread_local)
    total = near + leaf_far + parent_far
    return jnp.where(slot_index < counts[..., None], total, 0.0)


def solution(mesh):
    return jax.shard_map(
        shards,
        mesh=mesh,
        in_specs=(
            P(None, "gx", "gy", None, None),
            P("gx", "gy", None, None),
            P("gx", "gy", None),
            P(),
            P(),
            P(),
            P(),
        ),
        out_specs=P("gx", "gy", None, None),
        check_vma=False,
    )
```

```python
import functools

import jax
import numpy as np
import jax.numpy as jnp
from jax import lax
from jax.experimental import pallas as pl
from jax.experimental.pallas import tpu as pltpu
from jax.sharding import PartitionSpec as P

softening_sq = 0.0004
golden_turn = 2.399963229728653
highest = lax.Precision.HIGHEST


def sphere(point_count):
    middle = jnp.arange(point_count).astype(jnp.float32) + 0.5
    height = 1.0 - 2.0 * middle / point_count
    radial = jnp.sqrt(jnp.maximum(1.0 - height * height, 0.0))
    angle_turn = middle * golden_turn
    return jnp.stack([radial * jnp.cos(angle_turn), radial * jnp.sin(angle_turn), height])


def point_sum(targets, sources, weights):
    delta_x = targets[0][..., :, None] - sources[0][..., None, :]
    delta_y = targets[1][..., :, None] - sources[1][..., None, :]
    delta_z = targets[2][..., :, None] - sources[2][..., None, :]
    kernel = lax.rsqrt(delta_x * delta_x + delta_y * delta_y + delta_z * delta_z + softening_sq)
    return jnp.sum(kernel * weights[..., None, :], axis=-1)


def translation(unit_sphere, shift_x, shift_y, shift_z, radius):
    delta_x = (
        radius * (unit_sphere[0][:, None] - unit_sphere[0][None, :]) - shift_x[..., None, None]
    )
    delta_y = (
        radius * (unit_sphere[1][:, None] - unit_sphere[1][None, :]) - shift_y[..., None, None]
    )
    delta_z = (
        radius * (unit_sphere[2][:, None] - unit_sphere[2][None, :]) - shift_z[..., None, None]
    )
    return lax.rsqrt(delta_x * delta_x + delta_y * delta_y + delta_z * delta_z + softening_sq)


def child_points(unit_sphere):
    centre = jnp.arange(2).astype(jnp.float32) + 0.5
    point_count = unit_sphere.shape[1]
    box_shape = (2, 2, 2, point_count)
    along_x = jnp.broadcast_to(centre[:, None, None, None] + 0.9 * unit_sphere[0], box_shape)
    along_y = jnp.broadcast_to(centre[None, :, None, None] + 0.9 * unit_sphere[1], box_shape)
    along_z = jnp.broadcast_to(centre[None, None, :, None] + 0.9 * unit_sphere[2], box_shape)
    return jnp.stack([along_x, along_y, along_z]).reshape(3, 8 * point_count)


def rel_gather(buf, axis, dim, have=1):
    count = lax.axis_size(axis)
    while have < count:
        step = min(have, count - have)
        part = lax.slice_in_dim(buf, 0, step, axis=dim)
        got = lax.ppermute(part, axis, [(j, (j - have) % count) for j in range(count)])
        buf = jnp.concatenate([buf, got], axis=dim)
        have += step
    return buf


def exchange(items, axis, rider=None):
    count = lax.axis_size(axis)
    heads, tails = [], []
    for cells, dim, width in items:
        heads.append(lax.slice_in_dim(cells, 0, width, axis=dim))
        tails.append(lax.slice_in_dim(cells, cells.shape[dim] - width, cells.shape[dim], axis=dim))
    sent_tail = jnp.concatenate([t.reshape(-1) for t in tails])
    sent_head = jnp.concatenate(
        [h.reshape(-1) for h in heads] + ([] if rider is None else [rider.reshape(-1)])
    )
    from_left = lax.ppermute(sent_tail, axis, [(i, (i + 1) % count) for i in range(count)])
    from_right = lax.ppermute(sent_head, axis, [((i + 1) % count, i) for i in range(count)])
    out, start = [], 0
    for (cells, dim, width), head, tail in zip(items, heads, tails):
        size = head.size
        before = from_left[start : start + size].reshape(tail.shape)
        after = from_right[start : start + size].reshape(head.shape)
        out.append(jnp.concatenate([before, cells, after], axis=dim))
        start += size
    if rider is not None:
        out.append(from_right[start:].reshape(rider.shape))
    return out


def split_top(values):
    scaled = values * 65537.0
    return scaled - (scaled - values)


def m2l_kernel(shift_count, rows, table_ref, index_ref, base_ref, windows_ref, out_ref):
    out_ref[...] = jnp.zeros_like(out_ref)
    vectors = out_ref.shape[0]
    pieces = index_ref.shape[0] // (2 * shift_count)

    def split_dot(left, matrix_high, matrix_low, dims):
        both = lax.dot_general(left, matrix_high, dims, preferred_element_type=jnp.float32)
        cross = lax.dot_general(
            left[:vectors], matrix_low, dims, preferred_element_type=jnp.float32
        )
        return both[:vectors] + both[vectors:] + cross

    def gathered(sign, index):
        first = (sign * shift_count + index) * pieces
        block = jnp.concatenate(
            [windows_ref[index_ref[first + piece]] for piece in range(pieces)], axis=0
        )
        top = split_top(block)
        return jnp.concatenate([top, block - top], axis=0).astype(jnp.bfloat16)

    def body(index, carry):
        scale_x = table_ref[4 * index]
        scale_y = table_ref[4 * index + 1]
        scale_z = table_ref[4 * index + 2]
        offset = table_ref[4 * index + 3]
        fwd = gathered(0, index)
        back = gathered(1, index)
        for row in range(0, base_ref.shape[1], rows):
            square = (
                (base_ref[3, row : row + rows, :] + offset)
                + scale_x * base_ref[0, row : row + rows, :]
                + scale_y * base_ref[1, row : row + rows, :]
                + scale_z * base_ref[2, row : row + rows, :]
            )
            matrix = lax.rsqrt(square)
            matrix_top = split_top(matrix)
            matrix_high = matrix_top.astype(jnp.bfloat16)
            matrix_low = (matrix - matrix_top).astype(jnp.bfloat16)
            out_ref[:, row : row + rows] += split_dot(
                fwd, matrix_high, matrix_low, (((1,), (1,)), ((), ()))
            )
            out_ref[...] += split_dot(
                back[:, row : row + rows], matrix_high, matrix_low, (((1,), (0,)), ((), ()))
            )
        return carry

    lax.fori_loop(0, shift_count, body, 0)


def m2l(table, window_index, base, windows, vectors):
    shift_count = table.shape[0] // 4
    points = windows.shape[-1]
    return pl.pallas_call(
        functools.partial(m2l_kernel, shift_count, 128),
        out_shape=jax.ShapeDtypeStruct((vectors, points), jnp.float32),
        in_specs=[
            pl.BlockSpec(memory_space=pltpu.SMEM),
            pl.BlockSpec(memory_space=pltpu.SMEM),
            pl.BlockSpec(memory_space=pltpu.VMEM),
            pl.BlockSpec(memory_space=pltpu.VMEM),
        ],
        out_specs=pl.BlockSpec(memory_space=pltpu.VMEM),
        compiler_params=pltpu.CompilerParams(vmem_limit_bytes=48 * 1024 * 1024),
        cost_estimate=pl.CostEstimate(
            flops=12 * shift_count * vectors * points * points + 14 * shift_count * points * points,
            transcendentals=shift_count * points * points,
            bytes_accessed=4 * (windows.size + base.size + vectors * points),
        ),
    )(table, window_index, base, windows)


def far_shifts(span):
    shifts = []
    for dx in range(-span, span + 1):
        for dy in range(-span, span + 1):
            for dz in range(-span, span + 1):
                if max(abs(dx), abs(dy), abs(dz)) >= 2 and (dx, dy, dz) > (0, 0, 0):
                    shifts.append((dx, dy, dz))
    return shifts


def shards(offsets, charges, counts, c2e_leaf_up, c2e_leaf_down, c2e_top_up, c2e_top_down):
    slot_count = offsets.shape[-1]
    layers = offsets.shape[3]
    parent_layers = layers // 2
    points = c2e_leaf_up.shape[0]
    unit_sphere = sphere(points)
    slot_index = jnp.arange(slot_count)
    weights = jnp.where(slot_index < counts[..., None], charges, 0.0)
    packed = jnp.concatenate([offsets, weights[None]], axis=0)
    leaf_check_pts = 0.5 + 1.8 * unit_sphere
    leaf_check = point_sum(leaf_check_pts[:, None, None, None, :], offsets, weights)
    leaf_eq = jnp.einsum("ec,xyzc->xyze", c2e_leaf_up, leaf_check, precision=highest)
    children = child_points(unit_sphere)
    parent_weights = (
        leaf_eq.reshape(2, 2, parent_layers, 2, points)
        .transpose(2, 0, 1, 3, 4)
        .reshape(parent_layers, 8 * points)
    )
    parent_check_pts = 1.0 + 3.6 * unit_sphere
    parent_check = point_sum(parent_check_pts[:, None, :], children[:, None, :], parent_weights)
    parent_eq = jnp.einsum("ec,mc->me", c2e_top_up, parent_check, precision=highest)
    count_x = lax.axis_size("gx")
    count_y = lax.axis_size("gy")

    packed_x, eq_x, right_eq = exchange(
        [(packed, 1, 1), (leaf_eq, 0, 2)], "gx", rider=parent_eq
    )
    beside_all, cycle = exchange([(packed_x, 2, 1), (eq_x, 1, 2)], "gy")
    pair = jnp.stack([parent_eq, right_eq])[:, None]
    if count_x == 1:
        pair = parent_eq[None, None]
    gathered = rel_gather(rel_gather(pair, "gx", 0, min(2, count_x)), "gy", 1)
    kept = []
    for rel_x in range(count_x):
        for rel_y in range(count_y):
            off_x = (rel_x + count_x // 2) % count_x - count_x // 2
            off_y = (rel_y + count_y // 2) % count_y - count_y // 2
            if abs(off_x) > 1 or abs(off_y) > 1:
                kept.append((rel_x * count_y + rel_y, off_x, off_y))
    kept_index = np.array([k[0] for k in kept], np.int32)
    kept_x = np.array([2.0 * k[1] for k in kept], np.float32)
    kept_y = np.array([2.0 * k[2] for k in kept], np.float32)
    far_sources = jnp.take(gathered.reshape(count_x * count_y, parent_layers, points), kept_index, axis=0)
    layer_float = jnp.arange(parent_layers).astype(jnp.float32)
    depth_pairs = 2.0 * (layer_float[None, :] - layer_float[:, None])
    far_shape = (parent_layers, len(kept), parent_layers, points)
    source_pts = jnp.stack(
        [
            jnp.broadcast_to(kept_x[None, :, None, None] + 1.8 * unit_sphere[0], far_shape),
            jnp.broadcast_to(kept_y[None, :, None, None] + 1.8 * unit_sphere[1], far_shape),
            jnp.broadcast_to(depth_pairs[:, None, :, None] + 1.8 * unit_sphere[2], far_shape),
        ]
    ).reshape(3, parent_layers, -1)
    far_check = point_sum(
        jnp.broadcast_to(1.8 * unit_sphere[:, None, :], (3, parent_layers, points)),
        source_pts,
        far_sources.reshape(-1),
    )

    framed = jnp.pad(cycle, ((1, 1), (1, 1), (3, 3), (0, 0)))
    shifts = far_shifts(3)
    depth_windows = jnp.stack(
        [framed[:, :, depth : depth + layers] for depth in range(7)], axis=2
    ).reshape(-1, layers, points)
    window_index = np.array(
        [
            np.ravel_multi_index(
                (ix + sign * dx + 3, iy + sign * dy + 3, sign * dz + 3), framed.shape[:2] + (7,)
            )
            for sign in (1, -1)
            for dx, dy, dz in shifts
            for ix in range(2)
            for iy in range(2)
        ],
        np.int32,
    )
    base = jnp.stack(
        [0.9 * (unit_sphere[i][:, None] - unit_sphere[i][None, :]) for i in range(3)]
    )
    base = jnp.concatenate([base, jnp.sum(base * base, axis=0)[None]], axis=0)
    shift_array = np.array(shifts, np.float64)
    table = np.concatenate(
        [-2.0 * shift_array, (shift_array**2).sum(1, keepdims=True) + softening_sq], axis=1
    )
    table = jnp.asarray(table.astype(np.float32).reshape(-1))
    leaf_down_check = m2l(table, jnp.asarray(window_index), base, depth_windows, 4 * layers).reshape(
        2, 2, layers, points
    )
    parent_local = jnp.einsum("ec,mc->me", c2e_top_down, far_check, precision=highest)
    leaf_local = jnp.einsum("ec,xyzc->xyze", c2e_leaf_down, leaf_down_check, precision=highest)

    padded_around = jnp.pad(beside_all, ((0, 0), (0, 0), (0, 0), (1, 1), (0, 0)))
    around_shape = padded_around.shape[1:4]
    moves = [(mx, my, mz) for mx in (-1, 0, 1) for my in (-1, 0, 1) for mz in (-1, 0, 1)]
    box_rows = np.array(
        [
            [
                np.ravel_multi_index((bx + 1 + mx, by + 1 + my, bz + 1 + mz), around_shape)
                for bx in range(2)
                for by in range(2)
                for bz in range(layers)
            ]
            for mx, my, mz in moves
        ],
        np.int32,
    )
    source = jnp.take(
        padded_around.reshape(4, -1, slot_count), box_rows, axis=1
    ).reshape(4, len(moves), 2, 2, layers, slot_count)
    source = source.reshape(4, len(moves), 4 * layers, slot_count).transpose(0, 2, 1, 3)
    source = source.reshape(4, 4 * layers, len(moves) * slot_count)
    move = np.repeat(np.array(moves, np.float32), slot_count, axis=0)
    own = packed.reshape(4, 4 * layers, slot_count)
    delta_x = own[0][..., :, None] - source[0][..., None, :] - move[:, 0]
    delta_y = own[1][..., :, None] - source[1][..., None, :] - move[:, 1]
    delta_z = own[2][..., :, None] - source[2][..., None, :] - move[:, 2]
    kernel = lax.rsqrt(delta_x * delta_x + delta_y * delta_y + delta_z * delta_z + softening_sq)
    centre = moves.index((0, 0, 0))
    column = jnp.arange(len(moves) * slot_count)[None, :]
    itself = column == jnp.arange(slot_count)[:, None] + centre * slot_count
    kernel = jnp.where(itself, 0.0, kernel)
    near = jnp.sum(kernel * source[3][..., None, :], axis=-1).reshape(2, 2, layers, slot_count)

    leaf_down_pts = 0.5 + 1.8 * unit_sphere
    leaf_far = point_sum(offsets, leaf_down_pts[:, None, None, None, :], leaf_local)
    parent_down_pts = 1.0 + 3.6 * unit_sphere
    local_float = jnp.arange(2).astype(jnp.float32)
    layer_parity = (jnp.arange(layers) % 2).astype(jnp.float32)
    in_parent = jnp.stack(
        [
            local_float[:, None, None, None] + offsets[0],
            local_float[None, :, None, None] + offsets[1],
            layer_parity[None, None, :, None] + offsets[2],
        ]
    )
    spread_local = jnp.repeat(parent_local, 2, axis=0)[None, None]
    parent_far = point_sum(in_parent, parent_down_pts[:, None, None, None, :], spread_local)
    total = near + leaf_far + parent_far
    return jnp.where(slot_index < counts[..., None], total, 0.0)


def solution(mesh):
    return jax.shard_map(
        shards,
        mesh=mesh,
        in_specs=(
            P(None, "gx", "gy", None, None),
            P("gx", "gy", None, None),
            P("gx", "gy", None),
            P(),
            P(),
            P(),
            P(),
        ),
        out_specs=P("gx", "gy", None, None),
        check_vma=False,
    )
```

```python
import functools

import jax
import numpy as np
import jax.numpy as jnp
from jax import lax
from jax.experimental import pallas as pl
from jax.experimental.pallas import tpu as pltpu
from jax.sharding import PartitionSpec as P

softening_sq = 0.0004
golden_turn = 2.399963229728653
highest = lax.Precision.HIGHEST


def sphere(point_count):
    middle = jnp.arange(point_count).astype(jnp.float32) + 0.5
    height = 1.0 - 2.0 * middle / point_count
    radial = jnp.sqrt(jnp.maximum(1.0 - height * height, 0.0))
    angle_turn = middle * golden_turn
    return jnp.stack([radial * jnp.cos(angle_turn), radial * jnp.sin(angle_turn), height])


def point_sum(targets, sources, weights):
    delta_x = targets[0][..., :, None] - sources[0][..., None, :]
    delta_y = targets[1][..., :, None] - sources[1][..., None, :]
    delta_z = targets[2][..., :, None] - sources[2][..., None, :]
    kernel = lax.rsqrt(delta_x * delta_x + delta_y * delta_y + delta_z * delta_z + softening_sq)
    return jnp.sum(kernel * weights[..., None, :], axis=-1)


def translation(unit_sphere, shift_x, shift_y, shift_z, radius):
    delta_x = (
        radius * (unit_sphere[0][:, None] - unit_sphere[0][None, :]) - shift_x[..., None, None]
    )
    delta_y = (
        radius * (unit_sphere[1][:, None] - unit_sphere[1][None, :]) - shift_y[..., None, None]
    )
    delta_z = (
        radius * (unit_sphere[2][:, None] - unit_sphere[2][None, :]) - shift_z[..., None, None]
    )
    return lax.rsqrt(delta_x * delta_x + delta_y * delta_y + delta_z * delta_z + softening_sq)


def child_points(unit_sphere):
    centre = jnp.arange(2).astype(jnp.float32) + 0.5
    point_count = unit_sphere.shape[1]
    box_shape = (2, 2, 2, point_count)
    along_x = jnp.broadcast_to(centre[:, None, None, None] + 0.9 * unit_sphere[0], box_shape)
    along_y = jnp.broadcast_to(centre[None, :, None, None] + 0.9 * unit_sphere[1], box_shape)
    along_z = jnp.broadcast_to(centre[None, None, :, None] + 0.9 * unit_sphere[2], box_shape)
    return jnp.stack([along_x, along_y, along_z]).reshape(3, 8 * point_count)


def rel_gather(buf, axis, dim, have=1):
    count = lax.axis_size(axis)
    while have < count:
        step = min(have, count - have)
        part = lax.slice_in_dim(buf, 0, step, axis=dim)
        got = lax.ppermute(part, axis, [(j, (j - have) % count) for j in range(count)])
        buf = jnp.concatenate([buf, got], axis=dim)
        have += step
    return buf


def exchange(items, axis, rider=None):
    count = lax.axis_size(axis)
    heads, tails = [], []
    for cells, dim, width in items:
        heads.append(lax.slice_in_dim(cells, 0, width, axis=dim))
        tails.append(lax.slice_in_dim(cells, cells.shape[dim] - width, cells.shape[dim], axis=dim))
    sent_tail = jnp.concatenate([t.reshape(-1) for t in tails])
    sent_head = jnp.concatenate(
        [h.reshape(-1) for h in heads] + ([] if rider is None else [rider.reshape(-1)])
    )
    from_left = lax.ppermute(sent_tail, axis, [(i, (i + 1) % count) for i in range(count)])
    from_right = lax.ppermute(sent_head, axis, [((i + 1) % count, i) for i in range(count)])
    out, start = [], 0
    for (cells, dim, width), head, tail in zip(items, heads, tails):
        size = head.size
        before = from_left[start : start + size].reshape(tail.shape)
        after = from_right[start : start + size].reshape(head.shape)
        out.append(jnp.concatenate([before, cells, after], axis=dim))
        start += size
    if rider is not None:
        out.append(from_right[start:].reshape(rider.shape))
    return out


def split_top(values):
    scaled = values * 65537.0
    return scaled - (scaled - values)


def m2l_kernel(shift_count, rows, table_ref, index_ref, base_ref, windows_ref, out_ref):
    out_ref[...] = jnp.zeros_like(out_ref)
    vectors = out_ref.shape[0]
    pieces = index_ref.shape[0] // (2 * shift_count)

    def split_dot(left, matrix_high, matrix_low, dims):
        both = lax.dot_general(left, matrix_high, dims, preferred_element_type=jnp.float32)
        cross = lax.dot_general(
            left[:vectors], matrix_low, dims, preferred_element_type=jnp.float32
        )
        return both[:vectors] + both[vectors:] + cross

    def gathered(sign, index):
        first = (sign * shift_count + index) * pieces
        block = jnp.concatenate(
            [windows_ref[index_ref[first + piece]] for piece in range(pieces)], axis=0
        )
        top = split_top(block)
        return jnp.concatenate([top, block - top], axis=0).astype(jnp.bfloat16)

    def body(index, carry):
        scale_x = table_ref[4 * index]
        scale_y = table_ref[4 * index + 1]
        scale_z = table_ref[4 * index + 2]
        offset = table_ref[4 * index + 3]
        fwd = gathered(0, index)
        back = gathered(1, index)
        for row in range(0, base_ref.shape[1], rows):
            square = (
                (base_ref[3, row : row + rows, :] + offset)
                + scale_x * base_ref[0, row : row + rows, :]
                + scale_y * base_ref[1, row : row + rows, :]
                + scale_z * base_ref[2, row : row + rows, :]
            )
            matrix = lax.rsqrt(square)
            matrix_top = split_top(matrix)
            matrix_high = matrix_top.astype(jnp.bfloat16)
            matrix_low = (matrix - matrix_top).astype(jnp.bfloat16)
            out_ref[:, row : row + rows] += split_dot(
                fwd, matrix_high, matrix_low, (((1,), (1,)), ((), ()))
            )
            out_ref[...] += split_dot(
                back[:, row : row + rows], matrix_high, matrix_low, (((1,), (0,)), ((), ()))
            )
        return carry

    lax.fori_loop(0, shift_count, body, 0)


def m2l(table, window_index, base, windows, vectors):
    shift_count = table.shape[0] // 4
    points = windows.shape[-1]
    return pl.pallas_call(
        functools.partial(m2l_kernel, shift_count, 128),
        out_shape=jax.ShapeDtypeStruct((vectors, points), jnp.float32),
        in_specs=[
            pl.BlockSpec(memory_space=pltpu.SMEM),
            pl.BlockSpec(memory_space=pltpu.SMEM),
            pl.BlockSpec(memory_space=pltpu.VMEM),
            pl.BlockSpec(memory_space=pltpu.VMEM),
        ],
        out_specs=pl.BlockSpec(memory_space=pltpu.VMEM),
        compiler_params=pltpu.CompilerParams(vmem_limit_bytes=48 * 1024 * 1024),
        cost_estimate=pl.CostEstimate(
            flops=12 * shift_count * vectors * points * points + 14 * shift_count * points * points,
            transcendentals=shift_count * points * points,
            bytes_accessed=4 * (windows.size + base.size + vectors * points),
        ),
    )(table, window_index, base, windows)


def far_shifts(span):
    shifts = []
    for dx in range(-span, span + 1):
        for dy in range(-span, span + 1):
            for dz in range(-span, span + 1):
                if max(abs(dx), abs(dy), abs(dz)) >= 2 and (dx, dy, dz) > (0, 0, 0):
                    shifts.append((dx, dy, dz))
    return shifts


def shards(offsets, charges, counts, c2e_leaf_up, c2e_leaf_down, c2e_top_up, c2e_top_down):
    slot_count = offsets.shape[-1]
    layers = offsets.shape[3]
    parent_layers = layers // 2
    points = c2e_leaf_up.shape[0]
    unit_sphere = sphere(points)
    slot_index = jnp.arange(slot_count)
    weights = jnp.where(slot_index < counts[..., None], charges, 0.0)
    packed = jnp.concatenate([offsets, weights[None]], axis=0)
    leaf_check_pts = 0.5 + 1.8 * unit_sphere
    leaf_check = point_sum(leaf_check_pts[:, None, None, None, :], offsets, weights)
    leaf_eq = jnp.einsum("ec,xyzc->xyze", c2e_leaf_up, leaf_check, precision=highest)
    children = child_points(unit_sphere)
    parent_weights = (
        leaf_eq.reshape(2, 2, parent_layers, 2, points)
        .transpose(2, 0, 1, 3, 4)
        .reshape(parent_layers, 8 * points)
    )
    parent_check_pts = 1.0 + 3.6 * unit_sphere
    parent_check = point_sum(parent_check_pts[:, None, :], children[:, None, :], parent_weights)
    parent_eq = jnp.einsum("ec,mc->me", c2e_top_up, parent_check, precision=highest)
    count_x = lax.axis_size("gx")
    count_y = lax.axis_size("gy")

    packed_x, eq_x, right_eq = exchange(
        [(packed, 1, 1), (leaf_eq, 0, 2)], "gx", rider=parent_eq
    )
    beside_all, cycle = exchange([(packed_x, 2, 1), (eq_x, 1, 2)], "gy")
    pair = jnp.stack([parent_eq, right_eq])[:, None]
    if count_x == 1:
        pair = parent_eq[None, None]
    gathered = rel_gather(rel_gather(pair, "gx", 0, min(2, count_x)), "gy", 1)
    kept = []
    for rel_x in range(count_x):
        for rel_y in range(count_y):
            off_x = (rel_x + count_x // 2) % count_x - count_x // 2
            off_y = (rel_y + count_y // 2) % count_y - count_y // 2
            if abs(off_x) > 1 or abs(off_y) > 1:
                kept.append((rel_x * count_y + rel_y, off_x, off_y))
    kept_index = np.array([k[0] for k in kept], np.int32)
    kept_x = np.array([2.0 * k[1] for k in kept], np.float32)
    kept_y = np.array([2.0 * k[2] for k in kept], np.float32)
    far_sources = jnp.take(gathered.reshape(count_x * count_y, parent_layers, points), kept_index, axis=0)
    layer_float = jnp.arange(parent_layers).astype(jnp.float32)
    depth_pairs = 2.0 * (layer_float[None, :] - layer_float[:, None])
    far_shape = (parent_layers, len(kept), parent_layers, points)
    source_pts = jnp.stack(
        [
            jnp.broadcast_to(kept_x[None, :, None, None] + 1.8 * unit_sphere[0], far_shape),
            jnp.broadcast_to(kept_y[None, :, None, None] + 1.8 * unit_sphere[1], far_shape),
            jnp.broadcast_to(depth_pairs[:, None, :, None] + 1.8 * unit_sphere[2], far_shape),
        ]
    ).reshape(3, parent_layers, -1)
    far_check = point_sum(
        jnp.broadcast_to(1.8 * unit_sphere[:, None, :], (3, parent_layers, points)),
        source_pts,
        far_sources.reshape(-1),
    )

    framed = jnp.pad(cycle, ((1, 1), (1, 1), (3, 3), (0, 0)))
    shifts = far_shifts(3)
    depth_windows = jnp.stack(
        [framed[:, :, depth : depth + layers] for depth in range(7)], axis=2
    ).reshape(-1, layers, points)
    window_index = np.array(
        [
            np.ravel_multi_index(
                (ix + sign * dx + 3, iy + sign * dy + 3, sign * dz + 3), framed.shape[:2] + (7,)
            )
            for sign in (1, -1)
            for dx, dy, dz in shifts
            for ix in range(2)
            for iy in range(2)
        ],
        np.int32,
    )
    base = jnp.stack(
        [0.9 * (unit_sphere[i][:, None] - unit_sphere[i][None, :]) for i in range(3)]
    )
    base = jnp.concatenate([base, jnp.sum(base * base, axis=0)[None]], axis=0)
    shift_array = np.array(shifts, np.float64)
    table = np.concatenate(
        [-2.0 * shift_array, (shift_array**2).sum(1, keepdims=True) + softening_sq], axis=1
    )
    table = jnp.asarray(table.astype(np.float32).reshape(-1))
    leaf_down_check = m2l(table, jnp.asarray(window_index), base, depth_windows, 4 * layers).reshape(
        2, 2, layers, points
    )
    parent_local = jnp.einsum("ec,mc->me", c2e_top_down, far_check, precision=highest)
    leaf_local = jnp.einsum("ec,xyzc->xyze", c2e_leaf_down, leaf_down_check, precision=highest)

    padded_around = jnp.pad(beside_all, ((0, 0), (0, 0), (0, 0), (1, 1), (0, 0)))
    around_shape = padded_around.shape[1:4]
    moves = [(mx, my, mz) for mx in (-1, 0, 1) for my in (-1, 0, 1) for mz in (-1, 0, 1)]
    box_rows = np.array(
        [
            [
                np.ravel_multi_index((bx + 1 + mx, by + 1 + my, bz + 1 + mz), around_shape)
                for bx in range(2)
                for by in range(2)
                for bz in range(layers)
            ]
            for mx, my, mz in moves
        ],
        np.int32,
    )
    source = jnp.take(
        padded_around.reshape(4, -1, slot_count), box_rows, axis=1
    ).reshape(4, len(moves), 2, 2, layers, slot_count)
    source = source.reshape(4, len(moves), 4 * layers, slot_count).transpose(0, 2, 1, 3)
    source = source.reshape(4, 4 * layers, len(moves) * slot_count)
    move = np.repeat(np.array(moves, np.float32), slot_count, axis=0)
    own = packed.reshape(4, 4 * layers, slot_count)
    delta_x = own[0][..., :, None] - source[0][..., None, :] - move[:, 0]
    delta_y = own[1][..., :, None] - source[1][..., None, :] - move[:, 1]
    delta_z = own[2][..., :, None] - source[2][..., None, :] - move[:, 2]
    kernel = lax.rsqrt(delta_x * delta_x + delta_y * delta_y + delta_z * delta_z + softening_sq)
    itself = lax.rsqrt(jnp.full((), softening_sq, jnp.float32)) * own[3]
    near = (jnp.sum(kernel * source[3][..., None, :], axis=-1) - itself).reshape(
        2, 2, layers, slot_count
    )

    leaf_down_pts = 0.5 + 1.8 * unit_sphere
    leaf_far = point_sum(offsets, leaf_down_pts[:, None, None, None, :], leaf_local)
    parent_down_pts = 1.0 + 3.6 * unit_sphere
    local_float = jnp.arange(2).astype(jnp.float32)
    layer_parity = (jnp.arange(layers) % 2).astype(jnp.float32)
    in_parent = jnp.stack(
        [
            local_float[:, None, None, None] + offsets[0],
            local_float[None, :, None, None] + offsets[1],
            layer_parity[None, None, :, None] + offsets[2],
        ]
    )
    spread_local = jnp.repeat(parent_local, 2, axis=0)[None, None]
    parent_far = point_sum(in_parent, parent_down_pts[:, None, None, None, :], spread_local)
    total = near + leaf_far + parent_far
    return jnp.where(slot_index < counts[..., None], total, 0.0)


def solution(mesh):
    return jax.shard_map(
        shards,
        mesh=mesh,
        in_specs=(
            P(None, "gx", "gy", None, None),
            P("gx", "gy", None, None),
            P("gx", "gy", None),
            P(),
            P(),
            P(),
            P(),
        ),
        out_specs=P("gx", "gy", None, None),
        check_vma=False,
    )
```

```python
import functools

import jax
import numpy as np
import jax.numpy as jnp
from jax import lax
from jax.experimental import pallas as pl
from jax.experimental.pallas import tpu as pltpu
from jax.sharding import PartitionSpec as P

softening_sq = 0.0004
golden_turn = 2.399963229728653
highest = lax.Precision.HIGHEST


def sphere(point_count):
    middle = jnp.arange(point_count).astype(jnp.float32) + 0.5
    height = 1.0 - 2.0 * middle / point_count
    radial = jnp.sqrt(jnp.maximum(1.0 - height * height, 0.0))
    angle_turn = middle * golden_turn
    return jnp.stack([radial * jnp.cos(angle_turn), radial * jnp.sin(angle_turn), height])


def point_sum(targets, sources, weights):
    delta_x = targets[0][..., :, None] - sources[0][..., None, :]
    delta_y = targets[1][..., :, None] - sources[1][..., None, :]
    delta_z = targets[2][..., :, None] - sources[2][..., None, :]
    kernel = lax.rsqrt(delta_x * delta_x + delta_y * delta_y + delta_z * delta_z + softening_sq)
    return jnp.sum(kernel * weights[..., None, :], axis=-1)


def translation(unit_sphere, shift_x, shift_y, shift_z, radius):
    delta_x = (
        radius * (unit_sphere[0][:, None] - unit_sphere[0][None, :]) - shift_x[..., None, None]
    )
    delta_y = (
        radius * (unit_sphere[1][:, None] - unit_sphere[1][None, :]) - shift_y[..., None, None]
    )
    delta_z = (
        radius * (unit_sphere[2][:, None] - unit_sphere[2][None, :]) - shift_z[..., None, None]
    )
    return lax.rsqrt(delta_x * delta_x + delta_y * delta_y + delta_z * delta_z + softening_sq)


def child_points(unit_sphere):
    centre = jnp.arange(2).astype(jnp.float32) + 0.5
    point_count = unit_sphere.shape[1]
    box_shape = (2, 2, 2, point_count)
    along_x = jnp.broadcast_to(centre[:, None, None, None] + 0.9 * unit_sphere[0], box_shape)
    along_y = jnp.broadcast_to(centre[None, :, None, None] + 0.9 * unit_sphere[1], box_shape)
    along_z = jnp.broadcast_to(centre[None, None, :, None] + 0.9 * unit_sphere[2], box_shape)
    return jnp.stack([along_x, along_y, along_z]).reshape(3, 8 * point_count)


def rel_gather(buf, axis, dim, have=1):
    count = lax.axis_size(axis)
    while have < count:
        step = min(have, count - have)
        part = lax.slice_in_dim(buf, 0, step, axis=dim)
        got = lax.ppermute(part, axis, [(j, (j - have) % count) for j in range(count)])
        buf = jnp.concatenate([buf, got], axis=dim)
        have += step
    return buf


def exchange(items, axis, rider=None):
    count = lax.axis_size(axis)
    heads, tails = [], []
    for cells, dim, width in items:
        heads.append(lax.slice_in_dim(cells, 0, width, axis=dim))
        tails.append(lax.slice_in_dim(cells, cells.shape[dim] - width, cells.shape[dim], axis=dim))
    sent_tail = jnp.concatenate([t.reshape(-1) for t in tails])
    sent_head = jnp.concatenate(
        [h.reshape(-1) for h in heads] + ([] if rider is None else [rider.reshape(-1)])
    )
    from_left = lax.ppermute(sent_tail, axis, [(i, (i + 1) % count) for i in range(count)])
    from_right = lax.ppermute(sent_head, axis, [((i + 1) % count, i) for i in range(count)])
    out, start = [], 0
    for (cells, dim, width), head, tail in zip(items, heads, tails):
        size = head.size
        before = from_left[start : start + size].reshape(tail.shape)
        after = from_right[start : start + size].reshape(head.shape)
        out.append(jnp.concatenate([before, cells, after], axis=dim))
        start += size
    if rider is not None:
        out.append(from_right[start:].reshape(rider.shape))
    return out


def split_top(values):
    scaled = values * 65537.0
    return scaled - (scaled - values)


def m2l_kernel(shift_count, rows, table_ref, index_ref, base_ref, windows_ref, out_ref):
    out_ref[...] = jnp.zeros_like(out_ref)
    vectors = out_ref.shape[0]
    pieces = index_ref.shape[0] // (2 * shift_count)

    def split_dot(left, matrix_high, matrix_low, dims):
        both = lax.dot_general(left, matrix_high, dims, preferred_element_type=jnp.float32)
        cross = lax.dot_general(
            left[:vectors], matrix_low, dims, preferred_element_type=jnp.float32
        )
        return both[:vectors] + both[vectors:] + cross

    def gathered(sign, index):
        first = (sign * shift_count + index) * pieces
        block = jnp.concatenate(
            [windows_ref[index_ref[first + piece]] for piece in range(pieces)], axis=0
        )
        top = split_top(block)
        return jnp.concatenate([top, block - top], axis=0).astype(jnp.bfloat16)

    def body(index, carry):
        scale_x = table_ref[4 * index]
        scale_y = table_ref[4 * index + 1]
        scale_z = table_ref[4 * index + 2]
        offset = table_ref[4 * index + 3]
        fwd = gathered(0, index)
        back = gathered(1, index)
        for row in range(0, base_ref.shape[1], rows):
            square = (
                (base_ref[3, row : row + rows, :] + offset)
                + scale_x * base_ref[0, row : row + rows, :]
                + scale_y * base_ref[1, row : row + rows, :]
                + scale_z * base_ref[2, row : row + rows, :]
            )
            matrix = lax.rsqrt(square)
            matrix_top = split_top(matrix)
            matrix_high = matrix_top.astype(jnp.bfloat16)
            matrix_low = (matrix - matrix_top).astype(jnp.bfloat16)
            out_ref[:, row : row + rows] += split_dot(
                fwd, matrix_high, matrix_low, (((1,), (1,)), ((), ()))
            )
            out_ref[...] += split_dot(
                back[:, row : row + rows], matrix_high, matrix_low, (((1,), (0,)), ((), ()))
            )
        return carry

    lax.fori_loop(0, shift_count, body, 0)


def m2l(table, window_index, base, windows, vectors):
    shift_count = table.shape[0] // 4
    points = windows.shape[-1]
    return pl.pallas_call(
        functools.partial(m2l_kernel, shift_count, 128),
        out_shape=jax.ShapeDtypeStruct((vectors, points), jnp.float32),
        in_specs=[
            pl.BlockSpec(memory_space=pltpu.SMEM),
            pl.BlockSpec(memory_space=pltpu.SMEM),
            pl.BlockSpec(memory_space=pltpu.VMEM),
            pl.BlockSpec(memory_space=pltpu.VMEM),
        ],
        out_specs=pl.BlockSpec(memory_space=pltpu.VMEM),
        compiler_params=pltpu.CompilerParams(vmem_limit_bytes=48 * 1024 * 1024),
        cost_estimate=pl.CostEstimate(
            flops=12 * shift_count * vectors * points * points + 14 * shift_count * points * points,
            transcendentals=shift_count * points * points,
            bytes_accessed=4 * (windows.size + base.size + vectors * points),
        ),
    )(table, window_index, base, windows)


def far_shifts(span):
    shifts = []
    for dx in range(-span, span + 1):
        for dy in range(-span, span + 1):
            for dz in range(-span, span + 1):
                if max(abs(dx), abs(dy), abs(dz)) >= 2 and (dx, dy, dz) > (0, 0, 0):
                    shifts.append((dx, dy, dz))
    return shifts


def shards(offsets, charges, counts, c2e_leaf_up, c2e_leaf_down, c2e_top_up, c2e_top_down):
    slot_count = offsets.shape[-1]
    layers = offsets.shape[3]
    parent_layers = layers // 2
    points = c2e_leaf_up.shape[0]
    unit_sphere = sphere(points)
    slot_index = jnp.arange(slot_count)
    weights = jnp.where(slot_index < counts[..., None], charges, 0.0)
    packed = jnp.concatenate([offsets, weights[None]], axis=0)
    leaf_check_pts = 0.5 + 1.8 * unit_sphere
    leaf_check = point_sum(leaf_check_pts[:, None, None, None, :], offsets, weights)
    leaf_eq = jnp.einsum("ec,xyzc->xyze", c2e_leaf_up, leaf_check, precision=highest)
    children = child_points(unit_sphere)
    parent_weights = (
        leaf_eq.reshape(2, 2, parent_layers, 2, points)
        .transpose(2, 0, 1, 3, 4)
        .reshape(parent_layers, 8 * points)
    )
    parent_check_pts = 1.0 + 3.6 * unit_sphere
    parent_check = point_sum(parent_check_pts[:, None, :], children[:, None, :], parent_weights)
    parent_eq = jnp.einsum("ec,mc->me", c2e_top_up, parent_check, precision=highest)
    count_x = lax.axis_size("gx")
    count_y = lax.axis_size("gy")

    packed_x, eq_x, right_eq = exchange(
        [(packed, 1, 1), (leaf_eq, 0, 2)], "gx", rider=parent_eq
    )
    beside_all, cycle = exchange([(packed_x, 2, 1), (eq_x, 1, 2)], "gy")
    pair = jnp.stack([parent_eq, right_eq])[:, None]
    if count_x == 1:
        pair = parent_eq[None, None]
    gathered = rel_gather(rel_gather(pair, "gx", 0, min(2, count_x)), "gy", 1)
    kept = []
    for rel_x in range(count_x):
        for rel_y in range(count_y):
            off_x = (rel_x + count_x // 2) % count_x - count_x // 2
            off_y = (rel_y + count_y // 2) % count_y - count_y // 2
            if abs(off_x) > 1 or abs(off_y) > 1:
                kept.append((rel_x * count_y + rel_y, off_x, off_y))
    kept_index = np.array([k[0] for k in kept], np.int32)
    kept_x = np.array([2.0 * k[1] for k in kept], np.float32)
    kept_y = np.array([2.0 * k[2] for k in kept], np.float32)
    far_sources = jnp.take(gathered.reshape(count_x * count_y, parent_layers, points), kept_index, axis=0)
    layer_float = jnp.arange(parent_layers).astype(jnp.float32)
    depth_pairs = 2.0 * (layer_float[None, :] - layer_float[:, None])
    far_shape = (parent_layers, len(kept), parent_layers, points)
    source_pts = jnp.stack(
        [
            jnp.broadcast_to(kept_x[None, :, None, None] + 1.8 * unit_sphere[0], far_shape),
            jnp.broadcast_to(kept_y[None, :, None, None] + 1.8 * unit_sphere[1], far_shape),
            jnp.broadcast_to(depth_pairs[:, None, :, None] + 1.8 * unit_sphere[2], far_shape),
        ]
    ).reshape(3, parent_layers, -1)
    far_check = point_sum(
        jnp.broadcast_to(1.8 * unit_sphere[:, None, :], (3, parent_layers, points)),
        source_pts,
        far_sources.reshape(-1),
    )

    framed = jnp.pad(cycle, ((1, 1), (1, 1), (3, 3), (0, 0)))
    shifts = far_shifts(3)
    depth_windows = jnp.stack(
        [framed[:, :, depth : depth + layers] for depth in range(7)], axis=2
    ).reshape(-1, layers, points)
    window_index = np.array(
        [
            np.ravel_multi_index(
                (ix + sign * dx + 3, iy + sign * dy + 3, sign * dz + 3), framed.shape[:2] + (7,)
            )
            for sign in (1, -1)
            for dx, dy, dz in shifts
            for ix in range(2)
            for iy in range(2)
        ],
        np.int32,
    )
    base = jnp.stack(
        [0.9 * (unit_sphere[i][:, None] - unit_sphere[i][None, :]) for i in range(3)]
    )
    base = jnp.concatenate([base, jnp.sum(base * base, axis=0)[None]], axis=0)
    shift_array = np.array(shifts, np.float64)
    table = np.concatenate(
        [-2.0 * shift_array, (shift_array**2).sum(1, keepdims=True) + softening_sq], axis=1
    )
    table = jnp.asarray(table.astype(np.float32).reshape(-1))
    leaf_down_check = m2l(table, jnp.asarray(window_index), base, depth_windows, 4 * layers).reshape(
        2, 2, layers, points
    )
    parent_local = jnp.einsum("ec,mc->me", c2e_top_down, far_check, precision=highest)
    leaf_local = jnp.einsum("ec,xyzc->xyze", c2e_leaf_down, leaf_down_check, precision=highest)

    padded_around = jnp.pad(beside_all, ((0, 0), (0, 0), (0, 0), (1, 1), (0, 0)))
    around_shape = padded_around.shape[1:4]
    moves = [(mx, my, mz) for mx in (-1, 0, 1) for my in (-1, 0, 1) for mz in (-1, 0, 1)]
    box_rows = np.array(
        [
            [
                np.ravel_multi_index((bx + 1 + mx, by + 1 + my, bz + 1 + mz), around_shape)
                for bx in range(2)
                for by in range(2)
                for bz in range(layers)
            ]
            for mx, my, mz in moves
        ],
        np.int32,
    )
    source = jnp.take(
        padded_around.reshape(4, -1, slot_count), box_rows, axis=1
    ).reshape(4, len(moves), 2, 2, layers, slot_count)
    source = source.reshape(4, len(moves), 4 * layers, slot_count).transpose(0, 2, 1, 3)
    source = source.reshape(4, 4 * layers, len(moves) * slot_count)
    move = np.repeat(np.array(moves, np.float32), slot_count, axis=0)
    own = packed.reshape(4, 4 * layers, slot_count)
    placed = lax.optimization_barrier(source[:3] + move.T[:, None, :])
    delta_x = own[0][..., :, None] - placed[0][..., None, :]
    delta_y = own[1][..., :, None] - placed[1][..., None, :]
    delta_z = own[2][..., :, None] - placed[2][..., None, :]
    kernel = lax.rsqrt(delta_x * delta_x + delta_y * delta_y + delta_z * delta_z + softening_sq)
    itself = lax.rsqrt(jnp.full((), softening_sq, jnp.float32)) * own[3]
    near = (jnp.sum(kernel * source[3][..., None, :], axis=-1) - itself).reshape(
        2, 2, layers, slot_count
    )

    leaf_down_pts = 0.5 + 1.8 * unit_sphere
    leaf_far = point_sum(offsets, leaf_down_pts[:, None, None, None, :], leaf_local)
    parent_down_pts = 1.0 + 3.6 * unit_sphere
    local_float = jnp.arange(2).astype(jnp.float32)
    layer_parity = (jnp.arange(layers) % 2).astype(jnp.float32)
    in_parent = jnp.stack(
        [
            local_float[:, None, None, None] + offsets[0],
            local_float[None, :, None, None] + offsets[1],
            layer_parity[None, None, :, None] + offsets[2],
        ]
    )
    spread_local = jnp.repeat(parent_local, 2, axis=0)[None, None]
    parent_far = point_sum(in_parent, parent_down_pts[:, None, None, None, :], spread_local)
    total = near + leaf_far + parent_far
    return jnp.where(slot_index < counts[..., None], total, 0.0)


def solution(mesh):
    return jax.shard_map(
        shards,
        mesh=mesh,
        in_specs=(
            P(None, "gx", "gy", None, None),
            P("gx", "gy", None, None),
            P("gx", "gy", None),
            P(),
            P(),
            P(),
            P(),
        ),
        out_specs=P("gx", "gy", None, None),
        check_vma=False,
    )
```

```python
import functools

import jax
import numpy as np
import jax.numpy as jnp
from jax import lax
from jax.experimental import pallas as pl
from jax.experimental.pallas import tpu as pltpu
from jax.sharding import PartitionSpec as P

softening_sq = 0.0004
golden_turn = 2.399963229728653
highest = lax.Precision.HIGHEST


def sphere(point_count):
    middle = jnp.arange(point_count).astype(jnp.float32) + 0.5
    height = 1.0 - 2.0 * middle / point_count
    radial = jnp.sqrt(jnp.maximum(1.0 - height * height, 0.0))
    angle_turn = middle * golden_turn
    return jnp.stack([radial * jnp.cos(angle_turn), radial * jnp.sin(angle_turn), height])


def point_sum(targets, sources, weights):
    delta_x = targets[0][..., :, None] - sources[0][..., None, :]
    delta_y = targets[1][..., :, None] - sources[1][..., None, :]
    delta_z = targets[2][..., :, None] - sources[2][..., None, :]
    kernel = lax.rsqrt(delta_x * delta_x + delta_y * delta_y + delta_z * delta_z + softening_sq)
    return jnp.sum(kernel * weights[..., None, :], axis=-1)


def translation(unit_sphere, shift_x, shift_y, shift_z, radius):
    delta_x = (
        radius * (unit_sphere[0][:, None] - unit_sphere[0][None, :]) - shift_x[..., None, None]
    )
    delta_y = (
        radius * (unit_sphere[1][:, None] - unit_sphere[1][None, :]) - shift_y[..., None, None]
    )
    delta_z = (
        radius * (unit_sphere[2][:, None] - unit_sphere[2][None, :]) - shift_z[..., None, None]
    )
    return lax.rsqrt(delta_x * delta_x + delta_y * delta_y + delta_z * delta_z + softening_sq)


def child_points(unit_sphere):
    centre = jnp.arange(2).astype(jnp.float32) + 0.5
    point_count = unit_sphere.shape[1]
    box_shape = (2, 2, 2, point_count)
    along_x = jnp.broadcast_to(centre[:, None, None, None] + 0.9 * unit_sphere[0], box_shape)
    along_y = jnp.broadcast_to(centre[None, :, None, None] + 0.9 * unit_sphere[1], box_shape)
    along_z = jnp.broadcast_to(centre[None, None, :, None] + 0.9 * unit_sphere[2], box_shape)
    return jnp.stack([along_x, along_y, along_z]).reshape(3, 8 * point_count)


def rel_gather(buf, axis, dim, have=1):
    count = lax.axis_size(axis)
    while have < count:
        step = min(have, count - have)
        part = lax.slice_in_dim(buf, 0, step, axis=dim)
        got = lax.ppermute(part, axis, [(j, (j - have) % count) for j in range(count)])
        buf = jnp.concatenate([buf, got], axis=dim)
        have += step
    return buf


def exchange(items, axis, rider=None):
    count = lax.axis_size(axis)
    heads, tails = [], []
    for cells, dim, width in items:
        heads.append(lax.slice_in_dim(cells, 0, width, axis=dim))
        tails.append(lax.slice_in_dim(cells, cells.shape[dim] - width, cells.shape[dim], axis=dim))
    sent_tail = jnp.concatenate([t.reshape(-1) for t in tails])
    sent_head = jnp.concatenate(
        [h.reshape(-1) for h in heads] + ([] if rider is None else [rider.reshape(-1)])
    )
    from_left = lax.ppermute(sent_tail, axis, [(i, (i + 1) % count) for i in range(count)])
    from_right = lax.ppermute(sent_head, axis, [((i + 1) % count, i) for i in range(count)])
    out, start = [], 0
    for (cells, dim, width), head, tail in zip(items, heads, tails):
        size = head.size
        before = from_left[start : start + size].reshape(tail.shape)
        after = from_right[start : start + size].reshape(head.shape)
        out.append(jnp.concatenate([before, cells, after], axis=dim))
        start += size
    if rider is not None:
        out.append(from_right[start:].reshape(rider.shape))
    return out


def split_top(values):
    scaled = values * 65537.0
    return scaled - (scaled - values)


def m2l_kernel(shift_count, rows, table_ref, index_ref, base_ref, windows_ref, out_ref):
    out_ref[...] = jnp.zeros_like(out_ref)
    vectors = out_ref.shape[0]
    pieces = index_ref.shape[0] // (2 * shift_count)

    def split_dot(left, matrix_high, matrix_low, dims):
        both = lax.dot_general(left, matrix_high, dims, preferred_element_type=jnp.float32)
        cross = lax.dot_general(
            left[:vectors], matrix_low, dims, preferred_element_type=jnp.float32
        )
        return both[:vectors] + both[vectors:] + cross

    def gathered(sign, index):
        first = (sign * shift_count + index) * pieces
        block = jnp.concatenate(
            [windows_ref[index_ref[first + piece]] for piece in range(pieces)], axis=0
        )
        top = split_top(block)
        return jnp.concatenate([top, block - top], axis=0).astype(jnp.bfloat16)

    def body(index, carry):
        scale_x = table_ref[4 * index]
        scale_y = table_ref[4 * index + 1]
        scale_z = table_ref[4 * index + 2]
        offset = table_ref[4 * index + 3]
        fwd = gathered(0, index)
        back = gathered(1, index)
        for row in range(0, base_ref.shape[1], rows):
            square = (
                (base_ref[3, row : row + rows, :] + offset)
                + scale_x * base_ref[0, row : row + rows, :]
                + scale_y * base_ref[1, row : row + rows, :]
                + scale_z * base_ref[2, row : row + rows, :]
            )
            matrix = lax.rsqrt(square)
            matrix_top = lax.reduce_precision(matrix, exponent_bits=8, mantissa_bits=7)
            matrix_high = matrix_top.astype(jnp.bfloat16)
            matrix_low = (matrix - matrix_top).astype(jnp.bfloat16)
            out_ref[:, row : row + rows] += split_dot(
                fwd, matrix_high, matrix_low, (((1,), (1,)), ((), ()))
            )
            out_ref[...] += split_dot(
                back[:, row : row + rows], matrix_high, matrix_low, (((1,), (0,)), ((), ()))
            )
        return carry

    lax.fori_loop(0, shift_count, body, 0)


def m2l(table, window_index, base, windows, vectors):
    shift_count = table.shape[0] // 4
    points = windows.shape[-1]
    return pl.pallas_call(
        functools.partial(m2l_kernel, shift_count, 128),
        out_shape=jax.ShapeDtypeStruct((vectors, points), jnp.float32),
        in_specs=[
            pl.BlockSpec(memory_space=pltpu.SMEM),
            pl.BlockSpec(memory_space=pltpu.SMEM),
            pl.BlockSpec(memory_space=pltpu.VMEM),
            pl.BlockSpec(memory_space=pltpu.VMEM),
        ],
        out_specs=pl.BlockSpec(memory_space=pltpu.VMEM),
        compiler_params=pltpu.CompilerParams(vmem_limit_bytes=48 * 1024 * 1024),
        cost_estimate=pl.CostEstimate(
            flops=12 * shift_count * vectors * points * points + 14 * shift_count * points * points,
            transcendentals=shift_count * points * points,
            bytes_accessed=4 * (windows.size + base.size + vectors * points),
        ),
    )(table, window_index, base, windows)


def far_shifts(span):
    shifts = []
    for dx in range(-span, span + 1):
        for dy in range(-span, span + 1):
            for dz in range(-span, span + 1):
                if max(abs(dx), abs(dy), abs(dz)) >= 2 and (dx, dy, dz) > (0, 0, 0):
                    shifts.append((dx, dy, dz))
    return shifts


def shards(offsets, charges, counts, c2e_leaf_up, c2e_leaf_down, c2e_top_up, c2e_top_down):
    slot_count = offsets.shape[-1]
    layers = offsets.shape[3]
    parent_layers = layers // 2
    points = c2e_leaf_up.shape[0]
    unit_sphere = sphere(points)
    slot_index = jnp.arange(slot_count)
    weights = jnp.where(slot_index < counts[..., None], charges, 0.0)
    packed = jnp.concatenate([offsets, weights[None]], axis=0)
    leaf_check_pts = 0.5 + 1.8 * unit_sphere
    leaf_check = point_sum(leaf_check_pts[:, None, None, None, :], offsets, weights)
    leaf_eq = jnp.einsum("ec,xyzc->xyze", c2e_leaf_up, leaf_check, precision=highest)
    children = child_points(unit_sphere)
    parent_weights = (
        leaf_eq.reshape(2, 2, parent_layers, 2, points)
        .transpose(2, 0, 1, 3, 4)
        .reshape(parent_layers, 8 * points)
    )
    parent_check_pts = 1.0 + 3.6 * unit_sphere
    parent_check = point_sum(parent_check_pts[:, None, :], children[:, None, :], parent_weights)
    parent_eq = jnp.einsum("ec,mc->me", c2e_top_up, parent_check, precision=highest)
    count_x = lax.axis_size("gx")
    count_y = lax.axis_size("gy")

    packed_x, eq_x, right_eq = exchange(
        [(packed, 1, 1), (leaf_eq, 0, 2)], "gx", rider=parent_eq
    )
    beside_all, cycle = exchange([(packed_x, 2, 1), (eq_x, 1, 2)], "gy")
    pair = jnp.stack([parent_eq, right_eq])[:, None]
    if count_x == 1:
        pair = parent_eq[None, None]
    gathered = rel_gather(rel_gather(pair, "gx", 0, min(2, count_x)), "gy", 1)
    kept = []
    for rel_x in range(count_x):
        for rel_y in range(count_y):
            off_x = (rel_x + count_x // 2) % count_x - count_x // 2
            off_y = (rel_y + count_y // 2) % count_y - count_y // 2
            if abs(off_x) > 1 or abs(off_y) > 1:
                kept.append((rel_x * count_y + rel_y, off_x, off_y))
    kept_index = np.array([k[0] for k in kept], np.int32)
    kept_x = np.array([2.0 * k[1] for k in kept], np.float32)
    kept_y = np.array([2.0 * k[2] for k in kept], np.float32)
    far_sources = jnp.take(gathered.reshape(count_x * count_y, parent_layers, points), kept_index, axis=0)
    layer_float = jnp.arange(parent_layers).astype(jnp.float32)
    depth_pairs = 2.0 * (layer_float[None, :] - layer_float[:, None])
    far_shape = (parent_layers, len(kept), parent_layers, points)
    source_pts = jnp.stack(
        [
            jnp.broadcast_to(kept_x[None, :, None, None] + 1.8 * unit_sphere[0], far_shape),
            jnp.broadcast_to(kept_y[None, :, None, None] + 1.8 * unit_sphere[1], far_shape),
            jnp.broadcast_to(depth_pairs[:, None, :, None] + 1.8 * unit_sphere[2], far_shape),
        ]
    ).reshape(3, parent_layers, -1)
    far_check = point_sum(
        jnp.broadcast_to(1.8 * unit_sphere[:, None, :], (3, parent_layers, points)),
        source_pts,
        far_sources.reshape(-1),
    )

    framed = jnp.pad(cycle, ((1, 1), (1, 1), (3, 3), (0, 0)))
    shifts = far_shifts(3)
    depth_windows = jnp.stack(
        [framed[:, :, depth : depth + layers] for depth in range(7)], axis=2
    ).reshape(-1, layers, points)
    window_index = np.array(
        [
            np.ravel_multi_index(
                (ix + sign * dx + 3, iy + sign * dy + 3, sign * dz + 3), framed.shape[:2] + (7,)
            )
            for sign in (1, -1)
            for dx, dy, dz in shifts
            for ix in range(2)
            for iy in range(2)
        ],
        np.int32,
    )
    base = jnp.stack(
        [0.9 * (unit_sphere[i][:, None] - unit_sphere[i][None, :]) for i in range(3)]
    )
    base = jnp.concatenate([base, jnp.sum(base * base, axis=0)[None]], axis=0)
    shift_array = np.array(shifts, np.float64)
    table = np.concatenate(
        [-2.0 * shift_array, (shift_array**2).sum(1, keepdims=True) + softening_sq], axis=1
    )
    table = jnp.asarray(table.astype(np.float32).reshape(-1))
    leaf_down_check = m2l(table, jnp.asarray(window_index), base, depth_windows, 4 * layers).reshape(
        2, 2, layers, points
    )
    parent_local = jnp.einsum("ec,mc->me", c2e_top_down, far_check, precision=highest)
    leaf_local = jnp.einsum("ec,xyzc->xyze", c2e_leaf_down, leaf_down_check, precision=highest)

    padded_around = jnp.pad(beside_all, ((0, 0), (0, 0), (0, 0), (1, 1), (0, 0)))
    around_shape = padded_around.shape[1:4]
    moves = [(mx, my, mz) for mx in (-1, 0, 1) for my in (-1, 0, 1) for mz in (-1, 0, 1)]
    box_rows = np.array(
        [
            [
                np.ravel_multi_index((bx + 1 + mx, by + 1 + my, bz + 1 + mz), around_shape)
                for bx in range(2)
                for by in range(2)
                for bz in range(layers)
            ]
            for mx, my, mz in moves
        ],
        np.int32,
    )
    source = jnp.take(
        padded_around.reshape(4, -1, slot_count), box_rows, axis=1
    ).reshape(4, len(moves), 2, 2, layers, slot_count)
    source = source.reshape(4, len(moves), 4 * layers, slot_count).transpose(0, 2, 1, 3)
    source = source.reshape(4, 4 * layers, len(moves) * slot_count)
    move = np.repeat(np.array(moves, np.float32), slot_count, axis=0)
    own = packed.reshape(4, 4 * layers, slot_count)
    placed = lax.optimization_barrier(source[:3] + move.T[:, None, :])
    delta_x = own[0][..., :, None] - placed[0][..., None, :]
    delta_y = own[1][..., :, None] - placed[1][..., None, :]
    delta_z = own[2][..., :, None] - placed[2][..., None, :]
    kernel = lax.rsqrt(delta_x * delta_x + delta_y * delta_y + delta_z * delta_z + softening_sq)
    itself = lax.rsqrt(jnp.full((), softening_sq, jnp.float32)) * own[3]
    near = (jnp.sum(kernel * source[3][..., None, :], axis=-1) - itself).reshape(
        2, 2, layers, slot_count
    )

    leaf_down_pts = 0.5 + 1.8 * unit_sphere
    leaf_far = point_sum(offsets, leaf_down_pts[:, None, None, None, :], leaf_local)
    parent_down_pts = 1.0 + 3.6 * unit_sphere
    local_float = jnp.arange(2).astype(jnp.float32)
    layer_parity = (jnp.arange(layers) % 2).astype(jnp.float32)
    in_parent = jnp.stack(
        [
            local_float[:, None, None, None] + offsets[0],
            local_float[None, :, None, None] + offsets[1],
            layer_parity[None, None, :, None] + offsets[2],
        ]
    )
    spread_local = jnp.repeat(parent_local, 2, axis=0)[None, None]
    parent_far = point_sum(in_parent, parent_down_pts[:, None, None, None, :], spread_local)
    total = near + leaf_far + parent_far
    return jnp.where(slot_index < counts[..., None], total, 0.0)


def solution(mesh):
    return jax.shard_map(
        shards,
        mesh=mesh,
        in_specs=(
            P(None, "gx", "gy", None, None),
            P("gx", "gy", None, None),
            P("gx", "gy", None),
            P(),
            P(),
            P(),
            P(),
        ),
        out_specs=P("gx", "gy", None, None),
        check_vma=False,
    )
```

```python
import functools

import jax
import numpy as np
import jax.numpy as jnp
from jax import lax
from jax.experimental import pallas as pl
from jax.experimental.pallas import tpu as pltpu
from jax.sharding import PartitionSpec as P

softening_sq = 0.0004
golden_turn = 2.399963229728653
highest = lax.Precision.HIGHEST


def sphere(point_count):
    middle = jnp.arange(point_count).astype(jnp.float32) + 0.5
    height = 1.0 - 2.0 * middle / point_count
    radial = jnp.sqrt(jnp.maximum(1.0 - height * height, 0.0))
    angle_turn = middle * golden_turn
    return jnp.stack([radial * jnp.cos(angle_turn), radial * jnp.sin(angle_turn), height])


def point_sum(targets, sources, weights):
    delta_x = targets[0][..., :, None] - sources[0][..., None, :]
    delta_y = targets[1][..., :, None] - sources[1][..., None, :]
    delta_z = targets[2][..., :, None] - sources[2][..., None, :]
    kernel = lax.rsqrt(delta_x * delta_x + delta_y * delta_y + delta_z * delta_z + softening_sq)
    return jnp.sum(kernel * weights[..., None, :], axis=-1)


def translation(unit_sphere, shift_x, shift_y, shift_z, radius):
    delta_x = (
        radius * (unit_sphere[0][:, None] - unit_sphere[0][None, :]) - shift_x[..., None, None]
    )
    delta_y = (
        radius * (unit_sphere[1][:, None] - unit_sphere[1][None, :]) - shift_y[..., None, None]
    )
    delta_z = (
        radius * (unit_sphere[2][:, None] - unit_sphere[2][None, :]) - shift_z[..., None, None]
    )
    return lax.rsqrt(delta_x * delta_x + delta_y * delta_y + delta_z * delta_z + softening_sq)


def child_points(unit_sphere):
    centre = jnp.arange(2).astype(jnp.float32) + 0.5
    point_count = unit_sphere.shape[1]
    box_shape = (2, 2, 2, point_count)
    along_x = jnp.broadcast_to(centre[:, None, None, None] + 0.9 * unit_sphere[0], box_shape)
    along_y = jnp.broadcast_to(centre[None, :, None, None] + 0.9 * unit_sphere[1], box_shape)
    along_z = jnp.broadcast_to(centre[None, None, :, None] + 0.9 * unit_sphere[2], box_shape)
    return jnp.stack([along_x, along_y, along_z]).reshape(3, 8 * point_count)


def rel_gather(buf, axis, dim, have=1):
    count = lax.axis_size(axis)
    while have < count:
        step = min(have, count - have)
        part = lax.slice_in_dim(buf, 0, step, axis=dim)
        got = lax.ppermute(part, axis, [(j, (j - have) % count) for j in range(count)])
        buf = jnp.concatenate([buf, got], axis=dim)
        have += step
    return buf


def exchange(items, axis, rider=None):
    count = lax.axis_size(axis)
    heads, tails = [], []
    for cells, dim, width in items:
        heads.append(lax.slice_in_dim(cells, 0, width, axis=dim))
        tails.append(lax.slice_in_dim(cells, cells.shape[dim] - width, cells.shape[dim], axis=dim))
    sent_tail = jnp.concatenate([t.reshape(-1) for t in tails])
    sent_head = jnp.concatenate(
        [h.reshape(-1) for h in heads] + ([] if rider is None else [rider.reshape(-1)])
    )
    from_left = lax.ppermute(sent_tail, axis, [(i, (i + 1) % count) for i in range(count)])
    from_right = lax.ppermute(sent_head, axis, [((i + 1) % count, i) for i in range(count)])
    out, start = [], 0
    for (cells, dim, width), head, tail in zip(items, heads, tails):
        size = head.size
        before = from_left[start : start + size].reshape(tail.shape)
        after = from_right[start : start + size].reshape(head.shape)
        out.append(jnp.concatenate([before, cells, after], axis=dim))
        start += size
    if rider is not None:
        out.append(from_right[start:].reshape(rider.shape))
    return out


def split_top(values):
    scaled = values * 65537.0
    return scaled - (scaled - values)


def m2l_kernel(shift_count, rows, table_ref, index_ref, base_ref, windows_ref, out_ref):
    out_ref[...] = jnp.zeros_like(out_ref)
    vectors = out_ref.shape[0]
    pieces = index_ref.shape[0] // (2 * shift_count)

    def split_dot(left, matrix_high, matrix_low, dims):
        both = lax.dot_general(left, matrix_high, dims, preferred_element_type=jnp.float32)
        cross = lax.dot_general(
            left[:vectors], matrix_low, dims, preferred_element_type=jnp.float32
        )
        return both[:vectors] + both[vectors:] + cross

    def gathered(sign, index):
        first = (sign * shift_count + index) * pieces
        block = jnp.concatenate(
            [windows_ref[index_ref[first + piece]] for piece in range(pieces)], axis=0
        )
        top = split_top(block)
        return jnp.concatenate([top, block - top], axis=0).astype(jnp.bfloat16)

    def body(index, carry):
        scale_x = table_ref[4 * index]
        scale_y = table_ref[4 * index + 1]
        scale_z = table_ref[4 * index + 2]
        offset = table_ref[4 * index + 3]
        fwd = gathered(0, index)
        back = gathered(1, index)
        for row in range(0, base_ref.shape[1], rows):
            square = (
                (base_ref[3, row : row + rows, :] + offset)
                + scale_x * base_ref[0, row : row + rows, :]
                + scale_y * base_ref[1, row : row + rows, :]
                + scale_z * base_ref[2, row : row + rows, :]
            )
            matrix = lax.rsqrt(square)
            matrix_top = split_top(matrix)
            matrix_high = matrix_top.astype(jnp.bfloat16)
            matrix_low = (matrix - matrix_top).astype(jnp.bfloat16)
            out_ref[:, row : row + rows] += split_dot(
                fwd, matrix_high, matrix_low, (((1,), (1,)), ((), ()))
            )
            out_ref[...] += split_dot(
                back[:, row : row + rows], matrix_high, matrix_low, (((1,), (0,)), ((), ()))
            )
        return carry

    lax.fori_loop(0, shift_count, body, 0)


def m2l(table, window_index, base, windows, vectors):
    shift_count = table.shape[0] // 4
    points = windows.shape[-1]
    return pl.pallas_call(
        functools.partial(m2l_kernel, shift_count, 128),
        out_shape=jax.ShapeDtypeStruct((vectors, points), jnp.float32),
        in_specs=[
            pl.BlockSpec(memory_space=pltpu.SMEM),
            pl.BlockSpec(memory_space=pltpu.SMEM),
            pl.BlockSpec(memory_space=pltpu.VMEM),
            pl.BlockSpec(memory_space=pltpu.VMEM),
        ],
        out_specs=pl.BlockSpec(memory_space=pltpu.VMEM),
        compiler_params=pltpu.CompilerParams(vmem_limit_bytes=48 * 1024 * 1024),
        cost_estimate=pl.CostEstimate(
            flops=12 * shift_count * vectors * points * points + 14 * shift_count * points * points,
            transcendentals=shift_count * points * points,
            bytes_accessed=4 * (windows.size + base.size + vectors * points),
        ),
    )(table, window_index, base, windows)


def far_shifts(span):
    shifts = []
    for dx in range(-span, span + 1):
        for dy in range(-span, span + 1):
            for dz in range(-span, span + 1):
                if max(abs(dx), abs(dy), abs(dz)) >= 2 and (dx, dy, dz) > (0, 0, 0):
                    shifts.append((dx, dy, dz))
    return shifts


def shards(offsets, charges, counts, c2e_leaf_up, c2e_leaf_down, c2e_top_up, c2e_top_down):
    slot_count = offsets.shape[-1]
    layers = offsets.shape[3]
    parent_layers = layers // 2
    points = c2e_leaf_up.shape[0]
    unit_sphere = sphere(points)
    slot_index = jnp.arange(slot_count)
    weights = jnp.where(slot_index < counts[..., None], charges, 0.0)
    packed = jnp.concatenate([offsets, weights[None]], axis=0)
    leaf_check_pts = 0.5 + 1.8 * unit_sphere
    leaf_check = point_sum(leaf_check_pts[:, None, None, None, :], offsets, weights)
    leaf_eq = jnp.einsum("ec,xyzc->xyze", c2e_leaf_up, leaf_check, precision=highest)
    children = child_points(unit_sphere)
    parent_weights = (
        leaf_eq.reshape(2, 2, parent_layers, 2, points)
        .transpose(2, 0, 1, 3, 4)
        .reshape(parent_layers, 8 * points)
    )
    parent_check_pts = 1.0 + 3.6 * unit_sphere
    parent_check = point_sum(parent_check_pts[:, None, :], children[:, None, :], parent_weights)
    parent_eq = jnp.einsum("ec,mc->me", c2e_top_up, parent_check, precision=highest)
    count_x = lax.axis_size("gx")
    count_y = lax.axis_size("gy")

    packed_x, eq_x, right_eq = exchange(
        [(packed, 1, 1), (leaf_eq, 0, 2)], "gx", rider=parent_eq
    )
    beside_all, cycle = exchange([(packed_x, 2, 1), (eq_x, 1, 2)], "gy")
    pair = jnp.stack([parent_eq, right_eq])[:, None]
    if count_x == 1:
        pair = parent_eq[None, None]
    gathered = rel_gather(rel_gather(pair, "gx", 0, min(2, count_x)), "gy", 1)
    kept = []
    for rel_x in range(count_x):
        for rel_y in range(count_y):
            off_x = (rel_x + count_x // 2) % count_x - count_x // 2
            off_y = (rel_y + count_y // 2) % count_y - count_y // 2
            if abs(off_x) > 1 or abs(off_y) > 1:
                kept.append((rel_x * count_y + rel_y, off_x, off_y))
    kept_index = np.array([k[0] for k in kept], np.int32)
    kept_x = np.array([2.0 * k[1] for k in kept], np.float32)
    kept_y = np.array([2.0 * k[2] for k in kept], np.float32)
    far_sources = jnp.take(gathered.reshape(count_x * count_y, parent_layers, points), kept_index, axis=0)
    layer_float = jnp.arange(parent_layers).astype(jnp.float32)
    depth_pairs = 2.0 * (layer_float[None, :] - layer_float[:, None])
    far_shape = (parent_layers, len(kept), parent_layers, points)
    source_pts = jnp.stack(
        [
            jnp.broadcast_to(kept_x[None, :, None, None] + 1.8 * unit_sphere[0], far_shape),
            jnp.broadcast_to(kept_y[None, :, None, None] + 1.8 * unit_sphere[1], far_shape),
            jnp.broadcast_to(depth_pairs[:, None, :, None] + 1.8 * unit_sphere[2], far_shape),
        ]
    ).reshape(3, parent_layers, -1)
    check_far = 1.8 * unit_sphere
    check_square = jnp.sum(check_far * check_far, axis=0)
    source_square, source_scaled = lax.optimization_barrier(
        (jnp.sum(source_pts * source_pts, axis=0) + softening_sq, -2.0 * source_pts)
    )
    far_square = (
        (check_square[:, None] + source_square[:, None, :])
        + check_far[0][:, None] * source_scaled[0][:, None, :]
        + check_far[1][:, None] * source_scaled[1][:, None, :]
        + check_far[2][:, None] * source_scaled[2][:, None, :]
    )
    far_check = jnp.sum(lax.rsqrt(far_square) * far_sources.reshape(-1), axis=-1)

    framed = jnp.pad(cycle, ((1, 1), (1, 1), (3, 3), (0, 0)))
    shifts = far_shifts(3)
    depth_windows = jnp.stack(
        [framed[:, :, depth : depth + layers] for depth in range(7)], axis=2
    ).reshape(-1, layers, points)
    window_index = np.array(
        [
            np.ravel_multi_index(
                (ix + sign * dx + 3, iy + sign * dy + 3, sign * dz + 3), framed.shape[:2] + (7,)
            )
            for sign in (1, -1)
            for dx, dy, dz in shifts
            for ix in range(2)
            for iy in range(2)
        ],
        np.int32,
    )
    base = jnp.stack(
        [0.9 * (unit_sphere[i][:, None] - unit_sphere[i][None, :]) for i in range(3)]
    )
    base = jnp.concatenate([base, jnp.sum(base * base, axis=0)[None]], axis=0)
    shift_array = np.array(shifts, np.float64)
    table = np.concatenate(
        [-2.0 * shift_array, (shift_array**2).sum(1, keepdims=True) + softening_sq], axis=1
    )
    table = jnp.asarray(table.astype(np.float32).reshape(-1))
    leaf_down_check = m2l(table, jnp.asarray(window_index), base, depth_windows, 4 * layers).reshape(
        2, 2, layers, points
    )
    parent_local = jnp.einsum("ec,mc->me", c2e_top_down, far_check, precision=highest)
    leaf_local = jnp.einsum("ec,xyzc->xyze", c2e_leaf_down, leaf_down_check, precision=highest)

    padded_around = jnp.pad(beside_all, ((0, 0), (0, 0), (0, 0), (1, 1), (0, 0)))
    around_shape = padded_around.shape[1:4]
    moves = [(mx, my, mz) for mx in (-1, 0, 1) for my in (-1, 0, 1) for mz in (-1, 0, 1)]
    box_rows = np.array(
        [
            [
                np.ravel_multi_index((bx + 1 + mx, by + 1 + my, bz + 1 + mz), around_shape)
                for bx in range(2)
                for by in range(2)
                for bz in range(layers)
            ]
            for mx, my, mz in moves
        ],
        np.int32,
    )
    source = jnp.take(
        padded_around.reshape(4, -1, slot_count), box_rows, axis=1
    ).reshape(4, len(moves), 2, 2, layers, slot_count)
    source = source.reshape(4, len(moves), 4 * layers, slot_count).transpose(0, 2, 1, 3)
    source = source.reshape(4, 4 * layers, len(moves) * slot_count)
    move = np.repeat(np.array(moves, np.float32), slot_count, axis=0)
    own = packed.reshape(4, 4 * layers, slot_count)
    placed = lax.optimization_barrier(source[:3] + move.T[:, None, :])
    delta_x = own[0][..., :, None] - placed[0][..., None, :]
    delta_y = own[1][..., :, None] - placed[1][..., None, :]
    delta_z = own[2][..., :, None] - placed[2][..., None, :]
    kernel = lax.rsqrt(delta_x * delta_x + delta_y * delta_y + delta_z * delta_z + softening_sq)
    itself = lax.rsqrt(jnp.full((), softening_sq, jnp.float32)) * own[3]
    near = (jnp.sum(kernel * source[3][..., None, :], axis=-1) - itself).reshape(
        2, 2, layers, slot_count
    )

    leaf_down_pts = 0.5 + 1.8 * unit_sphere
    leaf_far = point_sum(offsets, leaf_down_pts[:, None, None, None, :], leaf_local)
    parent_down_pts = 1.0 + 3.6 * unit_sphere
    local_float = jnp.arange(2).astype(jnp.float32)
    layer_parity = (jnp.arange(layers) % 2).astype(jnp.float32)
    in_parent = jnp.stack(
        [
            local_float[:, None, None, None] + offsets[0],
            local_float[None, :, None, None] + offsets[1],
            layer_parity[None, None, :, None] + offsets[2],
        ]
    )
    spread_local = jnp.repeat(parent_local, 2, axis=0)[None, None]
    parent_far = point_sum(in_parent, parent_down_pts[:, None, None, None, :], spread_local)
    total = near + leaf_far + parent_far
    return jnp.where(slot_index < counts[..., None], total, 0.0)


def solution(mesh):
    return jax.shard_map(
        shards,
        mesh=mesh,
        in_specs=(
            P(None, "gx", "gy", None, None),
            P("gx", "gy", None, None),
            P("gx", "gy", None),
            P(),
            P(),
            P(),
            P(),
        ),
        out_specs=P("gx", "gy", None, None),
        check_vma=False,
    )
```

```python
import functools

import jax
import numpy as np
import jax.numpy as jnp
from jax import lax
from jax.experimental import pallas as pl
from jax.experimental.pallas import tpu as pltpu
from jax.sharding import PartitionSpec as P

softening_sq = 0.0004
golden_turn = 2.399963229728653
highest = lax.Precision.HIGHEST


def sphere(point_count):
    middle = jnp.arange(point_count).astype(jnp.float32) + 0.5
    height = 1.0 - 2.0 * middle / point_count
    radial = jnp.sqrt(jnp.maximum(1.0 - height * height, 0.0))
    angle_turn = middle * golden_turn
    return jnp.stack([radial * jnp.cos(angle_turn), radial * jnp.sin(angle_turn), height])


def point_sum(targets, sources, weights):
    delta_x = targets[0][..., :, None] - sources[0][..., None, :]
    delta_y = targets[1][..., :, None] - sources[1][..., None, :]
    delta_z = targets[2][..., :, None] - sources[2][..., None, :]
    kernel = lax.rsqrt(delta_x * delta_x + delta_y * delta_y + delta_z * delta_z + softening_sq)
    return jnp.sum(kernel * weights[..., None, :], axis=-1)


def translation(unit_sphere, shift_x, shift_y, shift_z, radius):
    delta_x = (
        radius * (unit_sphere[0][:, None] - unit_sphere[0][None, :]) - shift_x[..., None, None]
    )
    delta_y = (
        radius * (unit_sphere[1][:, None] - unit_sphere[1][None, :]) - shift_y[..., None, None]
    )
    delta_z = (
        radius * (unit_sphere[2][:, None] - unit_sphere[2][None, :]) - shift_z[..., None, None]
    )
    return lax.rsqrt(delta_x * delta_x + delta_y * delta_y + delta_z * delta_z + softening_sq)


def child_points(unit_sphere):
    centre = jnp.arange(2).astype(jnp.float32) + 0.5
    point_count = unit_sphere.shape[1]
    box_shape = (2, 2, 2, point_count)
    along_x = jnp.broadcast_to(centre[:, None, None, None] + 0.9 * unit_sphere[0], box_shape)
    along_y = jnp.broadcast_to(centre[None, :, None, None] + 0.9 * unit_sphere[1], box_shape)
    along_z = jnp.broadcast_to(centre[None, None, :, None] + 0.9 * unit_sphere[2], box_shape)
    return jnp.stack([along_x, along_y, along_z]).reshape(3, 8 * point_count)


def rel_gather(buf, axis, dim, have=1):
    count = lax.axis_size(axis)
    while have < count:
        step = min(have, count - have)
        part = lax.slice_in_dim(buf, 0, step, axis=dim)
        got = lax.ppermute(part, axis, [(j, (j - have) % count) for j in range(count)])
        buf = jnp.concatenate([buf, got], axis=dim)
        have += step
    return buf


def exchange(items, axis, rider=None):
    count = lax.axis_size(axis)
    heads, tails = [], []
    for cells, dim, width in items:
        heads.append(lax.slice_in_dim(cells, 0, width, axis=dim))
        tails.append(lax.slice_in_dim(cells, cells.shape[dim] - width, cells.shape[dim], axis=dim))
    sent_tail = jnp.concatenate([t.reshape(-1) for t in tails])
    sent_head = jnp.concatenate(
        [h.reshape(-1) for h in heads] + ([] if rider is None else [rider.reshape(-1)])
    )
    from_left = lax.ppermute(sent_tail, axis, [(i, (i + 1) % count) for i in range(count)])
    from_right = lax.ppermute(sent_head, axis, [((i + 1) % count, i) for i in range(count)])
    out, start = [], 0
    for (cells, dim, width), head, tail in zip(items, heads, tails):
        size = head.size
        before = from_left[start : start + size].reshape(tail.shape)
        after = from_right[start : start + size].reshape(head.shape)
        out.append(jnp.concatenate([before, cells, after], axis=dim))
        start += size
    if rider is not None:
        out.append(from_right[start:].reshape(rider.shape))
    return out


def split_top(values):
    scaled = values * 65537.0
    return scaled - (scaled - values)


def m2l_kernel(shift_count, rows, table_ref, index_ref, base_ref, windows_ref, out_ref, turned_ref):
    out_ref[...] = jnp.zeros_like(out_ref)
    turned_ref[...] = jnp.zeros_like(turned_ref)
    vectors = out_ref.shape[0]
    pieces = index_ref.shape[0] // (2 * shift_count)

    def split_dot(left, matrix_high, matrix_low, dims):
        both = lax.dot_general(left, matrix_high, dims, preferred_element_type=jnp.float32)
        cross = lax.dot_general(
            left[:vectors], matrix_low, dims, preferred_element_type=jnp.float32
        )
        return both[:vectors] + both[vectors:] + cross

    def gathered(sign, index):
        first = (sign * shift_count + index) * pieces
        block = jnp.concatenate(
            [windows_ref[index_ref[first + piece]] for piece in range(pieces)], axis=0
        )
        top = split_top(block)
        return jnp.concatenate([top, block - top], axis=0).astype(jnp.bfloat16)

    def body(index, carry):
        scale_x = table_ref[4 * index]
        scale_y = table_ref[4 * index + 1]
        scale_z = table_ref[4 * index + 2]
        offset = table_ref[4 * index + 3]
        fwd = gathered(0, index)
        back = gathered(1, index)
        for row in range(0, base_ref.shape[1], rows):
            square = (
                (base_ref[3, row : row + rows, :] + offset)
                + scale_x * base_ref[0, row : row + rows, :]
                + scale_y * base_ref[1, row : row + rows, :]
                + scale_z * base_ref[2, row : row + rows, :]
            )
            matrix = lax.rsqrt(square)
            matrix_top = split_top(matrix)
            matrix_high = matrix_top.astype(jnp.bfloat16)
            matrix_low = (matrix - matrix_top).astype(jnp.bfloat16)
            both = lax.dot_general(
                matrix_high, fwd, (((1,), (1,)), ((), ())), preferred_element_type=jnp.float32
            )
            cross = lax.dot_general(
                matrix_low, fwd[:vectors], (((1,), (1,)), ((), ())),
                preferred_element_type=jnp.float32,
            )
            turned_ref[row : row + rows, :] += both[:, :vectors] + both[:, vectors:] + cross
            out_ref[...] += split_dot(
                back[:, row : row + rows], matrix_high, matrix_low, (((1,), (0,)), ((), ()))
            )
        return carry

    lax.fori_loop(0, shift_count, body, 0)
    out_ref[...] += turned_ref[...].T


def m2l(table, window_index, base, windows, vectors):
    shift_count = table.shape[0] // 4
    points = windows.shape[-1]
    return pl.pallas_call(
        functools.partial(m2l_kernel, shift_count, 128),
        out_shape=jax.ShapeDtypeStruct((vectors, points), jnp.float32),
        in_specs=[
            pl.BlockSpec(memory_space=pltpu.SMEM),
            pl.BlockSpec(memory_space=pltpu.SMEM),
            pl.BlockSpec(memory_space=pltpu.VMEM),
            pl.BlockSpec(memory_space=pltpu.VMEM),
        ],
        out_specs=pl.BlockSpec(memory_space=pltpu.VMEM),
        scratch_shapes=[pltpu.VMEM((points, vectors), jnp.float32)],
        compiler_params=pltpu.CompilerParams(vmem_limit_bytes=48 * 1024 * 1024),
        cost_estimate=pl.CostEstimate(
            flops=12 * shift_count * vectors * points * points + 14 * shift_count * points * points,
            transcendentals=shift_count * points * points,
            bytes_accessed=4 * (windows.size + base.size + vectors * points),
        ),
    )(table, window_index, base, windows)


def far_shifts(span):
    shifts = []
    for dx in range(-span, span + 1):
        for dy in range(-span, span + 1):
            for dz in range(-span, span + 1):
                if max(abs(dx), abs(dy), abs(dz)) >= 2 and (dx, dy, dz) > (0, 0, 0):
                    shifts.append((dx, dy, dz))
    return shifts


def shards(offsets, charges, counts, c2e_leaf_up, c2e_leaf_down, c2e_top_up, c2e_top_down):
    slot_count = offsets.shape[-1]
    layers = offsets.shape[3]
    parent_layers = layers // 2
    points = c2e_leaf_up.shape[0]
    unit_sphere = sphere(points)
    slot_index = jnp.arange(slot_count)
    weights = jnp.where(slot_index < counts[..., None], charges, 0.0)
    packed = jnp.concatenate([offsets, weights[None]], axis=0)
    leaf_check_pts = 0.5 + 1.8 * unit_sphere
    leaf_check = point_sum(leaf_check_pts[:, None, None, None, :], offsets, weights)
    leaf_eq = jnp.einsum("ec,xyzc->xyze", c2e_leaf_up, leaf_check, precision=highest)
    children = child_points(unit_sphere)
    parent_weights = (
        leaf_eq.reshape(2, 2, parent_layers, 2, points)
        .transpose(2, 0, 1, 3, 4)
        .reshape(parent_layers, 8 * points)
    )
    parent_check_pts = 1.0 + 3.6 * unit_sphere
    parent_check = point_sum(parent_check_pts[:, None, :], children[:, None, :], parent_weights)
    parent_eq = jnp.einsum("ec,mc->me", c2e_top_up, parent_check, precision=highest)
    count_x = lax.axis_size("gx")
    count_y = lax.axis_size("gy")

    packed_x, eq_x, right_eq = exchange(
        [(packed, 1, 1), (leaf_eq, 0, 2)], "gx", rider=parent_eq
    )
    beside_all, cycle = exchange([(packed_x, 2, 1), (eq_x, 1, 2)], "gy")
    pair = jnp.stack([parent_eq, right_eq])[:, None]
    if count_x == 1:
        pair = parent_eq[None, None]
    gathered = rel_gather(rel_gather(pair, "gx", 0, min(2, count_x)), "gy", 1)
    kept = []
    for rel_x in range(count_x):
        for rel_y in range(count_y):
            off_x = (rel_x + count_x // 2) % count_x - count_x // 2
            off_y = (rel_y + count_y // 2) % count_y - count_y // 2
            if abs(off_x) > 1 or abs(off_y) > 1:
                kept.append((rel_x * count_y + rel_y, off_x, off_y))
    kept_index = np.array([k[0] for k in kept], np.int32)
    kept_x = np.array([2.0 * k[1] for k in kept], np.float32)
    kept_y = np.array([2.0 * k[2] for k in kept], np.float32)
    far_sources = jnp.take(gathered.reshape(count_x * count_y, parent_layers, points), kept_index, axis=0)
    layer_float = jnp.arange(parent_layers).astype(jnp.float32)
    depth_pairs = 2.0 * (layer_float[None, :] - layer_float[:, None])
    far_shape = (parent_layers, len(kept), parent_layers, points)
    source_pts = jnp.stack(
        [
            jnp.broadcast_to(kept_x[None, :, None, None] + 1.8 * unit_sphere[0], far_shape),
            jnp.broadcast_to(kept_y[None, :, None, None] + 1.8 * unit_sphere[1], far_shape),
            jnp.broadcast_to(depth_pairs[:, None, :, None] + 1.8 * unit_sphere[2], far_shape),
        ]
    ).reshape(3, parent_layers, -1)
    far_check = point_sum(
        jnp.broadcast_to(1.8 * unit_sphere[:, None, :], (3, parent_layers, points)),
        source_pts,
        far_sources.reshape(-1),
    )

    framed = jnp.pad(cycle, ((1, 1), (1, 1), (3, 3), (0, 0)))
    shifts = far_shifts(3)
    depth_windows = jnp.stack(
        [framed[:, :, depth : depth + layers] for depth in range(7)], axis=2
    ).reshape(-1, layers, points)
    window_index = np.array(
        [
            np.ravel_multi_index(
                (ix + sign * dx + 3, iy + sign * dy + 3, sign * dz + 3), framed.shape[:2] + (7,)
            )
            for sign in (1, -1)
            for dx, dy, dz in shifts
            for ix in range(2)
            for iy in range(2)
        ],
        np.int32,
    )
    base = jnp.stack(
        [0.9 * (unit_sphere[i][:, None] - unit_sphere[i][None, :]) for i in range(3)]
    )
    base = jnp.concatenate([base, jnp.sum(base * base, axis=0)[None]], axis=0)
    shift_array = np.array(shifts, np.float64)
    table = np.concatenate(
        [-2.0 * shift_array, (shift_array**2).sum(1, keepdims=True) + softening_sq], axis=1
    )
    table = jnp.asarray(table.astype(np.float32).reshape(-1))
    leaf_down_check = m2l(table, jnp.asarray(window_index), base, depth_windows, 4 * layers).reshape(
        2, 2, layers, points
    )
    parent_local = jnp.einsum("ec,mc->me", c2e_top_down, far_check, precision=highest)
    leaf_local = jnp.einsum("ec,xyzc->xyze", c2e_leaf_down, leaf_down_check, precision=highest)

    padded_around = jnp.pad(beside_all, ((0, 0), (0, 0), (0, 0), (1, 1), (0, 0)))
    around_shape = padded_around.shape[1:4]
    moves = [(mx, my, mz) for mx in (-1, 0, 1) for my in (-1, 0, 1) for mz in (-1, 0, 1)]
    box_rows = np.array(
        [
            [
                np.ravel_multi_index((bx + 1 + mx, by + 1 + my, bz + 1 + mz), around_shape)
                for bx in range(2)
                for by in range(2)
                for bz in range(layers)
            ]
            for mx, my, mz in moves
        ],
        np.int32,
    )
    source = jnp.take(
        padded_around.reshape(4, -1, slot_count), box_rows, axis=1
    ).reshape(4, len(moves), 2, 2, layers, slot_count)
    source = source.reshape(4, len(moves), 4 * layers, slot_count).transpose(0, 2, 1, 3)
    source = source.reshape(4, 4 * layers, len(moves) * slot_count)
    move = np.repeat(np.array(moves, np.float32), slot_count, axis=0)
    own = packed.reshape(4, 4 * layers, slot_count)
    placed = lax.optimization_barrier(source[:3] + move.T[:, None, :])
    delta_x = own[0][..., :, None] - placed[0][..., None, :]
    delta_y = own[1][..., :, None] - placed[1][..., None, :]
    delta_z = own[2][..., :, None] - placed[2][..., None, :]
    kernel = lax.rsqrt(delta_x * delta_x + delta_y * delta_y + delta_z * delta_z + softening_sq)
    itself = lax.rsqrt(jnp.full((), softening_sq, jnp.float32)) * own[3]
    near = (jnp.sum(kernel * source[3][..., None, :], axis=-1) - itself).reshape(
        2, 2, layers, slot_count
    )

    leaf_down_pts = 0.5 + 1.8 * unit_sphere
    leaf_far = point_sum(offsets, leaf_down_pts[:, None, None, None, :], leaf_local)
    parent_down_pts = 1.0 + 3.6 * unit_sphere
    local_float = jnp.arange(2).astype(jnp.float32)
    layer_parity = (jnp.arange(layers) % 2).astype(jnp.float32)
    in_parent = jnp.stack(
        [
            local_float[:, None, None, None] + offsets[0],
            local_float[None, :, None, None] + offsets[1],
            layer_parity[None, None, :, None] + offsets[2],
        ]
    )
    spread_local = jnp.repeat(parent_local, 2, axis=0)[None, None]
    parent_far = point_sum(in_parent, parent_down_pts[:, None, None, None, :], spread_local)
    total = near + leaf_far + parent_far
    return jnp.where(slot_index < counts[..., None], total, 0.0)


def solution(mesh):
    return jax.shard_map(
        shards,
        mesh=mesh,
        in_specs=(
            P(None, "gx", "gy", None, None),
            P("gx", "gy", None, None),
            P("gx", "gy", None),
            P(),
            P(),
            P(),
            P(),
        ),
        out_specs=P("gx", "gy", None, None),
        check_vma=False,
    )
```

```python
import functools

import jax
import numpy as np
import jax.numpy as jnp
from jax import lax
from jax.experimental import pallas as pl
from jax.experimental.pallas import tpu as pltpu
from jax.sharding import PartitionSpec as P

softening_sq = 0.0004
golden_turn = 2.399963229728653
highest = lax.Precision.HIGHEST


def sphere(point_count):
    middle = jnp.arange(point_count).astype(jnp.float32) + 0.5
    height = 1.0 - 2.0 * middle / point_count
    radial = jnp.sqrt(jnp.maximum(1.0 - height * height, 0.0))
    angle_turn = middle * golden_turn
    return jnp.stack([radial * jnp.cos(angle_turn), radial * jnp.sin(angle_turn), height])


def point_sum(targets, sources, weights):
    delta_x = targets[0][..., :, None] - sources[0][..., None, :]
    delta_y = targets[1][..., :, None] - sources[1][..., None, :]
    delta_z = targets[2][..., :, None] - sources[2][..., None, :]
    kernel = lax.rsqrt(delta_x * delta_x + delta_y * delta_y + delta_z * delta_z + softening_sq)
    return jnp.sum(kernel * weights[..., None, :], axis=-1)


def translation(unit_sphere, shift_x, shift_y, shift_z, radius):
    delta_x = (
        radius * (unit_sphere[0][:, None] - unit_sphere[0][None, :]) - shift_x[..., None, None]
    )
    delta_y = (
        radius * (unit_sphere[1][:, None] - unit_sphere[1][None, :]) - shift_y[..., None, None]
    )
    delta_z = (
        radius * (unit_sphere[2][:, None] - unit_sphere[2][None, :]) - shift_z[..., None, None]
    )
    return lax.rsqrt(delta_x * delta_x + delta_y * delta_y + delta_z * delta_z + softening_sq)


def child_points(unit_sphere):
    centre = jnp.arange(2).astype(jnp.float32) + 0.5
    point_count = unit_sphere.shape[1]
    box_shape = (2, 2, 2, point_count)
    along_x = jnp.broadcast_to(centre[:, None, None, None] + 0.9 * unit_sphere[0], box_shape)
    along_y = jnp.broadcast_to(centre[None, :, None, None] + 0.9 * unit_sphere[1], box_shape)
    along_z = jnp.broadcast_to(centre[None, None, :, None] + 0.9 * unit_sphere[2], box_shape)
    return jnp.stack([along_x, along_y, along_z]).reshape(3, 8 * point_count)


def rel_gather(buf, axis, dim, have=1):
    count = lax.axis_size(axis)
    while have < count:
        step = min(have, count - have)
        part = lax.slice_in_dim(buf, 0, step, axis=dim)
        got = lax.ppermute(part, axis, [(j, (j - have) % count) for j in range(count)])
        buf = jnp.concatenate([buf, got], axis=dim)
        have += step
    return buf


def exchange(items, axis, rider=None):
    count = lax.axis_size(axis)
    heads, tails = [], []
    for cells, dim, width in items:
        heads.append(lax.slice_in_dim(cells, 0, width, axis=dim))
        tails.append(lax.slice_in_dim(cells, cells.shape[dim] - width, cells.shape[dim], axis=dim))
    sent_tail = jnp.concatenate([t.reshape(-1) for t in tails])
    sent_head = jnp.concatenate(
        [h.reshape(-1) for h in heads] + ([] if rider is None else [rider.reshape(-1)])
    )
    from_left = lax.ppermute(sent_tail, axis, [(i, (i + 1) % count) for i in range(count)])
    from_right = lax.ppermute(sent_head, axis, [((i + 1) % count, i) for i in range(count)])
    out, start = [], 0
    for (cells, dim, width), head, tail in zip(items, heads, tails):
        size = head.size
        before = from_left[start : start + size].reshape(tail.shape)
        after = from_right[start : start + size].reshape(head.shape)
        out.append(jnp.concatenate([before, cells, after], axis=dim))
        start += size
    if rider is not None:
        out.append(from_right[start:].reshape(rider.shape))
    return out


def split_top(values):
    scaled = values * 65537.0
    return scaled - (scaled - values)


def m2l_kernel(shift_count, rows, table_ref, index_ref, base_ref, windows_ref, out_ref):
    out_ref[...] = jnp.zeros_like(out_ref)
    vectors = out_ref.shape[0]
    pieces = index_ref.shape[0] // (2 * shift_count)

    def split_dot(left, matrix_high, matrix_low, dims):
        both = lax.dot_general(left, matrix_high, dims, preferred_element_type=jnp.float32)
        cross = lax.dot_general(
            left[:vectors], matrix_low, dims, preferred_element_type=jnp.float32
        )
        return both[:vectors] + both[vectors:] + cross

    def gathered(sign, index):
        first = (sign * shift_count + index) * pieces
        block = jnp.concatenate(
            [windows_ref[index_ref[first + piece]] for piece in range(pieces)], axis=0
        )
        top = split_top(block)
        return jnp.concatenate([top, block - top], axis=0).astype(jnp.bfloat16)

    def body(index, carry):
        scale_x = table_ref[4 * index]
        scale_y = table_ref[4 * index + 1]
        scale_z = table_ref[4 * index + 2]
        offset = table_ref[4 * index + 3]
        fwd = gathered(0, index)
        back = gathered(1, index)
        for row in range(0, base_ref.shape[1], rows):
            square = (
                (base_ref[3, row : row + rows, :] + offset)
                + scale_x * base_ref[0, row : row + rows, :]
                + scale_y * base_ref[1, row : row + rows, :]
                + scale_z * base_ref[2, row : row + rows, :]
            )
            matrix = lax.rsqrt(square)
            matrix_top = split_top(matrix)
            matrix_high = matrix_top.astype(jnp.bfloat16)
            matrix_low = (matrix - matrix_top).astype(jnp.bfloat16)
            out_ref[:, row : row + rows] += split_dot(
                fwd, matrix_high, matrix_low, (((1,), (1,)), ((), ()))
            )
            out_ref[...] += split_dot(
                back[:, row : row + rows], matrix_high, matrix_low, (((1,), (0,)), ((), ()))
            )
        return carry

    lax.fori_loop(0, shift_count, body, 0)


def m2l(table, window_index, base, windows, vectors):
    shift_count = table.shape[0] // 4
    points = windows.shape[-1]
    return pl.pallas_call(
        functools.partial(m2l_kernel, shift_count, 128),
        out_shape=jax.ShapeDtypeStruct((vectors, points), jnp.float32),
        in_specs=[
            pl.BlockSpec(memory_space=pltpu.SMEM),
            pl.BlockSpec(memory_space=pltpu.SMEM),
            pl.BlockSpec(memory_space=pltpu.VMEM),
            pl.BlockSpec(memory_space=pltpu.VMEM),
        ],
        out_specs=pl.BlockSpec(memory_space=pltpu.VMEM),
        compiler_params=pltpu.CompilerParams(vmem_limit_bytes=48 * 1024 * 1024),
        cost_estimate=pl.CostEstimate(
            flops=12 * shift_count * vectors * points * points + 14 * shift_count * points * points,
            transcendentals=shift_count * points * points,
            bytes_accessed=4 * (windows.size + base.size + vectors * points),
        ),
    )(table, window_index, base, windows)


def far_shifts(span):
    shifts = []
    for dx in range(-span, span + 1):
        for dy in range(-span, span + 1):
            for dz in range(-span, span + 1):
                if max(abs(dx), abs(dy), abs(dz)) >= 2 and (dx, dy, dz) > (0, 0, 0):
                    shifts.append((dx, dy, dz))
    return shifts


def shards(offsets, charges, counts, c2e_leaf_up, c2e_leaf_down, c2e_top_up, c2e_top_down):
    slot_count = offsets.shape[-1]
    layers = offsets.shape[3]
    parent_layers = layers // 2
    points = c2e_leaf_up.shape[0]
    unit_sphere = sphere(points)
    slot_index = jnp.arange(slot_count)
    weights = jnp.where(slot_index < counts[..., None], charges, 0.0)
    packed = jnp.concatenate([offsets, weights[None]], axis=0)
    leaf_check_pts = 0.5 + 1.8 * unit_sphere
    leaf_check = point_sum(leaf_check_pts[:, None, None, None, :], offsets, weights)
    leaf_eq = jnp.einsum("ec,xyzc->xyze", c2e_leaf_up, leaf_check, precision=highest)
    children = child_points(unit_sphere)
    parent_weights = (
        leaf_eq.reshape(2, 2, parent_layers, 2, points)
        .transpose(2, 0, 1, 3, 4)
        .reshape(parent_layers, 8 * points)
    )
    parent_check_pts = 1.0 + 3.6 * unit_sphere
    parent_check = point_sum(parent_check_pts[:, None, :], children[:, None, :], parent_weights)
    parent_eq = jnp.einsum("ec,mc->me", c2e_top_up, parent_check, precision=highest)
    count_x = lax.axis_size("gx")
    count_y = lax.axis_size("gy")

    packed_x, eq_x, right_eq = exchange(
        [(packed, 1, 1), (leaf_eq, 0, 2)], "gx", rider=parent_eq
    )
    beside_all, cycle = exchange([(packed_x, 2, 1), (eq_x, 1, 2)], "gy")
    pair = jnp.stack([parent_eq, right_eq])[:, None]
    if count_x == 1:
        pair = parent_eq[None, None]
    gathered = rel_gather(rel_gather(pair, "gx", 0, min(2, count_x)), "gy", 1)
    kept = []
    for rel_x in range(count_x):
        for rel_y in range(count_y):
            off_x = (rel_x + count_x // 2) % count_x - count_x // 2
            off_y = (rel_y + count_y // 2) % count_y - count_y // 2
            if abs(off_x) > 1 or abs(off_y) > 1:
                kept.append((rel_x * count_y + rel_y, off_x, off_y))
    kept_index = np.array([k[0] for k in kept], np.int32)
    kept_x = np.array([2.0 * k[1] for k in kept], np.float32)
    kept_y = np.array([2.0 * k[2] for k in kept], np.float32)
    far_sources = jnp.take(gathered.reshape(count_x * count_y, parent_layers, points), kept_index, axis=0)
    layer_float = jnp.arange(parent_layers).astype(jnp.float32)
    depth_pairs = 2.0 * (layer_float[None, :] - layer_float[:, None])
    far_shape = (parent_layers, len(kept), parent_layers, points)
    source_pts = jnp.stack(
        [
            jnp.broadcast_to(kept_x[None, :, None, None] + 1.8 * unit_sphere[0], far_shape),
            jnp.broadcast_to(kept_y[None, :, None, None] + 1.8 * unit_sphere[1], far_shape),
            jnp.broadcast_to(depth_pairs[:, None, :, None] + 1.8 * unit_sphere[2], far_shape),
        ]
    ).reshape(3, parent_layers, -1)
    far_check = point_sum(
        jnp.broadcast_to(1.8 * unit_sphere[:, None, :], (3, parent_layers, points)),
        source_pts,
        far_sources.reshape(-1),
    )

    framed = jnp.pad(cycle, ((1, 1), (1, 1), (3, 3), (0, 0)))
    shifts = far_shifts(3)
    depth_windows = jnp.stack(
        [framed[:, :, depth : depth + layers] for depth in range(7)], axis=2
    ).reshape(-1, layers, points)
    window_index = np.array(
        [
            np.ravel_multi_index(
                (ix + sign * dx + 3, iy + sign * dy + 3, sign * dz + 3), framed.shape[:2] + (7,)
            )
            for sign in (1, -1)
            for dx, dy, dz in shifts
            for ix in range(2)
            for iy in range(2)
        ],
        np.int32,
    )
    base = jnp.stack(
        [0.9 * (unit_sphere[i][:, None] - unit_sphere[i][None, :]) for i in range(3)]
    )
    base = jnp.concatenate([base, jnp.sum(base * base, axis=0)[None]], axis=0)
    shift_array = np.array(shifts, np.float64)
    table = np.concatenate(
        [-2.0 * shift_array, (shift_array**2).sum(1, keepdims=True) + softening_sq], axis=1
    )
    table = jnp.asarray(table.astype(np.float32).reshape(-1))
    leaf_down_check = m2l(table, jnp.asarray(window_index), base, depth_windows, 4 * layers).reshape(
        2, 2, layers, points
    )
    parent_local = jnp.einsum("ec,mc->me", c2e_top_down, far_check, precision=highest)
    leaf_local = jnp.einsum("ec,xyzc->xyze", c2e_leaf_down, leaf_down_check, precision=highest)

    padded_around = jnp.pad(beside_all, ((0, 0), (0, 0), (0, 0), (1, 1), (0, 0)))
    around_shape = padded_around.shape[1:4]
    targets = [(bx, by, bz) for bx in range(2) for by in range(2) for bz in range(layers)]

    def neighbour_moves(bz):
        return [
            (mx, my, mz)
            for mx in (-1, 0, 1)
            for my in (-1, 0, 1)
            for mz in (-1, 0, 1)
            if 0 <= bz + mz < layers
        ]

    groups = {}
    for index, (bx, by, bz) in enumerate(targets):
        groups.setdefault(len(neighbour_moves(bz)), []).append(index)
    own = packed.reshape(4, 4 * layers, slot_count)
    around_rows = padded_around.reshape(4, -1, slot_count)
    self_term = lax.rsqrt(jnp.full((), softening_sq, jnp.float32))
    near_parts, order = [], []
    for members in groups.values():
        rows = np.array(
            [
                [
                    np.ravel_multi_index(
                        (targets[t][0] + 1 + mx, targets[t][1] + 1 + my, targets[t][2] + 1 + mz),
                        around_shape,
                    )
                    for mx, my, mz in neighbour_moves(targets[t][2])
                ]
                for t in members
            ],
            np.int32,
        )
        move = np.stack(
            [
                np.repeat(np.array(neighbour_moves(targets[t][2]), np.float32), slot_count, axis=0).T
                for t in members
            ],
            axis=1,
        )
        source = jnp.take(around_rows, rows.reshape(-1), axis=1).reshape(4, len(members), -1)
        mine = own[:, np.array(members)]
        placed = lax.optimization_barrier(source[:3] + move)
        delta_x = mine[0][..., :, None] - placed[0][..., None, :]
        delta_y = mine[1][..., :, None] - placed[1][..., None, :]
        delta_z = mine[2][..., :, None] - placed[2][..., None, :]
        kernel = lax.rsqrt(
            delta_x * delta_x + delta_y * delta_y + delta_z * delta_z + softening_sq
        )
        near_parts.append(
            jnp.sum(kernel * source[3][..., None, :], axis=-1) - self_term * mine[3]
        )
        order += members
    near = jnp.take(
        jnp.concatenate(near_parts, axis=0), np.argsort(np.array(order)), axis=0
    ).reshape(2, 2, layers, slot_count)

    leaf_down_pts = 0.5 + 1.8 * unit_sphere
    leaf_far = point_sum(offsets, leaf_down_pts[:, None, None, None, :], leaf_local)
    parent_down_pts = 1.0 + 3.6 * unit_sphere
    local_float = jnp.arange(2).astype(jnp.float32)
    layer_parity = (jnp.arange(layers) % 2).astype(jnp.float32)
    in_parent = jnp.stack(
        [
            local_float[:, None, None, None] + offsets[0],
            local_float[None, :, None, None] + offsets[1],
            layer_parity[None, None, :, None] + offsets[2],
        ]
    )
    spread_local = jnp.repeat(parent_local, 2, axis=0)[None, None]
    parent_far = point_sum(in_parent, parent_down_pts[:, None, None, None, :], spread_local)
    total = near + leaf_far + parent_far
    return jnp.where(slot_index < counts[..., None], total, 0.0)


def solution(mesh):
    return jax.shard_map(
        shards,
        mesh=mesh,
        in_specs=(
            P(None, "gx", "gy", None, None),
            P("gx", "gy", None, None),
            P("gx", "gy", None),
            P(),
            P(),
            P(),
            P(),
        ),
        out_specs=P("gx", "gy", None, None),
        check_vma=False,
    )
```

```python
import functools

import jax
import numpy as np
import jax.numpy as jnp
from jax import lax
from jax.experimental import pallas as pl
from jax.experimental.pallas import tpu as pltpu
from jax.sharding import PartitionSpec as P

softening_sq = 0.0004
golden_turn = 2.399963229728653
highest = lax.Precision.HIGHEST


def sphere(point_count):
    middle = jnp.arange(point_count).astype(jnp.float32) + 0.5
    height = 1.0 - 2.0 * middle / point_count
    radial = jnp.sqrt(jnp.maximum(1.0 - height * height, 0.0))
    angle_turn = middle * golden_turn
    return jnp.stack([radial * jnp.cos(angle_turn), radial * jnp.sin(angle_turn), height])


def point_sum(targets, sources, weights):
    delta_x = targets[0][..., :, None] - sources[0][..., None, :]
    delta_y = targets[1][..., :, None] - sources[1][..., None, :]
    delta_z = targets[2][..., :, None] - sources[2][..., None, :]
    kernel = lax.rsqrt(delta_x * delta_x + delta_y * delta_y + delta_z * delta_z + softening_sq)
    return jnp.sum(kernel * weights[..., None, :], axis=-1)


def translation(unit_sphere, shift_x, shift_y, shift_z, radius):
    delta_x = (
        radius * (unit_sphere[0][:, None] - unit_sphere[0][None, :]) - shift_x[..., None, None]
    )
    delta_y = (
        radius * (unit_sphere[1][:, None] - unit_sphere[1][None, :]) - shift_y[..., None, None]
    )
    delta_z = (
        radius * (unit_sphere[2][:, None] - unit_sphere[2][None, :]) - shift_z[..., None, None]
    )
    return lax.rsqrt(delta_x * delta_x + delta_y * delta_y + delta_z * delta_z + softening_sq)


def child_points(unit_sphere):
    centre = jnp.arange(2).astype(jnp.float32) + 0.5
    point_count = unit_sphere.shape[1]
    box_shape = (2, 2, 2, point_count)
    along_x = jnp.broadcast_to(centre[:, None, None, None] + 0.9 * unit_sphere[0], box_shape)
    along_y = jnp.broadcast_to(centre[None, :, None, None] + 0.9 * unit_sphere[1], box_shape)
    along_z = jnp.broadcast_to(centre[None, None, :, None] + 0.9 * unit_sphere[2], box_shape)
    return jnp.stack([along_x, along_y, along_z]).reshape(3, 8 * point_count)


def rel_gather(buf, axis, dim, have=1):
    count = lax.axis_size(axis)
    while have < count:
        step = min(have, count - have)
        part = lax.slice_in_dim(buf, 0, step, axis=dim)
        got = lax.ppermute(part, axis, [(j, (j - have) % count) for j in range(count)])
        buf = jnp.concatenate([buf, got], axis=dim)
        have += step
    return buf


def exchange(items, axis, rider=None):
    count = lax.axis_size(axis)
    heads, tails = [], []
    for cells, dim, width in items:
        heads.append(lax.slice_in_dim(cells, 0, width, axis=dim))
        tails.append(lax.slice_in_dim(cells, cells.shape[dim] - width, cells.shape[dim], axis=dim))
    sent_tail = jnp.concatenate([t.reshape(-1) for t in tails])
    sent_head = jnp.concatenate(
        [h.reshape(-1) for h in heads] + ([] if rider is None else [rider.reshape(-1)])
    )
    from_left = lax.ppermute(sent_tail, axis, [(i, (i + 1) % count) for i in range(count)])
    from_right = lax.ppermute(sent_head, axis, [((i + 1) % count, i) for i in range(count)])
    out, start = [], 0
    for (cells, dim, width), head, tail in zip(items, heads, tails):
        size = head.size
        before = from_left[start : start + size].reshape(tail.shape)
        after = from_right[start : start + size].reshape(head.shape)
        out.append(jnp.concatenate([before, cells, after], axis=dim))
        start += size
    if rider is not None:
        out.append(from_right[start:].reshape(rider.shape))
    return out


def split_top(values):
    scaled = values * 65537.0
    return scaled - (scaled - values)


def m2l_kernel(shift_count, rows, table_ref, index_ref, base_ref, windows_ref, out_ref):
    out_ref[...] = jnp.zeros_like(out_ref)
    vectors = out_ref.shape[0]
    pieces = index_ref.shape[0] // (2 * shift_count)

    def split_dot(left, matrix_high, matrix_low, dims):
        both = lax.dot_general(left, matrix_high, dims, preferred_element_type=jnp.float32)
        cross = lax.dot_general(
            left[:vectors], matrix_low, dims, preferred_element_type=jnp.float32
        )
        return both[:vectors] + both[vectors:] + cross

    def gathered(sign, index):
        first = (sign * shift_count + index) * pieces
        block = jnp.concatenate(
            [windows_ref[index_ref[first + piece]] for piece in range(pieces)], axis=0
        )
        top = split_top(block)
        return jnp.concatenate([top, block - top], axis=0).astype(jnp.bfloat16)

    def body(index, carry):
        scale_x = table_ref[4 * index]
        scale_y = table_ref[4 * index + 1]
        scale_z = table_ref[4 * index + 2]
        offset = table_ref[4 * index + 3]
        fwd = gathered(0, index)
        back = gathered(1, index)
        for row in range(0, base_ref.shape[1], rows):
            square = (
                (base_ref[3, row : row + rows, :] + offset)
                + scale_x * base_ref[0, row : row + rows, :]
                + scale_y * base_ref[1, row : row + rows, :]
                + scale_z * base_ref[2, row : row + rows, :]
            )
            matrix = lax.rsqrt(square)
            matrix_top = split_top(matrix)
            matrix_high = matrix_top.astype(jnp.bfloat16)
            matrix_low = (matrix - matrix_top).astype(jnp.bfloat16)
            out_ref[:, row : row + rows] += split_dot(
                fwd, matrix_high, matrix_low, (((1,), (1,)), ((), ()))
            )
            out_ref[...] += split_dot(
                back[:, row : row + rows], matrix_high, matrix_low, (((1,), (0,)), ((), ()))
            )
        return carry

    lax.fori_loop(0, shift_count, body, 0)


def m2l(table, window_index, base, windows, vectors):
    shift_count = table.shape[0] // 4
    points = windows.shape[-1]
    return pl.pallas_call(
        functools.partial(m2l_kernel, shift_count, 128),
        out_shape=jax.ShapeDtypeStruct((vectors, points), jnp.float32),
        in_specs=[
            pl.BlockSpec(memory_space=pltpu.SMEM),
            pl.BlockSpec(memory_space=pltpu.SMEM),
            pl.BlockSpec(memory_space=pltpu.VMEM),
            pl.BlockSpec(memory_space=pltpu.VMEM),
        ],
        out_specs=pl.BlockSpec(memory_space=pltpu.VMEM),
        compiler_params=pltpu.CompilerParams(vmem_limit_bytes=48 * 1024 * 1024),
        cost_estimate=pl.CostEstimate(
            flops=12 * shift_count * vectors * points * points + 14 * shift_count * points * points,
            transcendentals=shift_count * points * points,
            bytes_accessed=4 * (windows.size + base.size + vectors * points),
        ),
    )(table, window_index, base, windows)


def far_shifts(span):
    shifts = []
    for dx in range(-span, span + 1):
        for dy in range(-span, span + 1):
            for dz in range(-span, span + 1):
                if max(abs(dx), abs(dy), abs(dz)) >= 2 and (dx, dy, dz) > (0, 0, 0):
                    shifts.append((dx, dy, dz))
    return shifts


def shards(offsets, charges, counts, c2e_leaf_up, c2e_leaf_down, c2e_top_up, c2e_top_down):
    slot_count = offsets.shape[-1]
    layers = offsets.shape[3]
    parent_layers = layers // 2
    points = c2e_leaf_up.shape[0]
    unit_sphere = sphere(points)
    slot_index = jnp.arange(slot_count)
    weights = jnp.where(slot_index < counts[..., None], charges, 0.0)
    packed = jnp.concatenate([offsets, weights[None]], axis=0)
    leaf_check_pts = 0.5 + 1.8 * unit_sphere
    leaf_check = point_sum(leaf_check_pts[:, None, None, None, :], offsets, weights)
    leaf_eq = jnp.einsum("ec,xyzc->xyze", c2e_leaf_up, leaf_check, precision=highest)
    children = child_points(unit_sphere)
    parent_weights = (
        leaf_eq.reshape(2, 2, parent_layers, 2, points)
        .transpose(2, 0, 1, 3, 4)
        .reshape(parent_layers, 8 * points)
    )
    parent_check_pts = 1.0 + 3.6 * unit_sphere
    parent_check = point_sum(parent_check_pts[:, None, :], children[:, None, :], parent_weights)
    parent_eq = jnp.einsum("ec,mc->me", c2e_top_up, parent_check, precision=highest)
    count_x = lax.axis_size("gx")
    count_y = lax.axis_size("gy")

    packed_x, eq_x, right_eq = exchange(
        [(packed, 1, 1), (leaf_eq, 0, 2)], "gx", rider=parent_eq
    )
    beside_all, cycle = exchange([(packed_x, 2, 1), (eq_x, 1, 2)], "gy")
    pair = jnp.stack([parent_eq, right_eq])[:, None]
    if count_x == 1:
        pair = parent_eq[None, None]
    gathered = rel_gather(rel_gather(pair, "gx", 0, min(2, count_x)), "gy", 1)
    kept = []
    for rel_x in range(count_x):
        for rel_y in range(count_y):
            off_x = (rel_x + count_x // 2) % count_x - count_x // 2
            off_y = (rel_y + count_y // 2) % count_y - count_y // 2
            if abs(off_x) > 1 or abs(off_y) > 1:
                kept.append((rel_x * count_y + rel_y, off_x, off_y))
    kept_index = np.array([k[0] for k in kept], np.int32)
    kept_x = np.array([2.0 * k[1] for k in kept], np.float32)
    kept_y = np.array([2.0 * k[2] for k in kept], np.float32)
    far_sources = jnp.take(gathered.reshape(count_x * count_y, parent_layers, points), kept_index, axis=0)
    steps = list(range(1 - parent_layers, parent_layers))
    step_shape = (len(steps), len(kept), points)
    step_float = 2.0 * np.array(steps, np.float32)
    source_pts = jnp.stack(
        [
            jnp.broadcast_to(kept_x[None, :, None] + 1.8 * unit_sphere[0], step_shape),
            jnp.broadcast_to(kept_y[None, :, None] + 1.8 * unit_sphere[1], step_shape),
            jnp.broadcast_to(step_float[:, None, None] + 1.8 * unit_sphere[2], step_shape),
        ]
    ).reshape(3, -1)
    check_far = 1.8 * unit_sphere
    delta_x = check_far[0][:, None] - source_pts[0][None, :]
    delta_y = check_far[1][:, None] - source_pts[1][None, :]
    delta_z = check_far[2][:, None] - source_pts[2][None, :]
    far_kernel = lax.rsqrt(delta_x * delta_x + delta_y * delta_y + delta_z * delta_z + softening_sq)
    zero_layer = jnp.zeros((len(kept), points), jnp.float32)
    far_rows = []
    for target in range(parent_layers):
        weight = jnp.stack(
            [
                far_sources[:, target + g] if 0 <= target + g < parent_layers else zero_layer
                for g in steps
            ]
        ).reshape(-1)
        far_rows.append(jnp.sum(far_kernel * weight, axis=-1))
    far_check = jnp.stack(far_rows)

    framed = jnp.pad(cycle, ((1, 1), (1, 1), (3, 3), (0, 0)))
    shifts = far_shifts(3)
    depth_windows = jnp.stack(
        [framed[:, :, depth : depth + layers] for depth in range(7)], axis=2
    ).reshape(-1, layers, points)
    window_index = np.array(
        [
            np.ravel_multi_index(
                (ix + sign * dx + 3, iy + sign * dy + 3, sign * dz + 3), framed.shape[:2] + (7,)
            )
            for sign in (1, -1)
            for dx, dy, dz in shifts
            for ix in range(2)
            for iy in range(2)
        ],
        np.int32,
    )
    base = jnp.stack(
        [0.9 * (unit_sphere[i][:, None] - unit_sphere[i][None, :]) for i in range(3)]
    )
    base = jnp.concatenate([base, jnp.sum(base * base, axis=0)[None]], axis=0)
    shift_array = np.array(shifts, np.float64)
    table = np.concatenate(
        [-2.0 * shift_array, (shift_array**2).sum(1, keepdims=True) + softening_sq], axis=1
    )
    table = jnp.asarray(table.astype(np.float32).reshape(-1))
    leaf_down_check = m2l(table, jnp.asarray(window_index), base, depth_windows, 4 * layers).reshape(
        2, 2, layers, points
    )
    parent_local = jnp.einsum("ec,mc->me", c2e_top_down, far_check, precision=highest)
    leaf_local = jnp.einsum("ec,xyzc->xyze", c2e_leaf_down, leaf_down_check, precision=highest)

    padded_around = jnp.pad(beside_all, ((0, 0), (0, 0), (0, 0), (1, 1), (0, 0)))
    around_shape = padded_around.shape[1:4]
    targets = [(bx, by, bz) for bx in range(2) for by in range(2) for bz in range(layers)]

    def neighbour_moves(bz):
        return [
            (mx, my, mz)
            for mx in (-1, 0, 1)
            for my in (-1, 0, 1)
            for mz in (-1, 0, 1)
            if 0 <= bz + mz < layers
        ]

    groups = {}
    for index, (bx, by, bz) in enumerate(targets):
        groups.setdefault(len(neighbour_moves(bz)), []).append(index)
    own = packed.reshape(4, 4 * layers, slot_count)
    around_rows = padded_around.reshape(4, -1, slot_count)
    self_term = lax.rsqrt(jnp.full((), softening_sq, jnp.float32))
    near_parts, order = [], []
    for members in groups.values():
        rows = np.array(
            [
                [
                    np.ravel_multi_index(
                        (targets[t][0] + 1 + mx, targets[t][1] + 1 + my, targets[t][2] + 1 + mz),
                        around_shape,
                    )
                    for mx, my, mz in neighbour_moves(targets[t][2])
                ]
                for t in members
            ],
            np.int32,
        )
        move = np.stack(
            [
                np.repeat(np.array(neighbour_moves(targets[t][2]), np.float32), slot_count, axis=0).T
                for t in members
            ],
            axis=1,
        )
        source = jnp.take(around_rows, rows.reshape(-1), axis=1).reshape(4, len(members), -1)
        mine = own[:, np.array(members)]
        placed = lax.optimization_barrier(source[:3] + move)
        delta_x = mine[0][..., :, None] - placed[0][..., None, :]
        delta_y = mine[1][..., :, None] - placed[1][..., None, :]
        delta_z = mine[2][..., :, None] - placed[2][..., None, :]
        kernel = lax.rsqrt(
            delta_x * delta_x + delta_y * delta_y + delta_z * delta_z + softening_sq
        )
        near_parts.append(
            jnp.sum(kernel * source[3][..., None, :], axis=-1) - self_term * mine[3]
        )
        order += members
    near = jnp.take(
        jnp.concatenate(near_parts, axis=0), np.argsort(np.array(order)), axis=0
    ).reshape(2, 2, layers, slot_count)

    leaf_down_pts = 0.5 + 1.8 * unit_sphere
    leaf_far = point_sum(offsets, leaf_down_pts[:, None, None, None, :], leaf_local)
    parent_down_pts = 1.0 + 3.6 * unit_sphere
    local_float = jnp.arange(2).astype(jnp.float32)
    layer_parity = (jnp.arange(layers) % 2).astype(jnp.float32)
    in_parent = jnp.stack(
        [
            local_float[:, None, None, None] + offsets[0],
            local_float[None, :, None, None] + offsets[1],
            layer_parity[None, None, :, None] + offsets[2],
        ]
    )
    spread_local = jnp.repeat(parent_local, 2, axis=0)[None, None]
    parent_far = point_sum(in_parent, parent_down_pts[:, None, None, None, :], spread_local)
    total = near + leaf_far + parent_far
    return jnp.where(slot_index < counts[..., None], total, 0.0)


def solution(mesh):
    return jax.shard_map(
        shards,
        mesh=mesh,
        in_specs=(
            P(None, "gx", "gy", None, None),
            P("gx", "gy", None, None),
            P("gx", "gy", None),
            P(),
            P(),
            P(),
            P(),
        ),
        out_specs=P("gx", "gy", None, None),
        check_vma=False,
    )
```

```python
import functools

import jax
import numpy as np
import jax.numpy as jnp
from jax import lax
from jax.experimental import pallas as pl
from jax.experimental.pallas import tpu as pltpu
from jax.sharding import PartitionSpec as P

softening_sq = 0.0004
golden_turn = 2.399963229728653
highest = lax.Precision.HIGHEST


def sphere(point_count):
    middle = jnp.arange(point_count).astype(jnp.float32) + 0.5
    height = 1.0 - 2.0 * middle / point_count
    radial = jnp.sqrt(jnp.maximum(1.0 - height * height, 0.0))
    angle_turn = middle * golden_turn
    return jnp.stack([radial * jnp.cos(angle_turn), radial * jnp.sin(angle_turn), height])


def point_sum(targets, sources, weights):
    delta_x = targets[0][..., :, None] - sources[0][..., None, :]
    delta_y = targets[1][..., :, None] - sources[1][..., None, :]
    delta_z = targets[2][..., :, None] - sources[2][..., None, :]
    kernel = lax.rsqrt(delta_x * delta_x + delta_y * delta_y + delta_z * delta_z + softening_sq)
    return jnp.sum(kernel * weights[..., None, :], axis=-1)


def translation(unit_sphere, shift_x, shift_y, shift_z, radius):
    delta_x = (
        radius * (unit_sphere[0][:, None] - unit_sphere[0][None, :]) - shift_x[..., None, None]
    )
    delta_y = (
        radius * (unit_sphere[1][:, None] - unit_sphere[1][None, :]) - shift_y[..., None, None]
    )
    delta_z = (
        radius * (unit_sphere[2][:, None] - unit_sphere[2][None, :]) - shift_z[..., None, None]
    )
    return lax.rsqrt(delta_x * delta_x + delta_y * delta_y + delta_z * delta_z + softening_sq)


def child_points(unit_sphere):
    centre = jnp.arange(2).astype(jnp.float32) + 0.5
    point_count = unit_sphere.shape[1]
    box_shape = (2, 2, 2, point_count)
    along_x = jnp.broadcast_to(centre[:, None, None, None] + 0.9 * unit_sphere[0], box_shape)
    along_y = jnp.broadcast_to(centre[None, :, None, None] + 0.9 * unit_sphere[1], box_shape)
    along_z = jnp.broadcast_to(centre[None, None, :, None] + 0.9 * unit_sphere[2], box_shape)
    return jnp.stack([along_x, along_y, along_z]).reshape(3, 8 * point_count)


def rel_gather(buf, axis, dim, have=1):
    count = lax.axis_size(axis)
    while have < count:
        step = min(have, count - have)
        part = lax.slice_in_dim(buf, 0, step, axis=dim)
        got = lax.ppermute(part, axis, [(j, (j - have) % count) for j in range(count)])
        buf = jnp.concatenate([buf, got], axis=dim)
        have += step
    return buf


def exchange(items, axis, rider=None):
    count = lax.axis_size(axis)
    heads, tails = [], []
    for cells, dim, width in items:
        heads.append(lax.slice_in_dim(cells, 0, width, axis=dim))
        tails.append(lax.slice_in_dim(cells, cells.shape[dim] - width, cells.shape[dim], axis=dim))
    sent_tail = jnp.concatenate([t.reshape(-1) for t in tails])
    sent_head = jnp.concatenate(
        [h.reshape(-1) for h in heads] + ([] if rider is None else [rider.reshape(-1)])
    )
    from_left = lax.ppermute(sent_tail, axis, [(i, (i + 1) % count) for i in range(count)])
    from_right = lax.ppermute(sent_head, axis, [((i + 1) % count, i) for i in range(count)])
    out, start = [], 0
    for (cells, dim, width), head, tail in zip(items, heads, tails):
        size = head.size
        before = from_left[start : start + size].reshape(tail.shape)
        after = from_right[start : start + size].reshape(head.shape)
        out.append(jnp.concatenate([before, cells, after], axis=dim))
        start += size
    if rider is not None:
        out.append(from_right[start:].reshape(rider.shape))
    return out


def split_top(values):
    scaled = values * 65537.0
    return scaled - (scaled - values)


def m2l_kernel(shift_count, rows, table_ref, index_ref, base_ref, windows_ref, out_ref):
    out_ref[...] = jnp.zeros_like(out_ref)
    vectors = out_ref.shape[0]
    pieces = index_ref.shape[0] // (2 * shift_count)

    def split_dot(left, matrix_high, matrix_low, dims):
        both = lax.dot_general(left, matrix_high, dims, preferred_element_type=jnp.float32)
        cross = lax.dot_general(
            left[:vectors], matrix_low, dims, preferred_element_type=jnp.float32
        )
        return both[:vectors] + both[vectors:] + cross

    def gathered(sign, index):
        first = (sign * shift_count + index) * pieces
        block = jnp.concatenate(
            [windows_ref[index_ref[first + piece]] for piece in range(pieces)], axis=0
        )
        top = split_top(block)
        return jnp.concatenate([top, block - top], axis=0).astype(jnp.bfloat16)

    def body(index, carry):
        scale_x = table_ref[4 * index]
        scale_y = table_ref[4 * index + 1]
        scale_z = table_ref[4 * index + 2]
        offset = table_ref[4 * index + 3]
        fwd = gathered(0, index)
        back = gathered(1, index)
        for row in range(0, base_ref.shape[1], rows):
            square = (
                (base_ref[3, row : row + rows, :] + offset)
                + scale_x * base_ref[0, row : row + rows, :]
                + scale_y * base_ref[1, row : row + rows, :]
                + scale_z * base_ref[2, row : row + rows, :]
            )
            matrix = lax.rsqrt(square)
            matrix_top = split_top(matrix)
            matrix_high = matrix_top.astype(jnp.bfloat16)
            matrix_low = (matrix - matrix_top).astype(jnp.bfloat16)
            out_ref[:, row : row + rows] += split_dot(
                fwd, matrix_high, matrix_low, (((1,), (1,)), ((), ()))
            )
            out_ref[...] += split_dot(
                back[:, row : row + rows], matrix_high, matrix_low, (((1,), (0,)), ((), ()))
            )
        return carry

    lax.fori_loop(0, shift_count, body, 0)


def m2l(table, window_index, base, windows, vectors):
    shift_count = table.shape[0] // 4
    points = windows.shape[-1]
    return pl.pallas_call(
        functools.partial(m2l_kernel, shift_count, 128),
        out_shape=jax.ShapeDtypeStruct((vectors, points), jnp.float32),
        in_specs=[
            pl.BlockSpec(memory_space=pltpu.SMEM),
            pl.BlockSpec(memory_space=pltpu.SMEM),
            pl.BlockSpec(memory_space=pltpu.VMEM),
            pl.BlockSpec(memory_space=pltpu.VMEM),
        ],
        out_specs=pl.BlockSpec(memory_space=pltpu.VMEM),
        compiler_params=pltpu.CompilerParams(vmem_limit_bytes=48 * 1024 * 1024),
        cost_estimate=pl.CostEstimate(
            flops=12 * shift_count * vectors * points * points + 14 * shift_count * points * points,
            transcendentals=shift_count * points * points,
            bytes_accessed=4 * (windows.size + base.size + vectors * points),
        ),
    )(table, window_index, base, windows)


def far_shifts(span):
    shifts = []
    for dx in range(-span, span + 1):
        for dy in range(-span, span + 1):
            for dz in range(-span, span + 1):
                if max(abs(dx), abs(dy), abs(dz)) >= 2 and (dx, dy, dz) > (0, 0, 0):
                    shifts.append((dx, dy, dz))
    return shifts


def shards(offsets, charges, counts, c2e_leaf_up, c2e_leaf_down, c2e_top_up, c2e_top_down):
    slot_count = offsets.shape[-1]
    layers = offsets.shape[3]
    parent_layers = layers // 2
    points = c2e_leaf_up.shape[0]
    unit_sphere = sphere(points)
    slot_index = jnp.arange(slot_count)
    weights = jnp.where(slot_index < counts[..., None], charges, 0.0)
    packed = jnp.concatenate([offsets, weights[None]], axis=0)
    leaf_check_pts = 0.5 + 1.8 * unit_sphere
    leaf_check = point_sum(leaf_check_pts[:, None, None, None, :], offsets, weights)
    leaf_eq = jnp.einsum("ec,xyzc->xyze", c2e_leaf_up, leaf_check, precision=highest)
    children = child_points(unit_sphere)
    parent_weights = (
        leaf_eq.reshape(2, 2, parent_layers, 2, points)
        .transpose(2, 0, 1, 3, 4)
        .reshape(parent_layers, 8 * points)
    )
    parent_check_pts = 1.0 + 3.6 * unit_sphere
    parent_check = point_sum(parent_check_pts[:, None, :], children[:, None, :], parent_weights)
    parent_eq = jnp.einsum("ec,mc->me", c2e_top_up, parent_check, precision=highest)
    count_x = lax.axis_size("gx")
    count_y = lax.axis_size("gy")

    packed_x, eq_x, right_eq = exchange(
        [(packed, 1, 1), (leaf_eq, 0, 2)], "gx", rider=parent_eq
    )
    beside_all, cycle = exchange([(packed_x, 2, 1), (eq_x, 1, 2)], "gy")
    pair = jnp.stack([parent_eq, right_eq])[:, None]
    if count_x == 1:
        pair = parent_eq[None, None]
    gathered = rel_gather(rel_gather(pair, "gx", 0, min(2, count_x)), "gy", 1)
    kept = []
    for rel_x in range(count_x):
        for rel_y in range(count_y):
            off_x = (rel_x + count_x // 2) % count_x - count_x // 2
            off_y = (rel_y + count_y // 2) % count_y - count_y // 2
            if abs(off_x) > 1 or abs(off_y) > 1:
                kept.append((rel_x * count_y + rel_y, off_x, off_y))
    kept_index = np.array([k[0] for k in kept], np.int32)
    kept_x = np.array([2.0 * k[1] for k in kept], np.float32)
    kept_y = np.array([2.0 * k[2] for k in kept], np.float32)
    far_sources = jnp.take(gathered.reshape(count_x * count_y, parent_layers, points), kept_index, axis=0)
    layer_float = jnp.arange(parent_layers).astype(jnp.float32)
    depth_pairs = 2.0 * (layer_float[None, :] - layer_float[:, None])
    far_shape = (parent_layers, len(kept), parent_layers, points)
    source_pts = jnp.stack(
        [
            jnp.broadcast_to(kept_x[None, :, None, None] + 1.8 * unit_sphere[0], far_shape),
            jnp.broadcast_to(kept_y[None, :, None, None] + 1.8 * unit_sphere[1], far_shape),
            jnp.broadcast_to(depth_pairs[:, None, :, None] + 1.8 * unit_sphere[2], far_shape),
        ]
    ).reshape(3, parent_layers, -1)
    far_check = point_sum(
        jnp.broadcast_to(1.8 * unit_sphere[:, None, :], (3, parent_layers, points)),
        source_pts,
        far_sources.reshape(-1),
    )

    framed = jnp.pad(cycle, ((1, 1), (1, 1), (3, 3), (0, 0)))
    shifts = far_shifts(3)
    depth_windows = jnp.stack(
        [framed[:, :, depth : depth + layers] for depth in range(7)], axis=2
    ).reshape(-1, layers, points)
    window_index = np.array(
        [
            np.ravel_multi_index(
                (ix + sign * dx + 3, iy + sign * dy + 3, sign * dz + 3), framed.shape[:2] + (7,)
            )
            for sign in (1, -1)
            for dx, dy, dz in shifts
            for ix in range(2)
            for iy in range(2)
        ],
        np.int32,
    )
    base = jnp.stack(
        [0.9 * (unit_sphere[i][:, None] - unit_sphere[i][None, :]) for i in range(3)]
    )
    base = jnp.concatenate([base, jnp.sum(base * base, axis=0)[None]], axis=0)
    shift_array = np.array(shifts, np.float64)
    table = np.concatenate(
        [-2.0 * shift_array, (shift_array**2).sum(1, keepdims=True) + softening_sq], axis=1
    )
    table = jnp.asarray(table.astype(np.float32).reshape(-1))
    leaf_down_check = m2l(table, jnp.asarray(window_index), base, depth_windows, 4 * layers).reshape(
        2, 2, layers, points
    )
    parent_local = jnp.einsum("ec,mc->me", c2e_top_down, far_check, precision=highest)
    leaf_local = jnp.einsum("ec,xyzc->xyze", c2e_leaf_down, leaf_down_check, precision=highest)

    padded_around = jnp.pad(beside_all, ((0, 0), (0, 0), (0, 0), (1, 1), (0, 0)))
    around_shape = padded_around.shape[1:4]
    targets = [(bx, by, bz) for bx in range(2) for by in range(2) for bz in range(layers)]

    def neighbour_moves(bz):
        return [
            (mx, my, mz)
            for mx in (-1, 0, 1)
            for my in (-1, 0, 1)
            for mz in (-1, 0, 1)
            if 0 <= bz + mz < layers
        ]

    groups = {}
    for index, (bx, by, bz) in enumerate(targets):
        groups.setdefault(len(neighbour_moves(bz)), []).append(index)
    own = packed.reshape(4, 4 * layers, slot_count)
    around_rows = padded_around.reshape(4, -1, slot_count)
    self_term = lax.rsqrt(jnp.full((), softening_sq, jnp.float32))
    near_parts, order = [], []
    for members in groups.values():
        rows = np.array(
            [
                [
                    np.ravel_multi_index(
                        (targets[t][0] + 1 + mx, targets[t][1] + 1 + my, targets[t][2] + 1 + mz),
                        around_shape,
                    )
                    for mx, my, mz in neighbour_moves(targets[t][2])
                ]
                for t in members
            ],
            np.int32,
        )
        move = np.stack(
            [
                np.repeat(np.array(neighbour_moves(targets[t][2]), np.float32), slot_count, axis=0).T
                for t in members
            ],
            axis=1,
        )
        source = jnp.take(around_rows, rows.reshape(-1), axis=1).reshape(4, len(members), -1)
        mine = own[:, np.array(members)]
        placed = lax.optimization_barrier(source[:3] + move)
        delta_x = mine[0][..., :, None] - placed[0][..., None, :]
        delta_y = mine[1][..., :, None] - placed[1][..., None, :]
        delta_z = mine[2][..., :, None] - placed[2][..., None, :]
        kernel = lax.rsqrt(
            delta_x * delta_x + delta_y * delta_y + delta_z * delta_z + softening_sq
        )
        near_parts.append(
            jnp.sum(kernel * source[3][..., None, :], axis=-1) - self_term * mine[3]
        )
        order += members
    near = jnp.take(
        jnp.concatenate(near_parts, axis=0), np.argsort(np.array(order)), axis=0
    ).reshape(2, 2, layers, slot_count)

    leaf_down_pts = 0.5 + 1.8 * unit_sphere
    parent_down_pts = 1.0 + 3.6 * unit_sphere
    local_float = jnp.arange(2).astype(jnp.float32)
    layer_parity = (jnp.arange(layers) % 2).astype(jnp.float32)
    box_shape = (3, 2, 2, layers, points)
    parent_in_leaf = jnp.stack(
        [
            jnp.broadcast_to(parent_down_pts[0] - local_float[:, None, None, None], box_shape[1:]),
            jnp.broadcast_to(parent_down_pts[1] - local_float[None, :, None, None], box_shape[1:]),
            jnp.broadcast_to(parent_down_pts[2] - layer_parity[None, None, :, None], box_shape[1:]),
        ]
    )
    far_pts = jnp.concatenate(
        [jnp.broadcast_to(leaf_down_pts[:, None, None, None, :], box_shape), parent_in_leaf], axis=-1
    )
    far_weights = jnp.concatenate(
        [leaf_local, jnp.broadcast_to(jnp.repeat(parent_local, 2, axis=0), box_shape[1:])], axis=-1
    )
    total = near + point_sum(offsets, far_pts, far_weights)
    return jnp.where(slot_index < counts[..., None], total, 0.0)


def solution(mesh):
    return jax.shard_map(
        shards,
        mesh=mesh,
        in_specs=(
            P(None, "gx", "gy", None, None),
            P("gx", "gy", None, None),
            P("gx", "gy", None),
            P(),
            P(),
            P(),
            P(),
        ),
        out_specs=P("gx", "gy", None, None),
        check_vma=False,
    )
```
